32 devices in a mesh: groups: 2 (over y), seq: 4 (over z), wloop: 2 (over x), heads: 2 (over core).
Axes of the slice: x: 2, y: 2, z: 4, core: 2. Of those that a mesh axis runs over, the one named last changes fastest.
Arguments:
- activations: bfloat16 [4, 2048, 2048], P(('groups', 'wloop'), 'seq'), parts along dimension 0, may hold values from -6 to 6
- norm_gain: float32 [2048], replicated, may hold values from 0.1 to 1.9
- w_query: bfloat16 [2048, 2048], P('wloop', 'heads'), may hold values from -0.125 to 0.125
- w_keyvalue: bfloat16 [2048, 2, 2048], P('wloop', None, 'heads'), may hold values from -0.125 to 0.125
- w_output: bfloat16 [2048, 2048], P('heads', 'wloop'), may hold values from -0.125 to 0.125
- log_retain: float32 [4, 16, 2048], P(('groups', 'wloop'), 'heads', 'seq'), parts along dimension 0, may hold values from -3 to 0, as said below
- resets: int32 [4, 4], P(('groups', 'wloop'), 'seq'), parts along dimension 0, may hold values 0 or 1
Outputs:
- layer_out: bfloat16 [4, 2048, 2048], P(('groups', 'wloop'), 'seq', 'heads'), parts along dimension 0
The draws below stay inside these ranges and needn't reach their ends.
There are 2 independent parts, one for each index of `groups`. The reference program is written for one: setup_inputs(seed, part) draws one part's arguments, and reference() takes and returns one part's arrays. A program takes and returns all parts, laid end to end along the dimension named above; an argument that names none is the same for every part. Nothing has to cross between parts.
Inputs may be any that keep to these rules, and one draw needn't show every extreme that they name: `log_retain`: log retention per token and head, never above zero.
All inputs are finite; a program needn't handle non-finite values. No bound on the sum of `resets` on one device may be relied on, other than what follows from the above.
Results may differ from the reference program's by a relative error of at most 0.02.
Values may be sent and summed in bfloat16 or wider, within the bound.
No kernel may reach another device: no remote copies, remote signals or barrier semaphores. Data moves between devices by JAX's collectives and lax.ppermute only.
A program may use at most 128 MiB of HBM per device.

```python
import math
import jax
import jax.numpy as jnp
from jax import lax

D = 2048
HEADS = 16
SEG = 512
BATCH = 2
SEGMENTS = 4
PATH_STEPS = 2048
INNER = 2048


def draw_log_retain(key, part):
    lookup_vectors = jax.random.split(key, 7)
    array_dimensions = (BATCH, HEADS, PATH_STEPS)
    fast_share = 0.5
    fast = jax.random.bernoulli(lookup_vectors[0], fast_share, (BATCH, HEADS, 1))
    fast_rate = jnp.exp(jax.random.uniform(lookup_vectors[1], (BATCH, HEADS, 1), jnp.float32, math.log(2.5), math.log(4.0))) / min(40, SEG)
    slow_rate = jnp.exp(jax.random.uniform(lookup_vectors[2], (BATCH, HEADS, 1), jnp.float32, math.log(0.1), math.log(0.5))) / PATH_STEPS
    starting_position = jnp.where(fast, fast_rate, slow_rate)
    block_fading_multiplier = jnp.exp(jax.random.uniform(lookup_vectors[3], (BATCH, HEADS, SEGMENTS, 1), jnp.float32, -math.log(2.0), math.log(2.0)))
    block_fading_multiplier = jnp.broadcast_to(block_fading_multiplier, (BATCH, HEADS, SEGMENTS, SEG)).reshape(array_dimensions)
    step_fading_multiplier = jax.random.uniform(lookup_vectors[4], array_dimensions, jnp.float32, 0.7, 1.4)
    batch_bundle = jax.random.bernoulli(lookup_vectors[5], min(0.5, 2.0 / PATH_STEPS), array_dimensions)
    bundle_count = jnp.log(jax.random.uniform(lookup_vectors[6], array_dimensions, jnp.float32, 0.67, 0.8))
    return -starting_position * block_fading_multiplier * step_fading_multiplier + jnp.where(batch_bundle, bundle_count, 0.0)


def set_ends(array, rng, least, largest):
    place = [jax.random.randint(jax.random.fold_in(rng, axis), (), 0, length) for axis, length in enumerate(array.shape)]
    widest = array.shape.index(max(array.shape))
    neighbour = place[:widest] + [(place[widest] + 1) % array.shape[widest]] + place[widest + 1:]
    return array.at[tuple(place)].set(least).at[tuple(neighbour)].set(largest)


def steps_of(rng, extent, cuts, least, top_value):
    level = 1.0
    for dim, shards_of in cuts:
        draws = jax.random.uniform(jax.random.fold_in(jax.random.fold_in(rng, 6), dim), (shards_of,), jnp.float32, least / len(cuts), top_value / len(cuts))
        level = level * jnp.repeat(jnp.exp(draws), extent[dim] // shards_of).reshape((-1,) + (1,) * (len(extent) - 1 - dim))
    return level


def centred(key, shape, scale, reach, cuts=(), kind=jnp.bfloat16):
    gain = steps_of(key, shape, cuts, -0.22, 0.18) if cuts else 1.0
    entries = jax.random.normal(key, shape, jnp.float32) * scale * gain
    return jnp.minimum(jnp.maximum(entries, -reach), reach).astype(kind)


def setup_inputs(seed: int = 0, part: int = 0) -> dict:
    streams_of = jax.random.split(jax.random.key(seed), 8)
    part_keys = jax.random.split(jax.random.fold_in(streams_of[7], part), 8)
    return {
        "activations": centred(part_keys[0], (BATCH, PATH_STEPS, D), 1.0, 6.0, ((0, 2), (1, 4))),
        "norm_gain": jnp.clip(1.0 + 0.18 * jax.random.normal(streams_of[1], (D,), jnp.float32), 0.1, 1.9),
        "w_query": centred(streams_of[2], (D, INNER), D ** -0.5, 0.125, ((0, 2), (1, 2))),
        "w_keyvalue": centred(streams_of[3], (D, 2, INNER), D ** -0.5, 0.125, ((0, 2), (2, 2))),
        "w_output": centred(streams_of[4], (INNER, D), INNER ** -0.5, 0.125, ((0, 2), (1, 2))),
        "log_retain": draw_log_retain(jax.random.fold_in(jax.random.fold_in(streams_of[7], part), 71), part),
        "resets": set_ends((jax.random.randint(part_keys[6], (BATCH, SEGMENTS), 0, 6) < 1).astype(jnp.int32), jax.random.fold_in(part_keys[6], 1), 0, 1),
    }


SCORE_SCALE = 2.0

def rms_rows(values, eps):
    return values * lax.rsqrt(lax.optimization_barrier(jnp.mean(values * values, axis=-1, keepdims=True)) + eps)

def window_block(item, scale):
    query, lookup_vectors, values, prior_keys, prior_values, allow = item
    query = query.astype(jnp.float32)
    own = jnp.einsum('ihd,jhd->hij', query, lookup_vectors.astype(jnp.float32)) * scale
    prior = jnp.einsum('ihd,jhd->hij', query, prior_keys.astype(jnp.float32)) * scale
    span = query.shape[0]
    row_pos = lax.broadcasted_iota(jnp.int32, (span, span), 0)
    column_pos = lax.broadcasted_iota(jnp.int32, (span, span), 1)
    own_w = jnp.where(column_pos <= row_pos, jnp.exp(own), 0.0)
    prior_w = jnp.where((column_pos > row_pos) & allow, jnp.exp(prior), 0.0)
    total = lax.optimization_barrier(jnp.sum(jnp.concatenate([own_w, prior_w], axis=-1), axis=-1, keepdims=True))
    own_p = (own_w / total).astype(jnp.bfloat16).astype(jnp.float32)
    prior_p = (prior_w / total).astype(jnp.bfloat16).astype(jnp.float32)
    return jnp.einsum('hij,jhd->ihd', own_p, values.astype(jnp.float32)) + jnp.einsum('hij,jhd->ihd', prior_p, prior_values.astype(jnp.float32))

def trajectory(acts, retain, reset_row, norm_gain, w_query, w_keyvalue, w_output):
    length, width = acts.shape
    heads = retain.shape[0]
    inner = w_query.shape[1]
    head_dim = inner // heads
    segments = reset_row.shape[0]
    span = length // segments
    scale = SCORE_SCALE / math.sqrt(head_dim)
    normed = (rms_rows(acts.astype(jnp.float32), 1e-05) * norm_gain).astype(jnp.bfloat16)
    query_raw = jnp.dot(normed, w_query, preferred_element_type=jnp.float32)
    key_raw = jnp.dot(normed, w_keyvalue[:, 0, :], preferred_element_type=jnp.float32)
    value_raw = jnp.dot(normed, w_keyvalue[:, 1, :], preferred_element_type=jnp.float32)
    queries = rms_rows(query_raw.reshape(segments, span, heads, head_dim), 1e-06).astype(jnp.bfloat16)
    lookup_vectors = rms_rows(key_raw.reshape(segments, span, heads, head_dim), 1e-06).astype(jnp.bfloat16)
    values = value_raw.reshape(segments, span, heads, head_dim).astype(jnp.bfloat16)
    keep = (1 - reset_row).astype(jnp.float32)
    retain_seg = retain.reshape(heads, segments, span).transpose(1, 0, 2)
    climb = jnp.cumsum(retain_seg, axis=-1)
    whole = climb[:, :, -1]
    factor = jnp.exp(whole) * keep[:, None]
    weight = jnp.exp(whole[:, :, None] - climb)
    local_state = jnp.einsum('sht,sthd,sthe->shde', weight, lookup_vectors.astype(jnp.float32), values.astype(jnp.float32), precision=lax.Precision.HIGHEST)
    local_mass = lax.optimization_barrier(jnp.sum(weight * weight, axis=-1))

    def advance(carry, item):
        state, mass = carry
        fac, add_state, add_mass = item
        return ((fac[:, None, None] * state + add_state, fac * fac * mass + add_mass), (state, mass))
    start = (jnp.zeros((heads, head_dim, head_dim), jnp.float32), jnp.zeros((heads,), jnp.float32))
    _, (entering, entering_mass) = lax.scan(advance, start, (factor, local_state, local_mass))
    entering = entering * keep[:, None, None, None]
    entering_mass = entering_mass * keep[:, None]
    read = jnp.einsum('sthd,shde->sthe', queries.astype(jnp.float32), entering, precision=lax.Precision.HIGHEST)
    read = read * jnp.exp(climb).transpose(0, 2, 1)[..., None]
    read = read / jnp.sqrt(head_dim * (1.0 + entering_mass))[:, None, :, None]
    prior_keys = jnp.concatenate([jnp.zeros_like(lookup_vectors[:1]), lookup_vectors[:-1]], axis=0)
    prior_values = jnp.concatenate([jnp.zeros_like(values[:1]), values[:-1]], axis=0)
    allow = (keep > 0.5) & (jnp.arange(segments) > 0)
    window = lax.map(lambda item: window_block(item, scale), (queries, lookup_vectors, values, prior_keys, prior_values, allow))
    attended = (window + read).astype(jnp.bfloat16).reshape(length, inner)
    mixed = jnp.dot(attended, w_output, preferred_element_type=jnp.float32)
    return (acts.astype(jnp.float32) + mixed).astype(jnp.bfloat16)

def reference(activations, norm_gain, w_query, w_keyvalue, w_output, log_retain, resets):
    return lax.map(lambda item: trajectory(item[0], item[1], item[2], norm_gain, w_query, w_keyvalue, w_output), (activations, log_retain, resets))
```

```python
import math

import jax
import jax.numpy as jnp
from jax import lax
from jax.sharding import PartitionSpec as P

SCORE_SCALE = 2.0


def shifted(value, axis, steps):
    count = lax.axis_size(axis)
    initial, last = (max(0, -steps), min(count, count - steps))
    return lax.ppermute(value, axis, [(source, source + steps) for source in range(initial, last)])


def rms_rows(values, eps):
    return values * lax.rsqrt(jnp.mean(values * values, axis=-1, keepdims=True) + eps)


def window_mix(queries, lookup_vectors, values, prior_keys, prior_values, allow, scale):
    own = (
        jnp.einsum("bihd,bjhd->bhij", queries, lookup_vectors, preferred_element_type=jnp.float32)
        * scale
    )
    prior = (
        jnp.einsum("bihd,bjhd->bhij", queries, prior_keys, preferred_element_type=jnp.float32)
        * scale
    )
    span = queries.shape[1]
    row_pos = lax.broadcasted_iota(jnp.int32, (span, span), 0)
    column_pos = lax.broadcasted_iota(jnp.int32, (span, span), 1)
    own_w = jnp.where(column_pos <= row_pos, jnp.exp(own), 0.0)
    prior_w = jnp.where((column_pos > row_pos) & allow[:, None, None, None], jnp.exp(prior), 0.0)
    total = jnp.sum(own_w, axis=-1, keepdims=True) + jnp.sum(prior_w, axis=-1, keepdims=True)
    own_p = (own_w / total).astype(jnp.bfloat16)
    prior_p = (prior_w / total).astype(jnp.bfloat16)
    return jnp.einsum(
        "bhij,bjhd->bihd", own_p, values, preferred_element_type=jnp.float32
    ) + jnp.einsum("bhij,bjhd->bihd", prior_p, prior_values, preferred_element_type=jnp.float32)


def shards(activations, norm_gain, w_query, w_keyvalue, w_output, log_retain, resets):
    trajs, span, width = activations.shape
    heads_here = log_retain.shape[1]
    inner_here = w_query.shape[1]
    head_dim = inner_here // heads_here
    scale = SCORE_SCALE / math.sqrt(head_dim)
    count = trajs * span
    normed = (rms_rows(activations.astype(jnp.float32), 1e-05) * norm_gain).astype(jnp.bfloat16)
    normed = normed.reshape(count, width)
    ways = lax.axis_size("wloop")
    me = lax.axis_index("wloop")
    block = width // ways

    def feature_block(index):
        return lax.dynamic_slice_in_dim(normed, index * block, block, 1)

    stacked = [feature_block(me)]
    for step in range(1, ways):
        stacked.append(
            lax.ppermute(
                feature_block((me + step) % ways),
                "wloop",
                [(source, (source + step) % ways) for source in range(ways)],
            )
        )

    def gathered_sum(partials):
        total = partials[0]
        for step in range(1, ways):
            total = total + lax.ppermute(
                partials[step].astype(jnp.bfloat16),
                "wloop",
                [(source, (source - step) % ways) for source in range(ways)],
            ).astype(jnp.float32)
        return total

    pair_raw = gathered_sum(
        [
            jnp.einsum("td,dje->jte", rows, w_keyvalue, preferred_element_type=jnp.float32)
            for rows in stacked
        ]
    )
    query_raw = gathered_sum(
        [jnp.dot(rows, w_query, preferred_element_type=jnp.float32) for rows in stacked]
    )
    lookup_vectors = rms_rows(pair_raw[0].reshape(trajs, span, heads_here, head_dim), 1e-06).astype(
        jnp.bfloat16
    )
    values = pair_raw[1].reshape(trajs, span, heads_here, head_dim).astype(jnp.bfloat16)
    prior_keys, prior_values = shifted(
        (lookup_vectors.reshape(trajs, span, inner_here), values.reshape(trajs, span, inner_here)),
        "seq",
        1,
    )
    queries = rms_rows(query_raw.reshape(trajs, span, heads_here, head_dim), 1e-06).astype(
        jnp.bfloat16
    )
    keep = (1 - resets[:, 0]).astype(jnp.float32)
    climb = jnp.cumsum(log_retain, axis=-1)
    whole = climb[:, :, -1]
    factor = jnp.exp(whole) * keep[:, None]
    weight = jnp.exp(whole[:, :, None] - climb)
    local_state = jnp.einsum(
        "bht,bthd,bthe->bhde",
        weight,
        lookup_vectors.astype(jnp.float32),
        values.astype(jnp.float32),
        precision=lax.Precision.HIGHEST,
    )
    local_mass = jnp.sum(weight * weight, axis=-1)

    def relay_turn(turn, carry):
        state, mass = carry
        return (
            shifted(
                (factor[:, :, None, None] * state + local_state).astype(jnp.bfloat16), "seq", 1
            ).astype(jnp.float32),
            shifted((factor * factor * mass + local_mass).astype(jnp.bfloat16), "seq", 1).astype(
                jnp.float32
            ),
        )

    entering, entering_mass = lax.fori_loop(
        0,
        lax.axis_size("seq") - 1,
        relay_turn,
        (jnp.zeros_like(local_state), jnp.zeros_like(local_mass)),
    )
    entering = entering * keep[:, None, None, None]
    entering_mass = entering_mass * keep[:, None]
    read = jnp.einsum(
        "bthd,bhde->bthe", queries.astype(jnp.float32), entering, precision=lax.Precision.HIGHEST
    )
    read = read * jnp.exp(climb).transpose(0, 2, 1)[..., None]
    read = read / jnp.sqrt(head_dim * (1.0 + entering_mass))[:, None, :, None]
    allow = (keep > 0.5) & (lax.axis_index("seq") > 0)
    window = window_mix(
        queries,
        lookup_vectors,
        values,
        prior_keys.reshape(trajs, span, heads_here, head_dim),
        prior_values.reshape(trajs, span, heads_here, head_dim),
        allow,
        scale,
    )
    attended = (window + read).astype(jnp.bfloat16).reshape(count, inner_here)
    partial_out = jnp.dot(
        attended,
        lax.all_gather(w_output, "wloop", axis=1, tiled=True),
        preferred_element_type=jnp.float32,
    )
    summed = lax.psum_scatter(
        partial_out.astype(jnp.bfloat16), "heads", scatter_dimension=1, tiled=True
    ).astype(jnp.float32)
    share = summed.shape[1]
    residual = lax.dynamic_slice_in_dim(
        activations.reshape(count, width), lax.axis_index("heads") * share, share, 1
    )
    return (residual.astype(jnp.float32) + summed).astype(jnp.bfloat16).reshape(trajs, span, share)


def solution(mesh):
    placed = (
        P(("groups", "wloop"), "seq", None),
        P(),
        P("wloop", "heads"),
        P("wloop", None, "heads"),
        P("heads", "wloop"),
        P(("groups", "wloop"), "heads", "seq"),
        P(("groups", "wloop"), "seq"),
    )
    return jax.shard_map(
        shards,
        mesh=mesh,
        in_specs=placed,
        out_specs=P(("groups", "wloop"), "seq", "heads"),
        check_vma=False,
    )
```

```python
import math

import jax
import jax.numpy as jnp
from jax import lax
from jax.sharding import PartitionSpec as P

SCORE_SCALE = 2.0


def shifted(value, axis, steps):
    count = lax.axis_size(axis)
    initial, last = (max(0, -steps), min(count, count - steps))
    return lax.ppermute(value, axis, [(source, source + steps) for source in range(initial, last)])


def rms_rows(values, eps):
    return values * lax.rsqrt(jnp.mean(values * values, axis=-1, keepdims=True) + eps)


def window_mix(queries, lookup_vectors, values, prior_keys, prior_values, allow, scale):
    own = (
        jnp.einsum("bihd,bjhd->bhij", queries, lookup_vectors, preferred_element_type=jnp.float32)
        * scale
    )
    prior = (
        jnp.einsum("bihd,bjhd->bhij", queries, prior_keys, preferred_element_type=jnp.float32)
        * scale
    )
    span = queries.shape[1]
    row_pos = lax.broadcasted_iota(jnp.int32, (span, span), 0)
    column_pos = lax.broadcasted_iota(jnp.int32, (span, span), 1)
    own_w = jnp.where(column_pos <= row_pos, jnp.exp(own), 0.0)
    prior_w = jnp.where((column_pos > row_pos) & allow[:, None, None, None], jnp.exp(prior), 0.0)
    total = jnp.sum(own_w, axis=-1, keepdims=True) + jnp.sum(prior_w, axis=-1, keepdims=True)
    own_p = (own_w / total).astype(jnp.bfloat16)
    prior_p = (prior_w / total).astype(jnp.bfloat16)
    return jnp.einsum(
        "bhij,bjhd->bihd", own_p, values, preferred_element_type=jnp.float32
    ) + jnp.einsum("bhij,bjhd->bihd", prior_p, prior_values, preferred_element_type=jnp.float32)


def shards(activations, norm_gain, w_query, w_keyvalue, w_output, log_retain, resets):
    trajs, span, width = activations.shape
    heads_here = log_retain.shape[1]
    inner_here = w_query.shape[1]
    head_dim = inner_here // heads_here
    scale = SCORE_SCALE / math.sqrt(head_dim)
    count = trajs * span
    normed = (rms_rows(activations.astype(jnp.float32), 1e-05) * norm_gain).astype(jnp.bfloat16)
    normed = normed.reshape(count, width)
    ways = lax.axis_size("wloop")
    me = lax.axis_index("wloop")
    block = width // ways

    def feature_block(index):
        return lax.dynamic_slice_in_dim(normed, index * block, block, 1)

    cores = lax.axis_size("heads")
    core = lax.axis_index("heads")
    share_rows = count // cores

    def from_cores(part):
        pieces = [part]
        for step in range(1, cores):
            pieces.append(
                lax.ppermute(part, "heads", [(source, (source + step) % cores) for source in range(cores)])
            )
        order = (core - jnp.arange(cores)) % cores
        return jnp.take(jnp.stack(pieces), order, axis=0).reshape(count, block)

    stacked = [feature_block(me)]
    for step in range(1, ways):
        part = lax.dynamic_slice_in_dim(feature_block((me + step) % ways), core * share_rows, share_rows, 0)
        stacked.append(
            from_cores(
                lax.ppermute(
                    part,
                    "wloop",
                    [(source, (source + step) % ways) for source in range(ways)],
                )
            )
        )

    def gathered_sum(partials):
        total = partials[0]
        for step in range(1, ways):
            total = total + lax.ppermute(
                partials[step].astype(jnp.bfloat16),
                "wloop",
                [(source, (source - step) % ways) for source in range(ways)],
            ).astype(jnp.float32)
        return total

    pair_raw = gathered_sum(
        [
            jnp.einsum("td,dje->jte", rows, w_keyvalue, preferred_element_type=jnp.float32)
            for rows in stacked
        ]
    )
    query_raw = gathered_sum(
        [jnp.dot(rows, w_query, preferred_element_type=jnp.float32) for rows in stacked]
    )
    lookup_vectors = rms_rows(pair_raw[0].reshape(trajs, span, heads_here, head_dim), 1e-06).astype(
        jnp.bfloat16
    )
    values = pair_raw[1].reshape(trajs, span, heads_here, head_dim).astype(jnp.bfloat16)
    prior_keys, prior_values = shifted(
        (lookup_vectors.reshape(trajs, span, inner_here), values.reshape(trajs, span, inner_here)),
        "seq",
        1,
    )
    queries = rms_rows(query_raw.reshape(trajs, span, heads_here, head_dim), 1e-06).astype(
        jnp.bfloat16
    )
    keep = (1 - resets[:, 0]).astype(jnp.float32)
    climb = jnp.cumsum(log_retain, axis=-1)
    whole = climb[:, :, -1]
    factor = jnp.exp(whole) * keep[:, None]
    weight = jnp.exp(whole[:, :, None] - climb)
    local_state = jnp.einsum(
        "bht,bthd,bthe->bhde",
        weight,
        lookup_vectors.astype(jnp.float32),
        values.astype(jnp.float32),
        precision=lax.Precision.HIGHEST,
    )
    local_mass = jnp.sum(weight * weight, axis=-1)

    def relay_turn(turn, carry):
        state, mass = carry
        return (
            shifted(
                (factor[:, :, None, None] * state + local_state).astype(jnp.bfloat16), "seq", 1
            ).astype(jnp.float32),
            shifted((factor * factor * mass + local_mass).astype(jnp.bfloat16), "seq", 1).astype(
                jnp.float32
            ),
        )

    entering, entering_mass = lax.fori_loop(
        0,
        lax.axis_size("seq") - 1,
        relay_turn,
        (jnp.zeros_like(local_state), jnp.zeros_like(local_mass)),
    )
    entering = entering * keep[:, None, None, None]
    entering_mass = entering_mass * keep[:, None]
    read = jnp.einsum(
        "bthd,bhde->bthe", queries.astype(jnp.float32), entering, precision=lax.Precision.HIGHEST
    )
    read = read * jnp.exp(climb).transpose(0, 2, 1)[..., None]
    read = read / jnp.sqrt(head_dim * (1.0 + entering_mass))[:, None, :, None]
    allow = (keep > 0.5) & (lax.axis_index("seq") > 0)
    window = window_mix(
        queries,
        lookup_vectors,
        values,
        prior_keys.reshape(trajs, span, heads_here, head_dim),
        prior_values.reshape(trajs, span, heads_here, head_dim),
        allow,
        scale,
    )
    attended = (window + read).astype(jnp.bfloat16).reshape(count, inner_here)
    w_output = lax.optimization_barrier((w_output, query_raw))[0]
    partial_out = jnp.dot(
        attended,
        lax.all_gather(w_output, "wloop", axis=1, tiled=True),
        preferred_element_type=jnp.float32,
    )
    summed = lax.psum_scatter(
        partial_out.astype(jnp.bfloat16), "heads", scatter_dimension=1, tiled=True
    ).astype(jnp.float32)
    share = summed.shape[1]
    residual = lax.dynamic_slice_in_dim(
        activations.reshape(count, width), lax.axis_index("heads") * share, share, 1
    )
    return (residual.astype(jnp.float32) + summed).astype(jnp.bfloat16).reshape(trajs, span, share)


def solution(mesh):
    placed = (
        P(("groups", "wloop"), "seq", None),
        P(),
        P("wloop", "heads"),
        P("wloop", None, "heads"),
        P("heads", "wloop"),
        P(("groups", "wloop"), "heads", "seq"),
        P(("groups", "wloop"), "seq"),
    )
    return jax.shard_map(
        shards,
        mesh=mesh,
        in_specs=placed,
        out_specs=P(("groups", "wloop"), "seq", "heads"),
        check_vma=False,
    )
```

```python
import math

import jax
import jax.numpy as jnp
from jax import lax
from jax.sharding import PartitionSpec as P

SCORE_SCALE = 2.0


def shifted(value, axis, steps):
    count = lax.axis_size(axis)
    initial, last = (max(0, -steps), min(count, count - steps))
    return lax.ppermute(value, axis, [(source, source + steps) for source in range(initial, last)])


def rms_rows(values, eps):
    return values * lax.rsqrt(jnp.mean(values * values, axis=-1, keepdims=True) + eps)


def window_mix(queries, lookup_vectors, values, prior_keys, prior_values, allow, scale):
    own = (
        jnp.einsum("bihd,bjhd->bhij", queries, lookup_vectors, preferred_element_type=jnp.float32)
        * scale
    )
    prior = (
        jnp.einsum("bihd,bjhd->bhij", queries, prior_keys, preferred_element_type=jnp.float32)
        * scale
    )
    span = queries.shape[1]
    row_pos = lax.broadcasted_iota(jnp.int32, (span, span), 0)
    column_pos = lax.broadcasted_iota(jnp.int32, (span, span), 1)
    own_w = jnp.where(column_pos <= row_pos, jnp.exp(own), 0.0)
    prior_w = jnp.where((column_pos > row_pos) & allow[:, None, None, None], jnp.exp(prior), 0.0)
    total = jnp.sum(own_w, axis=-1, keepdims=True) + jnp.sum(prior_w, axis=-1, keepdims=True)
    own_p = (own_w / total).astype(jnp.bfloat16)
    prior_p = (prior_w / total).astype(jnp.bfloat16)
    return jnp.einsum(
        "bhij,bjhd->bihd", own_p, values, preferred_element_type=jnp.float32
    ) + jnp.einsum("bhij,bjhd->bihd", prior_p, prior_values, preferred_element_type=jnp.float32)


def shards(activations, norm_gain, w_query, w_keyvalue, w_output, log_retain, resets):
    trajs, span, width = activations.shape
    heads_here = log_retain.shape[1]
    inner_here = w_query.shape[1]
    head_dim = inner_here // heads_here
    scale = SCORE_SCALE / math.sqrt(head_dim)
    count = trajs * span
    normed = (rms_rows(activations.astype(jnp.float32), 1e-05) * norm_gain).astype(jnp.bfloat16)
    normed = normed.reshape(count, width)
    ways = lax.axis_size("wloop")
    me = lax.axis_index("wloop")
    block = width // ways

    def feature_block(index):
        return lax.dynamic_slice_in_dim(normed, index * block, block, 1)

    cores = lax.axis_size("heads")
    core = lax.axis_index("heads")
    share_rows = count // cores

    def from_cores(part):
        pieces = [part]
        for step in range(1, cores):
            pieces.append(
                lax.ppermute(part, "heads", [(source, (source + step) % cores) for source in range(cores)])
            )
        order = (core - jnp.arange(cores)) % cores
        return jnp.take(jnp.stack(pieces), order, axis=0).reshape(count, block)

    stacked = [feature_block(me)]
    for step in range(1, ways):
        part = lax.dynamic_slice_in_dim(feature_block((me + step) % ways), core * share_rows, share_rows, 0)
        stacked.append(
            from_cores(
                lax.ppermute(
                    part,
                    "wloop",
                    [(source, (source + step) % ways) for source in range(ways)],
                )
            )
        )

    def gathered_sum(partials, after=None):
        total = partials[0]
        for step in range(1, ways):
            outgoing = partials[step].astype(jnp.bfloat16)
            if after is not None:
                outgoing = lax.optimization_barrier((outgoing, after))[0]
            total = total + lax.ppermute(
                outgoing,
                "wloop",
                [(source, (source - step) % ways) for source in range(ways)],
            ).astype(jnp.float32)
        return total

    pair_raw = gathered_sum(
        [
            jnp.einsum("td,dje->jte", rows, w_keyvalue, preferred_element_type=jnp.float32)
            for rows in stacked
        ]
    )
    query_raw = gathered_sum(
        [jnp.dot(rows, w_query, preferred_element_type=jnp.float32) for rows in stacked],
        after=pair_raw,
    )
    lookup_vectors = rms_rows(pair_raw[0].reshape(trajs, span, heads_here, head_dim), 1e-06).astype(
        jnp.bfloat16
    )
    values = pair_raw[1].reshape(trajs, span, heads_here, head_dim).astype(jnp.bfloat16)
    prior_keys, prior_values = shifted(
        (lookup_vectors.reshape(trajs, span, inner_here), values.reshape(trajs, span, inner_here)),
        "seq",
        1,
    )
    queries = rms_rows(query_raw.reshape(trajs, span, heads_here, head_dim), 1e-06).astype(
        jnp.bfloat16
    )
    keep = (1 - resets[:, 0]).astype(jnp.float32)
    climb = jnp.cumsum(log_retain, axis=-1)
    whole = climb[:, :, -1]
    factor = jnp.exp(whole) * keep[:, None]
    weight = jnp.exp(whole[:, :, None] - climb)
    local_state = jnp.einsum(
        "bht,bthd,bthe->bhde",
        weight,
        lookup_vectors.astype(jnp.float32),
        values.astype(jnp.float32),
        precision=lax.Precision.HIGHEST,
    )
    local_mass = jnp.sum(weight * weight, axis=-1)

    local_both = jnp.concatenate(
        [local_state, jnp.broadcast_to(local_mass[:, :, None, None], local_state.shape[:2] + (1, head_dim))],
        axis=2,
    )
    factor_both = jnp.concatenate(
        [
            jnp.broadcast_to(factor[:, :, None, None], local_state.shape),
            jnp.broadcast_to((factor * factor)[:, :, None, None], local_state.shape[:2] + (1, head_dim)),
        ],
        axis=2,
    )

    def relay_turn(turn, carry):
        return shifted((factor_both * carry + local_both).astype(jnp.bfloat16), "seq", 1).astype(
            jnp.float32
        )

    entering_both = lax.fori_loop(
        0, lax.axis_size("seq") - 1, relay_turn, jnp.zeros_like(local_both)
    )
    entering = entering_both[:, :, :head_dim, :]
    entering_mass = entering_both[:, :, head_dim, 0]
    entering = entering * keep[:, None, None, None]
    entering_mass = entering_mass * keep[:, None]
    read = jnp.einsum(
        "bthd,bhde->bthe", queries.astype(jnp.float32), entering, precision=lax.Precision.HIGHEST
    )
    read = read * jnp.exp(climb).transpose(0, 2, 1)[..., None]
    read = read / jnp.sqrt(head_dim * (1.0 + entering_mass))[:, None, :, None]
    allow = (keep > 0.5) & (lax.axis_index("seq") > 0)
    window = window_mix(
        queries,
        lookup_vectors,
        values,
        prior_keys.reshape(trajs, span, heads_here, head_dim),
        prior_values.reshape(trajs, span, heads_here, head_dim),
        allow,
        scale,
    )
    attended = (window + read).astype(jnp.bfloat16).reshape(count, inner_here)
    w_output = lax.optimization_barrier((w_output, query_raw))[0]
    w_output_rows = lax.all_gather(w_output, "wloop", axis=1, tiled=True)
    cores = lax.axis_size("heads")
    core = lax.axis_index("heads")
    share = width // cores

    def output_share(index):
        return jnp.dot(
            attended,
            lax.dynamic_slice_in_dim(w_output_rows, index * share, share, 1),
            preferred_element_type=jnp.float32,
        )

    received = [
        lax.ppermute(
            output_share((core + step) % cores).astype(jnp.bfloat16),
            "heads",
            [(source, (source + step) % cores) for source in range(cores)],
        )
        for step in range(1, cores)
    ]
    summed = output_share(core)
    for piece in received:
        summed = summed + piece.astype(jnp.float32)
    residual = lax.dynamic_slice_in_dim(
        activations.reshape(count, width), core * share, share, 1
    )
    return (residual.astype(jnp.float32) + summed).astype(jnp.bfloat16).reshape(trajs, span, share)


def solution(mesh):
    placed = (
        P(("groups", "wloop"), "seq", None),
        P(),
        P("wloop", "heads"),
        P("wloop", None, "heads"),
        P("heads", "wloop"),
        P(("groups", "wloop"), "heads", "seq"),
        P(("groups", "wloop"), "seq"),
    )
    return jax.shard_map(
        shards,
        mesh=mesh,
        in_specs=placed,
        out_specs=P(("groups", "wloop"), "seq", "heads"),
        check_vma=False,
    )
```

```python
import math

import jax
import jax.numpy as jnp
from jax import lax
from jax.sharding import PartitionSpec as P

SCORE_SCALE = 2.0


def shifted(value, axis, steps):
    count = lax.axis_size(axis)
    initial, last = (max(0, -steps), min(count, count - steps))
    return lax.ppermute(value, axis, [(source, source + steps) for source in range(initial, last)])


def rms_rows(values, eps):
    return values * lax.rsqrt(jnp.mean(values * values, axis=-1, keepdims=True) + eps)


def window_mix(queries, lookup_vectors, values, prior_keys, prior_values, allow, scale):
    own = (
        jnp.einsum("bihd,bjhd->bhij", queries, lookup_vectors, preferred_element_type=jnp.float32)
        * scale
    )
    prior = (
        jnp.einsum("bihd,bjhd->bhij", queries, prior_keys, preferred_element_type=jnp.float32)
        * scale
    )
    span = queries.shape[1]
    row_pos = lax.broadcasted_iota(jnp.int32, (span, span), 0)
    column_pos = lax.broadcasted_iota(jnp.int32, (span, span), 1)
    own_w = jnp.where(column_pos <= row_pos, jnp.exp(own), 0.0)
    prior_w = jnp.where((column_pos > row_pos) & allow[:, None, None, None], jnp.exp(prior), 0.0)
    total = jnp.sum(own_w, axis=-1, keepdims=True) + jnp.sum(prior_w, axis=-1, keepdims=True)
    own_p = (own_w / total).astype(jnp.bfloat16)
    prior_p = (prior_w / total).astype(jnp.bfloat16)
    return jnp.einsum(
        "bhij,bjhd->bihd", own_p, values, preferred_element_type=jnp.float32
    ) + jnp.einsum("bhij,bjhd->bihd", prior_p, prior_values, preferred_element_type=jnp.float32)


def shards(activations, norm_gain, w_query, w_keyvalue, w_output, log_retain, resets):
    trajs, span, width = activations.shape
    heads_here = log_retain.shape[1]
    inner_here = w_query.shape[1]
    head_dim = inner_here // heads_here
    scale = SCORE_SCALE / math.sqrt(head_dim)
    count = trajs * span
    normed = (rms_rows(activations.astype(jnp.float32), 1e-05) * norm_gain).astype(jnp.bfloat16)
    normed = normed.reshape(count, width)
    ways = lax.axis_size("wloop")
    me = lax.axis_index("wloop")
    block = width // ways

    def feature_block(index):
        return lax.dynamic_slice_in_dim(normed, index * block, block, 1)

    cores = lax.axis_size("heads")
    core = lax.axis_index("heads")
    share_rows = count // cores

    def from_cores(part):
        pieces = [part]
        for step in range(1, cores):
            pieces.append(
                lax.ppermute(part, "heads", [(source, (source + step) % cores) for source in range(cores)])
            )
        order = (core - jnp.arange(cores)) % cores
        return jnp.take(jnp.stack(pieces), order, axis=0).reshape(count, block)

    stacked = [feature_block(me)]
    for step in range(1, ways):
        part = lax.dynamic_slice_in_dim(feature_block((me + step) % ways), core * share_rows, share_rows, 0)
        stacked.append(
            from_cores(
                lax.ppermute(
                    part,
                    "wloop",
                    [(source, (source + step) % ways) for source in range(ways)],
                )
            )
        )

    def gathered_sum(partials, after=None):
        total = partials[0]
        for step in range(1, ways):
            outgoing = partials[step].astype(jnp.bfloat16)
            if after is not None:
                outgoing = lax.optimization_barrier((outgoing, after))[0]
            total = total + lax.ppermute(
                outgoing,
                "wloop",
                [(source, (source - step) % ways) for source in range(ways)],
            ).astype(jnp.float32)
        return total

    pair_raw = gathered_sum(
        [
            jnp.einsum("td,dje->jte", rows, w_keyvalue, preferred_element_type=jnp.float32)
            for rows in stacked
        ]
    )
    query_raw = gathered_sum(
        [jnp.dot(rows, w_query, preferred_element_type=jnp.float32) for rows in stacked],
        after=pair_raw,
    )
    lookup_vectors = rms_rows(pair_raw[0].reshape(trajs, span, heads_here, head_dim), 1e-06).astype(
        jnp.bfloat16
    )
    values = pair_raw[1].reshape(trajs, span, heads_here, head_dim).astype(jnp.bfloat16)
    prior_keys, prior_values = shifted(
        (lookup_vectors.reshape(trajs, span, inner_here), values.reshape(trajs, span, inner_here)),
        "seq",
        1,
    )
    queries = rms_rows(query_raw.reshape(trajs, span, heads_here, head_dim), 1e-06).astype(
        jnp.bfloat16
    )
    keep = (1 - resets[:, 0]).astype(jnp.float32)
    climb = jnp.cumsum(log_retain, axis=-1)
    whole = climb[:, :, -1]
    factor = jnp.exp(whole) * keep[:, None]
    weight = jnp.exp(whole[:, :, None] - climb)
    local_state = jnp.einsum(
        "bht,bthd,bthe->bhde",
        weight,
        lookup_vectors.astype(jnp.float32),
        values.astype(jnp.float32),
        precision=lax.Precision.HIGHEST,
    )
    local_mass = jnp.sum(weight * weight, axis=-1)

    local_both = jnp.concatenate(
        [local_state, jnp.broadcast_to(local_mass[:, :, None, None], local_state.shape[:2] + (1, head_dim))],
        axis=2,
    )
    factor_both = jnp.concatenate(
        [
            jnp.broadcast_to(factor[:, :, None, None], local_state.shape),
            jnp.broadcast_to((factor * factor)[:, :, None, None], local_state.shape[:2] + (1, head_dim)),
        ],
        axis=2,
    )

    def relay_turn(turn, carry):
        return shifted((factor_both * carry + local_both).astype(jnp.bfloat16), "seq", 1).astype(
            jnp.float32
        )

    local_both, prior_keys, prior_values = lax.optimization_barrier((local_both, prior_keys, prior_values))
    entering_both = lax.fori_loop(
        0, lax.axis_size("seq") - 1, relay_turn, jnp.zeros_like(local_both)
    )
    entering = entering_both[:, :, :head_dim, :]
    entering_mass = entering_both[:, :, head_dim, 0]
    entering = entering * keep[:, None, None, None]
    entering_mass = entering_mass * keep[:, None]
    read = jnp.einsum(
        "bthd,bhde->bthe", queries.astype(jnp.float32), entering, precision=lax.Precision.HIGHEST
    )
    read = read * jnp.exp(climb).transpose(0, 2, 1)[..., None]
    read = read / jnp.sqrt(head_dim * (1.0 + entering_mass))[:, None, :, None]
    allow = (keep > 0.5) & (lax.axis_index("seq") > 0)
    window = window_mix(
        queries,
        lookup_vectors,
        values,
        prior_keys.reshape(trajs, span, heads_here, head_dim),
        prior_values.reshape(trajs, span, heads_here, head_dim),
        allow,
        scale,
    )
    attended = (window + read).astype(jnp.bfloat16).reshape(count, inner_here)
    w_output = lax.optimization_barrier((w_output, pair_raw))[0]
    w_output_rows = lax.all_gather(w_output, "wloop", axis=1, tiled=True)
    cores = lax.axis_size("heads")
    core = lax.axis_index("heads")
    share = width // cores

    def output_share(index):
        return jnp.dot(
            attended,
            lax.dynamic_slice_in_dim(w_output_rows, index * share, share, 1),
            preferred_element_type=jnp.float32,
        )

    received = [
        lax.ppermute(
            output_share((core + step) % cores).astype(jnp.bfloat16),
            "heads",
            [(source, (source + step) % cores) for source in range(cores)],
        )
        for step in range(1, cores)
    ]
    summed = output_share(core)
    for piece in received:
        summed = summed + piece.astype(jnp.float32)
    residual = lax.dynamic_slice_in_dim(
        activations.reshape(count, width), core * share, share, 1
    )
    return (residual.astype(jnp.float32) + summed).astype(jnp.bfloat16).reshape(trajs, span, share)


def solution(mesh):
    placed = (
        P(("groups", "wloop"), "seq", None),
        P(),
        P("wloop", "heads"),
        P("wloop", None, "heads"),
        P("heads", "wloop"),
        P(("groups", "wloop"), "heads", "seq"),
        P(("groups", "wloop"), "seq"),
    )
    return jax.shard_map(
        shards,
        mesh=mesh,
        in_specs=placed,
        out_specs=P(("groups", "wloop"), "seq", "heads"),
        check_vma=False,
    )
```

```python
import math

import jax
import jax.numpy as jnp
from jax import lax
from jax.sharding import PartitionSpec as P

SCORE_SCALE = 2.0


def shifted(value, axis, steps):
    count = lax.axis_size(axis)
    initial, last = (max(0, -steps), min(count, count - steps))
    return lax.ppermute(value, axis, [(source, source + steps) for source in range(initial, last)])


def rms_rows(values, eps):
    return values * lax.rsqrt(jnp.mean(values * values, axis=-1, keepdims=True) + eps)


def window_mix(queries, lookup_vectors, values, prior_keys, prior_values, allow, scale):
    own = (
        jnp.einsum("bihd,bjhd->bhij", queries, lookup_vectors, preferred_element_type=jnp.float32)
        * scale
    )
    prior = (
        jnp.einsum("bihd,bjhd->bhij", queries, prior_keys, preferred_element_type=jnp.float32)
        * scale
    )
    span = queries.shape[1]
    row_pos = lax.broadcasted_iota(jnp.int32, (span, span), 0)
    column_pos = lax.broadcasted_iota(jnp.int32, (span, span), 1)
    own_w = jnp.where(column_pos <= row_pos, jnp.exp(own), 0.0)
    prior_w = jnp.where((column_pos > row_pos) & allow[:, None, None, None], jnp.exp(prior), 0.0)
    total = jnp.sum(own_w, axis=-1, keepdims=True) + jnp.sum(prior_w, axis=-1, keepdims=True)
    own_p = (own_w / total).astype(jnp.bfloat16)
    prior_p = (prior_w / total).astype(jnp.bfloat16)
    return jnp.einsum(
        "bhij,bjhd->bihd", own_p, values, preferred_element_type=jnp.float32
    ) + jnp.einsum("bhij,bjhd->bihd", prior_p, prior_values, preferred_element_type=jnp.float32)


def shards(activations, norm_gain, w_query, w_keyvalue, w_output, log_retain, resets):
    trajs, span, width = activations.shape
    heads_here = log_retain.shape[1]
    inner_here = w_query.shape[1]
    head_dim = inner_here // heads_here
    scale = SCORE_SCALE / math.sqrt(head_dim)
    count = trajs * span
    normed = (rms_rows(activations.astype(jnp.float32), 1e-05) * norm_gain).astype(jnp.bfloat16)
    normed = normed.reshape(count, width)
    ways = lax.axis_size("wloop")
    me = lax.axis_index("wloop")
    block = width // ways

    def feature_block(index):
        return lax.dynamic_slice_in_dim(normed, index * block, block, 1)

    cores = lax.axis_size("heads")
    core = lax.axis_index("heads")
    share_rows = count // cores

    def from_cores(part):
        pieces = [part]
        for step in range(1, cores):
            pieces.append(
                lax.ppermute(part, "heads", [(source, (source + step) % cores) for source in range(cores)])
            )
        order = (core - jnp.arange(cores)) % cores
        return jnp.take(jnp.stack(pieces), order, axis=0).reshape(count, block)

    stacked = [feature_block(me)]
    for step in range(1, ways):
        part = lax.dynamic_slice_in_dim(feature_block((me + step) % ways), core * share_rows, share_rows, 0)
        stacked.append(
            from_cores(
                lax.ppermute(
                    part,
                    "wloop",
                    [(source, (source + step) % ways) for source in range(ways)],
                )
            )
        )

    def gathered_sum(partials, after=None):
        total = partials[0]
        for step in range(1, ways):
            outgoing = partials[step].astype(jnp.bfloat16)
            if after is not None:
                outgoing = lax.optimization_barrier((outgoing, after))[0]
            total = total + lax.ppermute(
                outgoing,
                "wloop",
                [(source, (source - step) % ways) for source in range(ways)],
            ).astype(jnp.float32)
        return total

    pair_raw = gathered_sum(
        [
            jnp.einsum("td,dje->jte", rows, w_keyvalue, preferred_element_type=jnp.float32)
            for rows in stacked
        ]
    )
    query_raw = gathered_sum(
        [jnp.dot(rows, w_query, preferred_element_type=jnp.float32) for rows in stacked],
        after=pair_raw,
    )
    lookup_vectors = rms_rows(pair_raw[0].reshape(trajs, span, heads_here, head_dim), 1e-06).astype(
        jnp.bfloat16
    )
    values = pair_raw[1].reshape(trajs, span, heads_here, head_dim).astype(jnp.bfloat16)
    prior_keys, prior_values = shifted(
        (lookup_vectors.reshape(trajs, span, inner_here), values.reshape(trajs, span, inner_here)),
        "seq",
        1,
    )
    queries = rms_rows(query_raw.reshape(trajs, span, heads_here, head_dim), 1e-06).astype(
        jnp.bfloat16
    )
    keep = (1 - resets[:, 0]).astype(jnp.float32)
    climb = jnp.cumsum(log_retain, axis=-1)
    whole = climb[:, :, -1]
    factor = jnp.exp(whole) * keep[:, None]
    weight = jnp.exp(whole[:, :, None] - climb)
    local_state = jnp.einsum(
        "bht,bthd,bthe->bhde",
        weight,
        lookup_vectors.astype(jnp.float32),
        values.astype(jnp.float32),
        precision=lax.Precision.HIGHEST,
    )
    local_mass = jnp.sum(weight * weight, axis=-1)

    local_both = jnp.concatenate(
        [local_state, jnp.broadcast_to(local_mass[:, :, None, None], local_state.shape[:2] + (1, head_dim))],
        axis=2,
    )
    factor_both = jnp.concatenate(
        [
            jnp.broadcast_to(factor[:, :, None, None], local_state.shape),
            jnp.broadcast_to((factor * factor)[:, :, None, None], local_state.shape[:2] + (1, head_dim)),
        ],
        axis=2,
    )

    def relay_turn(turn, carry):
        return shifted((factor_both * carry + local_both).astype(jnp.bfloat16), "seq", 1).astype(
            jnp.float32
        )

    local_both, prior_keys, prior_values = lax.optimization_barrier((local_both, prior_keys, prior_values))
    entering_both = jnp.zeros_like(local_both)
    for turn in range(lax.axis_size("seq") - 1):
        entering_both = relay_turn(turn, entering_both)
    entering = entering_both[:, :, :head_dim, :]
    entering_mass = entering_both[:, :, head_dim, 0]
    entering = entering * keep[:, None, None, None]
    entering_mass = entering_mass * keep[:, None]
    read = jnp.einsum(
        "bthd,bhde->bthe", queries.astype(jnp.float32), entering, precision=lax.Precision.HIGHEST
    )
    read = read * jnp.exp(climb).transpose(0, 2, 1)[..., None]
    read = read / jnp.sqrt(head_dim * (1.0 + entering_mass))[:, None, :, None]
    allow = (keep > 0.5) & (lax.axis_index("seq") > 0)
    window = window_mix(
        queries,
        lookup_vectors,
        values,
        prior_keys.reshape(trajs, span, heads_here, head_dim),
        prior_values.reshape(trajs, span, heads_here, head_dim),
        allow,
        scale,
    )
    attended = (window + read).astype(jnp.bfloat16).reshape(count, inner_here)
    w_output = lax.optimization_barrier((w_output, pair_raw))[0]
    w_output_rows = lax.all_gather(w_output, "wloop", axis=1, tiled=True)
    cores = lax.axis_size("heads")
    core = lax.axis_index("heads")
    share = width // cores

    def output_share(index):
        return jnp.dot(
            attended,
            lax.dynamic_slice_in_dim(w_output_rows, index * share, share, 1),
            preferred_element_type=jnp.float32,
        )

    received = [
        lax.ppermute(
            output_share((core + step) % cores).astype(jnp.bfloat16),
            "heads",
            [(source, (source + step) % cores) for source in range(cores)],
        )
        for step in range(1, cores)
    ]
    summed = output_share(core)
    for piece in received:
        summed = summed + piece.astype(jnp.float32)
    residual = lax.dynamic_slice_in_dim(
        activations.reshape(count, width), core * share, share, 1
    )
    return (residual.astype(jnp.float32) + summed).astype(jnp.bfloat16).reshape(trajs, span, share)


def solution(mesh):
    placed = (
        P(("groups", "wloop"), "seq", None),
        P(),
        P("wloop", "heads"),
        P("wloop", None, "heads"),
        P("heads", "wloop"),
        P(("groups", "wloop"), "heads", "seq"),
        P(("groups", "wloop"), "seq"),
    )
    return jax.shard_map(
        shards,
        mesh=mesh,
        in_specs=placed,
        out_specs=P(("groups", "wloop"), "seq", "heads"),
        check_vma=False,
    )
```

```python
import math

import jax
import jax.numpy as jnp
from jax import lax
from jax.sharding import PartitionSpec as P

SCORE_SCALE = 2.0


def shifted(value, axis, steps):
    count = lax.axis_size(axis)
    initial, last = (max(0, -steps), min(count, count - steps))
    return lax.ppermute(value, axis, [(source, source + steps) for source in range(initial, last)])


def rms_rows(values, eps):
    return values * lax.rsqrt(jnp.mean(values * values, axis=-1, keepdims=True) + eps)


def window_mix(queries, lookup_vectors, values, prior_keys, prior_values, allow, scale):
    own = (
        jnp.einsum("bihd,bjhd->bhij", queries, lookup_vectors, preferred_element_type=jnp.float32)
        * scale
    )
    prior = (
        jnp.einsum("bihd,bjhd->bhij", queries, prior_keys, preferred_element_type=jnp.float32)
        * scale
    )
    span = queries.shape[1]
    row_pos = lax.broadcasted_iota(jnp.int32, (span, span), 0)
    column_pos = lax.broadcasted_iota(jnp.int32, (span, span), 1)
    own_w = jnp.where(column_pos <= row_pos, jnp.exp(own), 0.0)
    prior_w = jnp.where((column_pos > row_pos) & allow[:, None, None, None], jnp.exp(prior), 0.0)
    total = jnp.sum(own_w, axis=-1, keepdims=True) + jnp.sum(prior_w, axis=-1, keepdims=True)
    own_p = (own_w / total).astype(jnp.bfloat16)
    prior_p = (prior_w / total).astype(jnp.bfloat16)
    return jnp.einsum(
        "bhij,bjhd->bihd", own_p, values, preferred_element_type=jnp.float32
    ) + jnp.einsum("bhij,bjhd->bihd", prior_p, prior_values, preferred_element_type=jnp.float32)


def shards(activations, norm_gain, w_query, w_keyvalue, w_output, log_retain, resets):
    trajs, span, width = activations.shape
    heads_here = log_retain.shape[1]
    inner_here = w_query.shape[1]
    head_dim = inner_here // heads_here
    scale = SCORE_SCALE / math.sqrt(head_dim)
    count = trajs * span
    normed = (rms_rows(activations.astype(jnp.float32), 1e-05) * norm_gain).astype(jnp.bfloat16)
    normed = normed.reshape(count, width)
    ways = lax.axis_size("wloop")
    me = lax.axis_index("wloop")
    block = width // ways

    def feature_block(index):
        return lax.dynamic_slice_in_dim(normed, index * block, block, 1)

    cores = lax.axis_size("heads")
    core = lax.axis_index("heads")
    share_rows = count // cores

    def from_cores(part):
        pieces = [part]
        for step in range(1, cores):
            pieces.append(
                lax.ppermute(part, "heads", [(source, (source + step) % cores) for source in range(cores)])
            )
        order = (core - jnp.arange(cores)) % cores
        return jnp.take(jnp.stack(pieces), order, axis=0).reshape(count, block)

    stacked = [feature_block(me)]
    for step in range(1, ways):
        part = lax.dynamic_slice_in_dim(feature_block((me + step) % ways), core * share_rows, share_rows, 0)
        stacked.append(
            from_cores(
                lax.ppermute(
                    part,
                    "wloop",
                    [(source, (source + step) % ways) for source in range(ways)],
                )
            )
        )

    def gathered_sum(partials, after=None):
        total = partials[0]
        for step in range(1, ways):
            outgoing = partials[step].astype(jnp.bfloat16)
            if after is not None:
                outgoing = lax.optimization_barrier((outgoing, after))[0]
            total = total + lax.ppermute(
                outgoing,
                "wloop",
                [(source, (source - step) % ways) for source in range(ways)],
            ).astype(jnp.float32)
        return total

    pair_raw = gathered_sum(
        [
            jnp.einsum("td,dje->jte", rows, w_keyvalue, preferred_element_type=jnp.float32)
            for rows in stacked
        ]
    )
    query_raw = gathered_sum(
        [jnp.dot(rows, w_query, preferred_element_type=jnp.float32) for rows in stacked],
        after=pair_raw,
    )
    lookup_vectors = rms_rows(pair_raw[0].reshape(trajs, span, heads_here, head_dim), 1e-06).astype(
        jnp.bfloat16
    )
    values = pair_raw[1].reshape(trajs, span, heads_here, head_dim).astype(jnp.bfloat16)
    prior_keys, prior_values = shifted(
        (lookup_vectors.reshape(trajs, span, inner_here), values.reshape(trajs, span, inner_here)),
        "seq",
        1,
    )
    queries = rms_rows(query_raw.reshape(trajs, span, heads_here, head_dim), 1e-06).astype(
        jnp.bfloat16
    )
    keep = (1 - resets[:, 0]).astype(jnp.float32)
    climb = jnp.cumsum(log_retain, axis=-1)
    whole = climb[:, :, -1]
    factor = jnp.exp(whole) * keep[:, None]
    weight = jnp.exp(whole[:, :, None] - climb)
    weighted = weight.transpose(0, 2, 1)[..., None] * lookup_vectors.astype(jnp.float32)
    weighted_hi = weighted.astype(jnp.bfloat16)
    weighted_lo = (weighted - weighted_hi.astype(jnp.float32)).astype(jnp.bfloat16)
    local_state = jnp.einsum(
        "bthd,bthe->bhde", weighted_hi, values, preferred_element_type=jnp.float32
    ) + jnp.einsum("bthd,bthe->bhde", weighted_lo, values, preferred_element_type=jnp.float32)
    local_mass = jnp.sum(weight * weight, axis=-1)

    local_both = jnp.concatenate(
        [local_state, jnp.broadcast_to(local_mass[:, :, None, None], local_state.shape[:2] + (1, head_dim))],
        axis=2,
    )
    factor_both = jnp.concatenate(
        [
            jnp.broadcast_to(factor[:, :, None, None], local_state.shape),
            jnp.broadcast_to((factor * factor)[:, :, None, None], local_state.shape[:2] + (1, head_dim)),
        ],
        axis=2,
    )

    def relay_turn(turn, carry):
        return shifted((factor_both * carry + local_both).astype(jnp.bfloat16), "seq", 1).astype(
            jnp.float32
        )

    local_both, prior_keys, prior_values = lax.optimization_barrier((local_both, prior_keys, prior_values))
    entering_both = jnp.zeros_like(local_both)
    for turn in range(lax.axis_size("seq") - 1):
        entering_both = relay_turn(turn, entering_both)
    entering = entering_both[:, :, :head_dim, :]
    entering_mass = entering_both[:, :, head_dim, 0]
    entering = entering * keep[:, None, None, None]
    entering_mass = entering_mass * keep[:, None]
    read = jnp.einsum(
        "bthd,bhde->bthe", queries, entering.astype(jnp.bfloat16), preferred_element_type=jnp.float32
    )
    read = read * jnp.exp(climb).transpose(0, 2, 1)[..., None]
    read = read / jnp.sqrt(head_dim * (1.0 + entering_mass))[:, None, :, None]
    allow = (keep > 0.5) & (lax.axis_index("seq") > 0)
    window = window_mix(
        queries,
        lookup_vectors,
        values,
        prior_keys.reshape(trajs, span, heads_here, head_dim),
        prior_values.reshape(trajs, span, heads_here, head_dim),
        allow,
        scale,
    )
    attended = (window + read).astype(jnp.bfloat16).reshape(count, inner_here)
    w_output = lax.optimization_barrier((w_output, pair_raw))[0]
    w_output_rows = lax.all_gather(w_output, "wloop", axis=1, tiled=True)
    cores = lax.axis_size("heads")
    core = lax.axis_index("heads")
    share = width // cores

    def output_share(index):
        return jnp.dot(
            attended,
            lax.dynamic_slice_in_dim(w_output_rows, index * share, share, 1),
            preferred_element_type=jnp.float32,
        )

    received = [
        lax.ppermute(
            output_share((core + step) % cores).astype(jnp.bfloat16),
            "heads",
            [(source, (source + step) % cores) for source in range(cores)],
        )
        for step in range(1, cores)
    ]
    summed = output_share(core)
    for piece in received:
        summed = summed + piece.astype(jnp.float32)
    residual = lax.dynamic_slice_in_dim(
        activations.reshape(count, width), core * share, share, 1
    )
    return (residual.astype(jnp.float32) + summed).astype(jnp.bfloat16).reshape(trajs, span, share)


def solution(mesh):
    placed = (
        P(("groups", "wloop"), "seq", None),
        P(),
        P("wloop", "heads"),
        P("wloop", None, "heads"),
        P("heads", "wloop"),
        P(("groups", "wloop"), "heads", "seq"),
        P(("groups", "wloop"), "seq"),
    )
    return jax.shard_map(
        shards,
        mesh=mesh,
        in_specs=placed,
        out_specs=P(("groups", "wloop"), "seq", "heads"),
        check_vma=False,
    )
```

```python
import math

import jax
import jax.numpy as jnp
from jax import lax
from jax.sharding import PartitionSpec as P

SCORE_SCALE = 2.0


def shifted(value, axis, steps):
    count = lax.axis_size(axis)
    initial, last = (max(0, -steps), min(count, count - steps))
    return lax.ppermute(value, axis, [(source, source + steps) for source in range(initial, last)])


def rms_rows(values, eps):
    return values * lax.rsqrt(jnp.mean(values * values, axis=-1, keepdims=True) + eps)


def window_mix(queries, lookup_vectors, values, prior_keys, prior_values, allow, scale):
    own = (
        jnp.einsum("bihd,bjhd->bhij", queries, lookup_vectors, preferred_element_type=jnp.float32)
        * scale
    )
    prior = (
        jnp.einsum("bihd,bjhd->bhij", queries, prior_keys, preferred_element_type=jnp.float32)
        * scale
    )
    span = queries.shape[1]
    row_pos = lax.broadcasted_iota(jnp.int32, (span, span), 0)
    column_pos = lax.broadcasted_iota(jnp.int32, (span, span), 1)
    own_w = jnp.where(column_pos <= row_pos, jnp.exp(own), 0.0)
    prior_w = jnp.where((column_pos > row_pos) & allow[:, None, None, None], jnp.exp(prior), 0.0)
    total = jnp.sum(own_w, axis=-1, keepdims=True) + jnp.sum(prior_w, axis=-1, keepdims=True)
    own_p = (own_w / total).astype(jnp.bfloat16)
    prior_p = (prior_w / total).astype(jnp.bfloat16)
    return jnp.einsum(
        "bhij,bjhd->bihd", own_p, values, preferred_element_type=jnp.float32
    ) + jnp.einsum("bhij,bjhd->bihd", prior_p, prior_values, preferred_element_type=jnp.float32)


def shards(activations, norm_gain, w_query, w_keyvalue, w_output, log_retain, resets):
    trajs, span, width = activations.shape
    heads_here = log_retain.shape[1]
    inner_here = w_query.shape[1]
    head_dim = inner_here // heads_here
    scale = SCORE_SCALE / math.sqrt(head_dim)
    count = trajs * span
    normed = (rms_rows(activations.astype(jnp.float32), 1e-05) * norm_gain).astype(jnp.bfloat16)
    normed = normed.reshape(count, width)
    ways = lax.axis_size("wloop")
    me = lax.axis_index("wloop")
    block = width // ways

    def feature_block(index):
        return lax.dynamic_slice_in_dim(normed, index * block, block, 1)

    cores = lax.axis_size("heads")
    core = lax.axis_index("heads")
    share_rows = count // cores

    def from_cores(part):
        pieces = [part]
        for step in range(1, cores):
            pieces.append(
                lax.ppermute(part, "heads", [(source, (source + step) % cores) for source in range(cores)])
            )
        order = (core - jnp.arange(cores)) % cores
        return jnp.take(jnp.stack(pieces), order, axis=0).reshape(count, block)

    stacked = [feature_block(me)]
    for step in range(1, ways):
        part = lax.dynamic_slice_in_dim(feature_block((me + step) % ways), core * share_rows, share_rows, 0)
        stacked.append(
            from_cores(
                lax.ppermute(
                    part,
                    "wloop",
                    [(source, (source + step) % ways) for source in range(ways)],
                )
            )
        )

    def gathered_sum(partials, after=None):
        total = partials[0]
        for step in range(1, ways):
            outgoing = partials[step].astype(jnp.bfloat16)
            if after is not None:
                outgoing = lax.optimization_barrier((outgoing, after))[0]
            total = total + lax.ppermute(
                outgoing,
                "wloop",
                [(source, (source - step) % ways) for source in range(ways)],
            ).astype(jnp.float32)
        return total

    pair_raw = gathered_sum(
        [
            jnp.einsum("td,dje->jte", rows, w_keyvalue, preferred_element_type=jnp.float32)
            for rows in stacked
        ]
    )
    query_raw = gathered_sum(
        [jnp.dot(rows, w_query, preferred_element_type=jnp.float32) for rows in stacked],
        after=pair_raw,
    )
    lookup_vectors = rms_rows(pair_raw[0].reshape(trajs, span, heads_here, head_dim), 1e-06).astype(
        jnp.bfloat16
    )
    values = pair_raw[1].reshape(trajs, span, heads_here, head_dim).astype(jnp.bfloat16)
    prior_keys, prior_values = shifted(
        (lookup_vectors.reshape(trajs, span, inner_here), values.reshape(trajs, span, inner_here)),
        "seq",
        1,
    )
    queries = rms_rows(query_raw.reshape(trajs, span, heads_here, head_dim), 1e-06).astype(
        jnp.bfloat16
    )
    keep = (1 - resets[:, 0]).astype(jnp.float32)
    climb = jnp.cumsum(log_retain, axis=-1)
    whole = climb[:, :, -1]
    factor = jnp.exp(whole) * keep[:, None]
    weight = jnp.exp(whole[:, :, None] - climb)
    local_state = jnp.einsum(
        "bht,bthd,bthe->bhde",
        weight,
        lookup_vectors.astype(jnp.float32),
        values.astype(jnp.float32),
        precision=lax.Precision.HIGHEST,
    )
    local_mass = jnp.sum(weight * weight, axis=-1)

    def as_block(per_head):
        padded = jnp.pad(per_head, ((0, 0), (0, head_dim * head_dim - heads_here)))
        return padded.reshape(trajs, 1, head_dim, head_dim)

    local_both = jnp.concatenate([local_state, as_block(local_mass)], axis=1)
    factor_both = jnp.concatenate(
        [jnp.broadcast_to(factor[:, :, None, None], local_state.shape), as_block(factor * factor)],
        axis=1,
    )

    def relay_turn(turn, carry):
        return shifted((factor_both * carry + local_both).astype(jnp.bfloat16), "seq", 1).astype(
            jnp.float32
        )

    local_both, prior_keys, prior_values = lax.optimization_barrier((local_both, prior_keys, prior_values))
    entering_both = jnp.zeros_like(local_both)
    for turn in range(lax.axis_size("seq") - 1):
        entering_both = relay_turn(turn, entering_both)
    entering = entering_both[:, :heads_here]
    entering_mass = entering_both[:, heads_here].reshape(trajs, head_dim * head_dim)[:, :heads_here]
    entering = entering * keep[:, None, None, None]
    entering_mass = entering_mass * keep[:, None]
    read = jnp.einsum(
        "bthd,bhde->bthe", queries, entering.astype(jnp.bfloat16), preferred_element_type=jnp.float32
    )
    read = read * jnp.exp(climb).transpose(0, 2, 1)[..., None]
    read = read / jnp.sqrt(head_dim * (1.0 + entering_mass))[:, None, :, None]
    allow = (keep > 0.5) & (lax.axis_index("seq") > 0)
    window = window_mix(
        queries,
        lookup_vectors,
        values,
        prior_keys.reshape(trajs, span, heads_here, head_dim),
        prior_values.reshape(trajs, span, heads_here, head_dim),
        allow,
        scale,
    )
    attended = (window + read).astype(jnp.bfloat16).reshape(count, inner_here)
    w_output = lax.optimization_barrier((w_output, pair_raw))[0]
    w_output_rows = lax.all_gather(w_output, "wloop", axis=1, tiled=True)
    cores = lax.axis_size("heads")
    core = lax.axis_index("heads")
    share = width // cores

    def output_share(index):
        return jnp.dot(
            attended,
            lax.dynamic_slice_in_dim(w_output_rows, index * share, share, 1),
            preferred_element_type=jnp.float32,
        )

    received = [
        lax.ppermute(
            output_share((core + step) % cores).astype(jnp.bfloat16),
            "heads",
            [(source, (source + step) % cores) for source in range(cores)],
        )
        for step in range(1, cores)
    ]
    summed = output_share(core)
    for piece in received:
        summed = summed + piece.astype(jnp.float32)
    residual = lax.dynamic_slice_in_dim(
        activations.reshape(count, width), core * share, share, 1
    )
    return (residual.astype(jnp.float32) + summed).astype(jnp.bfloat16).reshape(trajs, span, share)


def solution(mesh):
    placed = (
        P(("groups", "wloop"), "seq", None),
        P(),
        P("wloop", "heads"),
        P("wloop", None, "heads"),
        P("heads", "wloop"),
        P(("groups", "wloop"), "heads", "seq"),
        P(("groups", "wloop"), "seq"),
    )
    return jax.shard_map(
        shards,
        mesh=mesh,
        in_specs=placed,
        out_specs=P(("groups", "wloop"), "seq", "heads"),
        check_vma=False,
    )
```

```python
import math

import jax
import jax.numpy as jnp
from jax import lax
from jax.sharding import PartitionSpec as P

SCORE_SCALE = 2.0


def shifted(value, axis, steps):
    count = lax.axis_size(axis)
    initial, last = (max(0, -steps), min(count, count - steps))
    return lax.ppermute(value, axis, [(source, source + steps) for source in range(initial, last)])


def rms_rows(values, eps):
    return values * lax.rsqrt(jnp.mean(values * values, axis=-1, keepdims=True) + eps)


def window_mix(queries, lookup_vectors, values, prior_keys, prior_values, allow, scale):
    own = (
        jnp.einsum("bihd,bjhd->bhij", queries, lookup_vectors, preferred_element_type=jnp.float32)
        * scale
    )
    prior = (
        jnp.einsum("bihd,bjhd->bhij", queries, prior_keys, preferred_element_type=jnp.float32)
        * scale
    )
    span = queries.shape[1]
    row_pos = lax.broadcasted_iota(jnp.int32, (span, span), 0)
    column_pos = lax.broadcasted_iota(jnp.int32, (span, span), 1)
    own_w = jnp.where(column_pos <= row_pos, jnp.exp(own), 0.0)
    prior_w = jnp.where((column_pos > row_pos) & allow[:, None, None, None], jnp.exp(prior), 0.0)
    total = jnp.sum(own_w, axis=-1, keepdims=True) + jnp.sum(prior_w, axis=-1, keepdims=True)
    own_p = (own_w / total).astype(jnp.bfloat16)
    prior_p = (prior_w / total).astype(jnp.bfloat16)
    return jnp.einsum(
        "bhij,bjhd->bihd", own_p, values, preferred_element_type=jnp.float32
    ) + jnp.einsum("bhij,bjhd->bihd", prior_p, prior_values, preferred_element_type=jnp.float32)


def shards(activations, norm_gain, w_query, w_keyvalue, w_output, log_retain, resets):
    trajs, span, width = activations.shape
    heads_here = log_retain.shape[1]
    inner_here = w_query.shape[1]
    head_dim = inner_here // heads_here
    scale = SCORE_SCALE / math.sqrt(head_dim)
    count = trajs * span
    normed = (rms_rows(activations.astype(jnp.float32), 1e-05) * norm_gain).astype(jnp.bfloat16)
    normed = normed.reshape(count, width)
    ways = lax.axis_size("wloop")
    me = lax.axis_index("wloop")
    block = width // ways

    def feature_block(index):
        return lax.dynamic_slice_in_dim(normed, index * block, block, 1)

    cores = lax.axis_size("heads")
    core = lax.axis_index("heads")
    share_rows = count // cores

    def from_cores(part):
        pieces = [part]
        for step in range(1, cores):
            pieces.append(
                lax.ppermute(part, "heads", [(source, (source + step) % cores) for source in range(cores)])
            )
        order = (core - jnp.arange(cores)) % cores
        return jnp.take(jnp.stack(pieces), order, axis=0).reshape(count, block)

    stacked = [feature_block(me)]
    for step in range(1, ways):
        part = lax.dynamic_slice_in_dim(feature_block((me + step) % ways), core * share_rows, share_rows, 0)
        stacked.append(
            from_cores(
                lax.ppermute(
                    part,
                    "wloop",
                    [(source, (source + step) % ways) for source in range(ways)],
                )
            )
        )

    def gathered_sum(partials, after=None):
        total = partials[0]
        for step in range(1, ways):
            outgoing = partials[step].astype(jnp.bfloat16)
            if after is not None:
                outgoing = lax.optimization_barrier((outgoing, after))[0]
            total = total + lax.ppermute(
                outgoing,
                "wloop",
                [(source, (source - step) % ways) for source in range(ways)],
            ).astype(jnp.float32)
        return total

    pair_raw = jnp.stack(
        [
            gathered_sum(
                [jnp.dot(rows, w_keyvalue[:, kind, :], preferred_element_type=jnp.float32) for rows in stacked]
            )
            for kind in range(2)
        ]
    )
    query_raw = gathered_sum(
        [jnp.dot(rows, w_query, preferred_element_type=jnp.float32) for rows in stacked],
        after=pair_raw,
    )
    lookup_vectors = rms_rows(pair_raw[0].reshape(trajs, span, heads_here, head_dim), 1e-06).astype(
        jnp.bfloat16
    )
    values = pair_raw[1].reshape(trajs, span, heads_here, head_dim).astype(jnp.bfloat16)
    prior_both = shifted(
        jnp.concatenate(
            [lookup_vectors.reshape(trajs, span, inner_here), values.reshape(trajs, span, inner_here)],
            axis=-1,
        ),
        "seq",
        1,
    )
    prior_keys, prior_values = prior_both[..., :inner_here], prior_both[..., inner_here:]
    queries = rms_rows(query_raw.reshape(trajs, span, heads_here, head_dim), 1e-06).astype(
        jnp.bfloat16
    )
    keep = (1 - resets[:, 0]).astype(jnp.float32)
    climb = jnp.cumsum(log_retain, axis=-1)
    whole = climb[:, :, -1]
    factor = jnp.exp(whole) * keep[:, None]
    weight = jnp.exp(whole[:, :, None] - climb)
    local_state = jnp.einsum(
        "bht,bthd,bthe->bhde",
        weight,
        lookup_vectors.astype(jnp.float32),
        values.astype(jnp.float32),
        precision=lax.Precision.HIGHEST,
    )
    local_mass = jnp.sum(weight * weight, axis=-1)

    def as_block(per_head):
        padded = jnp.pad(per_head, ((0, 0), (0, head_dim * head_dim - heads_here)))
        return padded.reshape(trajs, 1, head_dim, head_dim)

    local_both = jnp.concatenate([local_state, as_block(local_mass)], axis=1)
    factor_both = jnp.concatenate(
        [jnp.broadcast_to(factor[:, :, None, None], local_state.shape), as_block(factor * factor)],
        axis=1,
    )

    def relay_turn(turn, carry):
        return shifted((factor_both * carry + local_both).astype(jnp.bfloat16), "seq", 1).astype(
            jnp.float32
        )

    local_both, prior_keys, prior_values = lax.optimization_barrier((local_both, prior_keys, prior_values))
    entering_both = jnp.zeros_like(local_both)
    for turn in range(lax.axis_size("seq") - 1):
        entering_both = relay_turn(turn, entering_both)
    entering = entering_both[:, :heads_here]
    entering_mass = entering_both[:, heads_here].reshape(trajs, head_dim * head_dim)[:, :heads_here]
    entering = entering * keep[:, None, None, None]
    entering_mass = entering_mass * keep[:, None]
    read = jnp.einsum(
        "bthd,bhde->bthe", queries, entering.astype(jnp.bfloat16), preferred_element_type=jnp.float32
    )
    read = read * jnp.exp(climb).transpose(0, 2, 1)[..., None]
    read = read / jnp.sqrt(head_dim * (1.0 + entering_mass))[:, None, :, None]
    allow = (keep > 0.5) & (lax.axis_index("seq") > 0)
    window = window_mix(
        queries,
        lookup_vectors,
        values,
        prior_keys.reshape(trajs, span, heads_here, head_dim),
        prior_values.reshape(trajs, span, heads_here, head_dim),
        allow,
        scale,
    )
    attended = (window + read).astype(jnp.bfloat16).reshape(count, inner_here)
    w_output = lax.optimization_barrier((w_output, pair_raw))[0]
    w_output_rows = lax.all_gather(w_output, "wloop", axis=1, tiled=True)
    cores = lax.axis_size("heads")
    core = lax.axis_index("heads")
    share = width // cores

    def output_share(index):
        return jnp.dot(
            attended,
            lax.dynamic_slice_in_dim(w_output_rows, index * share, share, 1),
            preferred_element_type=jnp.float32,
        )

    received = [
        lax.ppermute(
            output_share((core + step) % cores).astype(jnp.bfloat16),
            "heads",
            [(source, (source + step) % cores) for source in range(cores)],
        )
        for step in range(1, cores)
    ]
    summed = output_share(core)
    for piece in received:
        summed = summed + piece.astype(jnp.float32)
    residual = lax.dynamic_slice_in_dim(
        activations.reshape(count, width), core * share, share, 1
    )
    return (residual.astype(jnp.float32) + summed).astype(jnp.bfloat16).reshape(trajs, span, share)


def solution(mesh):
    placed = (
        P(("groups", "wloop"), "seq", None),
        P(),
        P("wloop", "heads"),
        P("wloop", None, "heads"),
        P("heads", "wloop"),
        P(("groups", "wloop"), "heads", "seq"),
        P(("groups", "wloop"), "seq"),
    )
    return jax.shard_map(
        shards,
        mesh=mesh,
        in_specs=placed,
        out_specs=P(("groups", "wloop"), "seq", "heads"),
        check_vma=False,
    )
```

```python
import math

import jax
import jax.numpy as jnp
from jax import lax
from jax.sharding import PartitionSpec as P

SCORE_SCALE = 2.0


def shifted(value, axis, steps):
    count = lax.axis_size(axis)
    initial, last = (max(0, -steps), min(count, count - steps))
    return lax.ppermute(value, axis, [(source, source + steps) for source in range(initial, last)])


def rms_rows(values, eps):
    return values * lax.rsqrt(jnp.mean(values * values, axis=-1, keepdims=True) + eps)


def window_mix(queries, lookup_vectors, values, prior_keys, prior_values, allow, scale):
    own = (
        jnp.einsum("bihd,bjhd->bhij", queries, lookup_vectors, preferred_element_type=jnp.float32)
        * scale
    )
    prior = (
        jnp.einsum("bihd,bjhd->bhij", queries, prior_keys, preferred_element_type=jnp.float32)
        * scale
    )
    span = queries.shape[1]
    row_pos = lax.broadcasted_iota(jnp.int32, (span, span), 0)
    column_pos = lax.broadcasted_iota(jnp.int32, (span, span), 1)
    own_w = jnp.where(column_pos <= row_pos, jnp.exp(own), 0.0)
    prior_w = jnp.where((column_pos > row_pos) & allow[:, None, None, None], jnp.exp(prior), 0.0)
    total = jnp.sum(own_w, axis=-1, keepdims=True) + jnp.sum(prior_w, axis=-1, keepdims=True)
    own_p = (own_w / total).astype(jnp.bfloat16)
    prior_p = (prior_w / total).astype(jnp.bfloat16)
    return jnp.einsum(
        "bhij,bjhd->bihd", own_p, values, preferred_element_type=jnp.float32
    ) + jnp.einsum("bhij,bjhd->bihd", prior_p, prior_values, preferred_element_type=jnp.float32)


def shards(activations, norm_gain, w_query, w_keyvalue, w_output, log_retain, resets):
    trajs, span, width = activations.shape
    heads_here = log_retain.shape[1]
    inner_here = w_query.shape[1]
    head_dim = inner_here // heads_here
    scale = SCORE_SCALE / math.sqrt(head_dim)
    count = trajs * span
    normed = (rms_rows(activations.astype(jnp.float32), 1e-05) * norm_gain).astype(jnp.bfloat16)
    normed = normed.reshape(count, width)
    ways = lax.axis_size("wloop")
    me = lax.axis_index("wloop")
    block = width // ways

    def feature_block(index):
        return lax.dynamic_slice_in_dim(normed, index * block, block, 1)

    cores = lax.axis_size("heads")
    core = lax.axis_index("heads")
    share_rows = count // cores

    def from_cores(part):
        pieces = [part]
        for step in range(1, cores):
            pieces.append(
                lax.ppermute(part, "heads", [(source, (source + step) % cores) for source in range(cores)])
            )
        order = (core - jnp.arange(cores)) % cores
        return jnp.take(jnp.stack(pieces), order, axis=0).reshape(count, block)

    stacked = [feature_block(me)]
    for step in range(1, ways):
        part = lax.dynamic_slice_in_dim(feature_block((me + step) % ways), core * share_rows, share_rows, 0)
        stacked.append(
            from_cores(
                lax.ppermute(
                    part,
                    "wloop",
                    [(source, (source + step) % ways) for source in range(ways)],
                )
            )
        )

    def gathered_sum(partials, after=None):
        total = partials[0]
        for step in range(1, ways):
            outgoing = partials[step].astype(jnp.bfloat16)
            if after is not None:
                outgoing = lax.optimization_barrier((outgoing, after))[0]
            total = total + lax.ppermute(
                outgoing,
                "wloop",
                [(source, (source - step) % ways) for source in range(ways)],
            ).astype(jnp.float32)
        return total

    kv_partials = [
        jnp.einsum("td,dje->jte", rows, w_keyvalue, preferred_element_type=jnp.float32)
        for rows in stacked
    ]
    pieces = 2
    rows_per = count // pieces
    raw_chunks, key_chunks, value_chunks, prior_chunks = [], [], [], []
    for piece in range(pieces):
        raw = gathered_sum([p[:, piece * rows_per : (piece + 1) * rows_per] for p in kv_partials])
        keys_here = rms_rows(raw[0].reshape(rows_per, heads_here, head_dim), 1e-06).astype(jnp.bfloat16)
        values_here = raw[1].reshape(rows_per, heads_here, head_dim).astype(jnp.bfloat16)
        prior_chunks.append(
            shifted(
                (keys_here.reshape(rows_per, inner_here), values_here.reshape(rows_per, inner_here)),
                "seq",
                1,
            )
        )
        raw_chunks.append(raw)
        key_chunks.append(keys_here)
        value_chunks.append(values_here)
    pair_raw = jnp.concatenate(raw_chunks, axis=1)
    query_raw = gathered_sum(
        [jnp.dot(rows, w_query, preferred_element_type=jnp.float32) for rows in stacked],
        after=pair_raw,
    )
    lookup_vectors = jnp.concatenate(key_chunks, axis=0).reshape(trajs, span, heads_here, head_dim)
    values = jnp.concatenate(value_chunks, axis=0).reshape(trajs, span, heads_here, head_dim)
    prior_keys = jnp.concatenate([p[0] for p in prior_chunks], axis=0).reshape(trajs, span, inner_here)
    prior_values = jnp.concatenate([p[1] for p in prior_chunks], axis=0).reshape(trajs, span, inner_here)
    queries = rms_rows(query_raw.reshape(trajs, span, heads_here, head_dim), 1e-06).astype(
        jnp.bfloat16
    )
    keep = (1 - resets[:, 0]).astype(jnp.float32)
    climb = jnp.cumsum(log_retain, axis=-1)
    whole = climb[:, :, -1]
    factor = jnp.exp(whole) * keep[:, None]
    weight = jnp.exp(whole[:, :, None] - climb)
    local_state = jnp.einsum(
        "bht,bthd,bthe->bhde",
        weight,
        lookup_vectors.astype(jnp.float32),
        values.astype(jnp.float32),
        precision=lax.Precision.HIGHEST,
    )
    local_mass = jnp.sum(weight * weight, axis=-1)

    def as_block(per_head):
        padded = jnp.pad(per_head, ((0, 0), (0, head_dim * head_dim - heads_here)))
        return padded.reshape(trajs, 1, head_dim, head_dim)

    local_both = jnp.concatenate([local_state, as_block(local_mass)], axis=1)
    factor_both = jnp.concatenate(
        [jnp.broadcast_to(factor[:, :, None, None], local_state.shape), as_block(factor * factor)],
        axis=1,
    )

    def relay_turn(turn, carry):
        return shifted((factor_both * carry + local_both).astype(jnp.bfloat16), "seq", 1).astype(
            jnp.float32
        )

    local_both, prior_keys, prior_values = lax.optimization_barrier((local_both, prior_keys, prior_values))
    entering_both = jnp.zeros_like(local_both)
    for turn in range(lax.axis_size("seq") - 1):
        entering_both = relay_turn(turn, entering_both)
    entering = entering_both[:, :heads_here]
    entering_mass = entering_both[:, heads_here].reshape(trajs, head_dim * head_dim)[:, :heads_here]
    entering = entering * keep[:, None, None, None]
    entering_mass = entering_mass * keep[:, None]
    read = jnp.einsum(
        "bthd,bhde->bthe", queries, entering.astype(jnp.bfloat16), preferred_element_type=jnp.float32
    )
    read = read * jnp.exp(climb).transpose(0, 2, 1)[..., None]
    read = read / jnp.sqrt(head_dim * (1.0 + entering_mass))[:, None, :, None]
    allow = (keep > 0.5) & (lax.axis_index("seq") > 0)
    window = window_mix(
        queries,
        lookup_vectors,
        values,
        prior_keys.reshape(trajs, span, heads_here, head_dim),
        prior_values.reshape(trajs, span, heads_here, head_dim),
        allow,
        scale,
    )
    attended = (window + read).astype(jnp.bfloat16).reshape(count, inner_here)
    w_output = lax.optimization_barrier((w_output, pair_raw))[0]
    w_output_rows = lax.all_gather(w_output, "wloop", axis=1, tiled=True)
    cores = lax.axis_size("heads")
    core = lax.axis_index("heads")
    share = width // cores

    def output_share(index):
        return jnp.dot(
            attended,
            lax.dynamic_slice_in_dim(w_output_rows, index * share, share, 1),
            preferred_element_type=jnp.float32,
        )

    received = [
        lax.ppermute(
            output_share((core + step) % cores).astype(jnp.bfloat16),
            "heads",
            [(source, (source + step) % cores) for source in range(cores)],
        )
        for step in range(1, cores)
    ]
    summed = output_share(core)
    for piece in received:
        summed = summed + piece.astype(jnp.float32)
    residual = lax.dynamic_slice_in_dim(
        activations.reshape(count, width), core * share, share, 1
    )
    return (residual.astype(jnp.float32) + summed).astype(jnp.bfloat16).reshape(trajs, span, share)


def solution(mesh):
    placed = (
        P(("groups", "wloop"), "seq", None),
        P(),
        P("wloop", "heads"),
        P("wloop", None, "heads"),
        P("heads", "wloop"),
        P(("groups", "wloop"), "heads", "seq"),
        P(("groups", "wloop"), "seq"),
    )
    return jax.shard_map(
        shards,
        mesh=mesh,
        in_specs=placed,
        out_specs=P(("groups", "wloop"), "seq", "heads"),
        check_vma=False,
    )
```

```python
import math

import jax
import jax.numpy as jnp
from jax import lax
from jax.sharding import PartitionSpec as P

SCORE_SCALE = 2.0


def shifted(value, axis, steps):
    count = lax.axis_size(axis)
    initial, last = (max(0, -steps), min(count, count - steps))
    return lax.ppermute(value, axis, [(source, source + steps) for source in range(initial, last)])


def rms_rows(values, eps):
    return values * lax.rsqrt(jnp.mean(values * values, axis=-1, keepdims=True) + eps)


def window_mix(queries, lookup_vectors, values, prior_keys, prior_values, allow, scale):
    own = (
        jnp.einsum("bihd,bjhd->bhij", queries, lookup_vectors, preferred_element_type=jnp.float32)
        * scale
    )
    prior = (
        jnp.einsum("bihd,bjhd->bhij", queries, prior_keys, preferred_element_type=jnp.float32)
        * scale
    )
    span = queries.shape[1]
    row_pos = lax.broadcasted_iota(jnp.int32, (span, span), 0)
    column_pos = lax.broadcasted_iota(jnp.int32, (span, span), 1)
    own_w = jnp.where(column_pos <= row_pos, jnp.exp(own), 0.0)
    prior_w = jnp.where((column_pos > row_pos) & allow[:, None, None, None], jnp.exp(prior), 0.0)
    total = jnp.sum(own_w, axis=-1, keepdims=True) + jnp.sum(prior_w, axis=-1, keepdims=True)
    own_p = (own_w / total).astype(jnp.bfloat16)
    prior_p = (prior_w / total).astype(jnp.bfloat16)
    return jnp.einsum(
        "bhij,bjhd->bihd", own_p, values, preferred_element_type=jnp.float32
    ) + jnp.einsum("bhij,bjhd->bihd", prior_p, prior_values, preferred_element_type=jnp.float32)


def shards(activations, norm_gain, w_query, w_keyvalue, w_output, log_retain, resets):
    trajs, span, width = activations.shape
    heads_here = log_retain.shape[1]
    inner_here = w_query.shape[1]
    head_dim = inner_here // heads_here
    scale = SCORE_SCALE / math.sqrt(head_dim)
    count = trajs * span
    normed = (rms_rows(activations.astype(jnp.float32), 1e-05) * norm_gain).astype(jnp.bfloat16)
    normed = normed.reshape(count, width)
    ways = lax.axis_size("wloop")
    me = lax.axis_index("wloop")
    block = width // ways

    def feature_block(index):
        return lax.dynamic_slice_in_dim(normed, index * block, block, 1)

    cores = lax.axis_size("heads")
    core = lax.axis_index("heads")
    share_rows = count // cores

    def from_cores(part):
        pieces = [part]
        for step in range(1, cores):
            pieces.append(
                lax.ppermute(part, "heads", [(source, (source + step) % cores) for source in range(cores)])
            )
        order = (core - jnp.arange(cores)) % cores
        return jnp.take(jnp.stack(pieces), order, axis=0).reshape(count, block)

    stacked = [feature_block(me)]
    for step in range(1, ways):
        part = lax.dynamic_slice_in_dim(feature_block((me + step) % ways), core * share_rows, share_rows, 0)
        stacked.append(
            from_cores(
                lax.ppermute(
                    part,
                    "wloop",
                    [(source, (source + step) % ways) for source in range(ways)],
                )
            )
        )

    def gathered_sum(partials, after=None):
        total = partials[0]
        for step in range(1, ways):
            outgoing = partials[step].astype(jnp.bfloat16)
            if after is not None:
                outgoing = lax.optimization_barrier((outgoing, after))[0]
            total = total + lax.ppermute(
                outgoing,
                "wloop",
                [(source, (source - step) % ways) for source in range(ways)],
            ).astype(jnp.float32)
        return total

    kv_partials = [
        jnp.einsum("td,dje->jte", rows, w_keyvalue, preferred_element_type=jnp.float32)
        for rows in stacked
    ]
    pieces = 2
    rows_per = count // pieces
    raw_chunks, key_chunks, value_chunks, prior_chunks = [], [], [], []
    for piece in range(pieces):
        raw = gathered_sum(
            [p[:, piece * rows_per : (piece + 1) * rows_per] for p in kv_partials],
            after=key_chunks[-1] if key_chunks else None,
        )
        keys_here = rms_rows(raw[0].reshape(rows_per, heads_here, head_dim), 1e-06).astype(jnp.bfloat16)
        values_here = raw[1].reshape(rows_per, heads_here, head_dim).astype(jnp.bfloat16)
        keys_here, values_here = lax.optimization_barrier((keys_here, values_here))
        prior_chunks.append(
            shifted(
                (keys_here.reshape(rows_per, inner_here), values_here.reshape(rows_per, inner_here)),
                "seq",
                1,
            )
        )
        raw_chunks.append(raw)
        key_chunks.append(keys_here)
        value_chunks.append(values_here)
    pair_raw = jnp.concatenate(raw_chunks, axis=1)
    query_raw = gathered_sum(
        [jnp.dot(rows, w_query, preferred_element_type=jnp.float32) for rows in stacked],
        after=pair_raw,
    )
    lookup_vectors = jnp.concatenate(key_chunks, axis=0).reshape(trajs, span, heads_here, head_dim)
    values = jnp.concatenate(value_chunks, axis=0).reshape(trajs, span, heads_here, head_dim)
    prior_keys = jnp.concatenate([p[0] for p in prior_chunks], axis=0).reshape(trajs, span, inner_here)
    prior_values = jnp.concatenate([p[1] for p in prior_chunks], axis=0).reshape(trajs, span, inner_here)
    queries = rms_rows(query_raw.reshape(trajs, span, heads_here, head_dim), 1e-06).astype(
        jnp.bfloat16
    )
    keep = (1 - resets[:, 0]).astype(jnp.float32)
    climb = jnp.cumsum(log_retain, axis=-1)
    whole = climb[:, :, -1]
    factor = jnp.exp(whole) * keep[:, None]
    weight = jnp.exp(whole[:, :, None] - climb)
    local_state = jnp.einsum(
        "bht,bthd,bthe->bhde",
        weight,
        lookup_vectors.astype(jnp.float32),
        values.astype(jnp.float32),
        precision=lax.Precision.HIGHEST,
    )
    local_mass = jnp.sum(weight * weight, axis=-1)

    def as_block(per_head):
        padded = jnp.pad(per_head, ((0, 0), (0, head_dim * head_dim - heads_here)))
        return padded.reshape(trajs, 1, head_dim, head_dim)

    local_both = jnp.concatenate([local_state, as_block(local_mass)], axis=1)
    factor_both = jnp.concatenate(
        [jnp.broadcast_to(factor[:, :, None, None], local_state.shape), as_block(factor * factor)],
        axis=1,
    )

    def relay_turn(turn, carry):
        return shifted((factor_both * carry + local_both).astype(jnp.bfloat16), "seq", 1).astype(
            jnp.float32
        )

    local_both, prior_keys, prior_values = lax.optimization_barrier((local_both, prior_keys, prior_values))
    entering_both = jnp.zeros_like(local_both)
    for turn in range(lax.axis_size("seq") - 1):
        entering_both = relay_turn(turn, entering_both)
    entering = entering_both[:, :heads_here]
    entering_mass = entering_both[:, heads_here].reshape(trajs, head_dim * head_dim)[:, :heads_here]
    entering = entering * keep[:, None, None, None]
    entering_mass = entering_mass * keep[:, None]
    read = jnp.einsum(
        "bthd,bhde->bthe", queries, entering.astype(jnp.bfloat16), preferred_element_type=jnp.float32
    )
    read = read * jnp.exp(climb).transpose(0, 2, 1)[..., None]
    read = read / jnp.sqrt(head_dim * (1.0 + entering_mass))[:, None, :, None]
    allow = (keep > 0.5) & (lax.axis_index("seq") > 0)
    window = window_mix(
        queries,
        lookup_vectors,
        values,
        prior_keys.reshape(trajs, span, heads_here, head_dim),
        prior_values.reshape(trajs, span, heads_here, head_dim),
        allow,
        scale,
    )
    attended = (window + read).astype(jnp.bfloat16).reshape(count, inner_here)
    w_output = lax.optimization_barrier((w_output, pair_raw))[0]
    w_output_rows = lax.all_gather(w_output, "wloop", axis=1, tiled=True)
    cores = lax.axis_size("heads")
    core = lax.axis_index("heads")
    share = width // cores

    def output_share(index):
        return jnp.dot(
            attended,
            lax.dynamic_slice_in_dim(w_output_rows, index * share, share, 1),
            preferred_element_type=jnp.float32,
        )

    received = [
        lax.ppermute(
            output_share((core + step) % cores).astype(jnp.bfloat16),
            "heads",
            [(source, (source + step) % cores) for source in range(cores)],
        )
        for step in range(1, cores)
    ]
    summed = output_share(core)
    for piece in received:
        summed = summed + piece.astype(jnp.float32)
    residual = lax.dynamic_slice_in_dim(
        activations.reshape(count, width), core * share, share, 1
    )
    return (residual.astype(jnp.float32) + summed).astype(jnp.bfloat16).reshape(trajs, span, share)


def solution(mesh):
    placed = (
        P(("groups", "wloop"), "seq", None),
        P(),
        P("wloop", "heads"),
        P("wloop", None, "heads"),
        P("heads", "wloop"),
        P(("groups", "wloop"), "heads", "seq"),
        P(("groups", "wloop"), "seq"),
    )
    return jax.shard_map(
        shards,
        mesh=mesh,
        in_specs=placed,
        out_specs=P(("groups", "wloop"), "seq", "heads"),
        check_vma=False,
    )
```

```python
import math

import jax
import jax.numpy as jnp
from jax import lax
from jax.sharding import PartitionSpec as P

SCORE_SCALE = 2.0


def shifted(value, axis, steps):
    count = lax.axis_size(axis)
    initial, last = (max(0, -steps), min(count, count - steps))
    return lax.ppermute(value, axis, [(source, source + steps) for source in range(initial, last)])


def rms_rows(values, eps):
    return values * lax.rsqrt(jnp.mean(values * values, axis=-1, keepdims=True) + eps)


def window_mix(queries, lookup_vectors, values, prior_keys, prior_values, allow, scale):
    own = (
        jnp.einsum("bihd,bjhd->bhij", queries, lookup_vectors, preferred_element_type=jnp.float32)
        * scale
    )
    prior = (
        jnp.einsum("bihd,bjhd->bhij", queries, prior_keys, preferred_element_type=jnp.float32)
        * scale
    )
    span = queries.shape[1]
    row_pos = lax.broadcasted_iota(jnp.int32, (span, span), 0)
    column_pos = lax.broadcasted_iota(jnp.int32, (span, span), 1)
    own_w = jnp.where(column_pos <= row_pos, jnp.exp(own), 0.0)
    prior_w = jnp.where((column_pos > row_pos) & allow[:, None, None, None], jnp.exp(prior), 0.0)
    total = jnp.sum(own_w, axis=-1, keepdims=True) + jnp.sum(prior_w, axis=-1, keepdims=True)
    own_p = (own_w / total).astype(jnp.bfloat16)
    prior_p = (prior_w / total).astype(jnp.bfloat16)
    return jnp.einsum(
        "bhij,bjhd->bihd", own_p, values, preferred_element_type=jnp.float32
    ) + jnp.einsum("bhij,bjhd->bihd", prior_p, prior_values, preferred_element_type=jnp.float32)


def shards(activations, norm_gain, w_query, w_keyvalue, w_output, log_retain, resets):
    trajs, span, width = activations.shape
    heads_here = log_retain.shape[1]
    inner_here = w_query.shape[1]
    head_dim = inner_here // heads_here
    scale = SCORE_SCALE / math.sqrt(head_dim)
    count = trajs * span
    normed = (rms_rows(activations.astype(jnp.float32), 1e-05) * norm_gain).astype(jnp.bfloat16)
    normed = normed.reshape(count, width)
    ways = lax.axis_size("wloop")
    me = lax.axis_index("wloop")
    block = width // ways

    def feature_block(index):
        return lax.dynamic_slice_in_dim(normed, index * block, block, 1)

    cores = lax.axis_size("heads")
    core = lax.axis_index("heads")
    share_rows = count // cores

    def from_cores(part):
        pieces = [part]
        for step in range(1, cores):
            pieces.append(
                lax.ppermute(part, "heads", [(source, (source + step) % cores) for source in range(cores)])
            )
        order = (core - jnp.arange(cores)) % cores
        return jnp.take(jnp.stack(pieces), order, axis=0).reshape(count, block)

    stacked = [feature_block(me)]
    for step in range(1, ways):
        part = lax.dynamic_slice_in_dim(feature_block((me + step) % ways), core * share_rows, share_rows, 0)
        stacked.append(
            from_cores(
                lax.ppermute(
                    part,
                    "wloop",
                    [(source, (source + step) % ways) for source in range(ways)],
                )
            )
        )

    def gathered_sum(partials, after=None):
        total = partials[0]
        for step in range(1, ways):
            outgoing = partials[step].astype(jnp.bfloat16)
            if after is not None:
                outgoing = lax.optimization_barrier((outgoing, after))[0]
            total = total + lax.ppermute(
                outgoing,
                "wloop",
                [(source, (source - step) % ways) for source in range(ways)],
            ).astype(jnp.float32)
        return total

    pieces = 2
    rows_per = count // pieces
    raw_chunks, key_chunks, value_chunks, prior_chunks = [], [], [], []
    for piece in range(pieces):
        raw = gathered_sum(
            [
                jnp.einsum(
                    "td,dje->jte",
                    rows[piece * rows_per : (piece + 1) * rows_per],
                    w_keyvalue,
                    preferred_element_type=jnp.float32,
                )
                for rows in stacked
            ],
            after=key_chunks[-1] if key_chunks else None,
        )
        keys_here = rms_rows(raw[0].reshape(rows_per, heads_here, head_dim), 1e-06).astype(jnp.bfloat16)
        values_here = raw[1].reshape(rows_per, heads_here, head_dim).astype(jnp.bfloat16)
        keys_here, values_here = lax.optimization_barrier((keys_here, values_here))
        prior_chunks.append(
            shifted(
                (keys_here.reshape(rows_per, inner_here), values_here.reshape(rows_per, inner_here)),
                "seq",
                1,
            )
        )
        raw_chunks.append(raw)
        key_chunks.append(keys_here)
        value_chunks.append(values_here)
    pair_raw = jnp.concatenate(raw_chunks, axis=1)
    query_raw = gathered_sum(
        [jnp.dot(rows, w_query, preferred_element_type=jnp.float32) for rows in stacked],
        after=key_chunks[-1],
    )
    lookup_vectors = jnp.concatenate(key_chunks, axis=0).reshape(trajs, span, heads_here, head_dim)
    values = jnp.concatenate(value_chunks, axis=0).reshape(trajs, span, heads_here, head_dim)
    prior_keys = jnp.concatenate([p[0] for p in prior_chunks], axis=0).reshape(trajs, span, inner_here)
    prior_values = jnp.concatenate([p[1] for p in prior_chunks], axis=0).reshape(trajs, span, inner_here)
    queries = rms_rows(query_raw.reshape(trajs, span, heads_here, head_dim), 1e-06).astype(
        jnp.bfloat16
    )
    keep = (1 - resets[:, 0]).astype(jnp.float32)
    climb = jnp.cumsum(log_retain, axis=-1)
    whole = climb[:, :, -1]
    factor = jnp.exp(whole) * keep[:, None]
    weight = jnp.exp(whole[:, :, None] - climb)
    local_state = jnp.einsum(
        "bht,bthd,bthe->bhde",
        weight,
        lookup_vectors.astype(jnp.float32),
        values.astype(jnp.float32),
        precision=lax.Precision.HIGHEST,
    )
    local_mass = jnp.sum(weight * weight, axis=-1)

    def as_block(per_head):
        padded = jnp.pad(per_head, ((0, 0), (0, head_dim * head_dim - heads_here)))
        return padded.reshape(trajs, 1, head_dim, head_dim)

    local_both = jnp.concatenate([local_state, as_block(local_mass)], axis=1)
    factor_both = jnp.concatenate(
        [jnp.broadcast_to(factor[:, :, None, None], local_state.shape), as_block(factor * factor)],
        axis=1,
    )

    def relay_turn(turn, carry):
        return shifted((factor_both * carry + local_both).astype(jnp.bfloat16), "seq", 1).astype(
            jnp.float32
        )

    local_both, prior_keys, prior_values = lax.optimization_barrier((local_both, prior_keys, prior_values))
    entering_both = jnp.zeros_like(local_both)
    for turn in range(lax.axis_size("seq") - 1):
        entering_both = relay_turn(turn, entering_both)
    entering = entering_both[:, :heads_here]
    entering_mass = entering_both[:, heads_here].reshape(trajs, head_dim * head_dim)[:, :heads_here]
    entering = entering * keep[:, None, None, None]
    entering_mass = entering_mass * keep[:, None]
    read = jnp.einsum(
        "bthd,bhde->bthe", queries, entering.astype(jnp.bfloat16), preferred_element_type=jnp.float32
    )
    read = read * jnp.exp(climb).transpose(0, 2, 1)[..., None]
    read = read / jnp.sqrt(head_dim * (1.0 + entering_mass))[:, None, :, None]
    allow = (keep > 0.5) & (lax.axis_index("seq") > 0)
    window = window_mix(
        queries,
        lookup_vectors,
        values,
        prior_keys.reshape(trajs, span, heads_here, head_dim),
        prior_values.reshape(trajs, span, heads_here, head_dim),
        allow,
        scale,
    )
    attended = (window + read).astype(jnp.bfloat16).reshape(count, inner_here)
    w_output = lax.optimization_barrier((w_output, key_chunks[-1]))[0]
    out_cols = w_output.shape[1]
    from_ranks = [w_output] + [
        lax.ppermute(w_output, "wloop", [(source, (source + step) % ways) for source in range(ways)])
        for step in range(1, ways)
    ]
    rank_order = (me - jnp.arange(ways)) % ways
    w_output_rows = (
        jnp.take(jnp.stack(from_ranks), rank_order, axis=0).transpose(1, 0, 2).reshape(w_output.shape[0], ways * out_cols)
    )
    cores = lax.axis_size("heads")
    core = lax.axis_index("heads")
    share = width // cores

    def output_share(index):
        return jnp.dot(
            attended,
            lax.dynamic_slice_in_dim(w_output_rows, index * share, share, 1),
            preferred_element_type=jnp.float32,
        )

    received = [
        lax.ppermute(
            output_share((core + step) % cores).astype(jnp.bfloat16),
            "heads",
            [(source, (source + step) % cores) for source in range(cores)],
        )
        for step in range(1, cores)
    ]
    summed = output_share(core)
    for piece in received:
        summed = summed + piece.astype(jnp.float32)
    residual = lax.dynamic_slice_in_dim(
        activations.reshape(count, width), core * share, share, 1
    )
    return (residual.astype(jnp.float32) + summed).astype(jnp.bfloat16).reshape(trajs, span, share)


def solution(mesh):
    placed = (
        P(("groups", "wloop"), "seq", None),
        P(),
        P("wloop", "heads"),
        P("wloop", None, "heads"),
        P("heads", "wloop"),
        P(("groups", "wloop"), "heads", "seq"),
        P(("groups", "wloop"), "seq"),
    )
    return jax.shard_map(
        shards,
        mesh=mesh,
        in_specs=placed,
        out_specs=P(("groups", "wloop"), "seq", "heads"),
        check_vma=False,
    )
```

```python
import math

import jax
import jax.numpy as jnp
from jax import lax
from jax.sharding import PartitionSpec as P

SCORE_SCALE = 2.0


def shifted(value, axis, steps):
    count = lax.axis_size(axis)
    initial, last = (max(0, -steps), min(count, count - steps))
    return lax.ppermute(value, axis, [(source, source + steps) for source in range(initial, last)])


def rms_rows(values, eps):
    return values * lax.rsqrt(jnp.mean(values * values, axis=-1, keepdims=True) + eps)


def window_mix(queries, lookup_vectors, values, prior_keys, prior_values, allow, scale):
    own = (
        jnp.einsum("bihd,bjhd->bhij", queries, lookup_vectors, preferred_element_type=jnp.float32)
        * scale
    )
    prior = (
        jnp.einsum("bihd,bjhd->bhij", queries, prior_keys, preferred_element_type=jnp.float32)
        * scale
    )
    span = queries.shape[1]
    row_pos = lax.broadcasted_iota(jnp.int32, (span, span), 0)
    column_pos = lax.broadcasted_iota(jnp.int32, (span, span), 1)
    own_w = jnp.where(column_pos <= row_pos, jnp.exp(own), 0.0)
    prior_w = jnp.where((column_pos > row_pos) & allow[:, None, None, None], jnp.exp(prior), 0.0)
    total = jnp.sum(own_w, axis=-1, keepdims=True) + jnp.sum(prior_w, axis=-1, keepdims=True)
    own_p = (own_w / total).astype(jnp.bfloat16)
    prior_p = (prior_w / total).astype(jnp.bfloat16)
    return jnp.einsum(
        "bhij,bjhd->bihd", own_p, values, preferred_element_type=jnp.float32
    ) + jnp.einsum("bhij,bjhd->bihd", prior_p, prior_values, preferred_element_type=jnp.float32)


def shards(activations, norm_gain, w_query, w_keyvalue, w_output, log_retain, resets):
    trajs, span, width = activations.shape
    heads_here = log_retain.shape[1]
    inner_here = w_query.shape[1]
    head_dim = inner_here // heads_here
    scale = SCORE_SCALE / math.sqrt(head_dim)
    count = trajs * span
    normed = (rms_rows(activations.astype(jnp.float32), 1e-05) * norm_gain).astype(jnp.bfloat16)
    normed = normed.reshape(count, width)
    ways = lax.axis_size("wloop")
    me = lax.axis_index("wloop")
    block = width // ways

    def feature_block(index):
        return lax.dynamic_slice_in_dim(normed, index * block, block, 1)

    cores = lax.axis_size("heads")
    core = lax.axis_index("heads")
    share_rows = count // cores

    def from_cores(part):
        pieces = [part]
        for step in range(1, cores):
            pieces.append(
                lax.ppermute(part, "heads", [(source, (source + step) % cores) for source in range(cores)])
            )
        order = (core - jnp.arange(cores)) % cores
        return jnp.take(jnp.stack(pieces), order, axis=0).reshape(count, block)

    stacked = [feature_block(me)]
    for step in range(1, ways):
        part = lax.dynamic_slice_in_dim(feature_block((me + step) % ways), core * share_rows, share_rows, 0)
        stacked.append(
            from_cores(
                lax.ppermute(
                    part,
                    "wloop",
                    [(source, (source + step) % ways) for source in range(ways)],
                )
            )
        )

    def gathered_sum(partials, after=None):
        total = partials[0]
        for step in range(1, ways):
            outgoing = partials[step].astype(jnp.bfloat16)
            if after is not None:
                outgoing = lax.optimization_barrier((outgoing, after))[0]
            total = total + lax.ppermute(
                outgoing,
                "wloop",
                [(source, (source - step) % ways) for source in range(ways)],
            ).astype(jnp.float32)
        return total

    kv_partials = [
        jnp.einsum("td,dje->jte", rows, w_keyvalue, preferred_element_type=jnp.float32)
        for rows in stacked
    ]
    pieces = 2
    rows_per = count // pieces
    raw_chunks, key_chunks, value_chunks, prior_chunks = [], [], [], []
    for piece in range(pieces):
        raw = gathered_sum(
            [p[:, piece * rows_per : (piece + 1) * rows_per] for p in kv_partials],
            after=key_chunks[-1] if key_chunks else None,
        )
        if prior_chunks:
            raw = lax.optimization_barrier((raw, prior_chunks[-1]))[0]
        keys_here = rms_rows(raw[0].reshape(rows_per, heads_here, head_dim), 1e-06).astype(jnp.bfloat16)
        values_here = raw[1].reshape(rows_per, heads_here, head_dim).astype(jnp.bfloat16)
        keys_here, values_here = lax.optimization_barrier((keys_here, values_here))
        prior_chunks.append(
            shifted(
                (keys_here.reshape(rows_per, inner_here), values_here.reshape(rows_per, inner_here)),
                "seq",
                1,
            )
        )
        raw_chunks.append(raw)
        key_chunks.append(keys_here)
        value_chunks.append(values_here)
    pair_raw = jnp.concatenate(raw_chunks, axis=1)
    query_raw = gathered_sum(
        [jnp.dot(rows, w_query, preferred_element_type=jnp.float32) for rows in stacked],
        after=pair_raw,
    )
    lookup_vectors = jnp.concatenate(key_chunks, axis=0).reshape(trajs, span, heads_here, head_dim)
    values = jnp.concatenate(value_chunks, axis=0).reshape(trajs, span, heads_here, head_dim)
    prior_keys = jnp.concatenate([p[0] for p in prior_chunks], axis=0).reshape(trajs, span, inner_here)
    prior_values = jnp.concatenate([p[1] for p in prior_chunks], axis=0).reshape(trajs, span, inner_here)
    queries = rms_rows(query_raw.reshape(trajs, span, heads_here, head_dim), 1e-06).astype(
        jnp.bfloat16
    )
    keep = (1 - resets[:, 0]).astype(jnp.float32)
    climb = jnp.cumsum(log_retain, axis=-1)
    whole = climb[:, :, -1]
    factor = jnp.exp(whole) * keep[:, None]
    weight = jnp.exp(whole[:, :, None] - climb)
    local_state = jnp.einsum(
        "bht,bthd,bthe->bhde",
        weight,
        lookup_vectors.astype(jnp.float32),
        values.astype(jnp.float32),
        precision=lax.Precision.HIGHEST,
    )
    local_mass = jnp.sum(weight * weight, axis=-1)

    def as_block(per_head):
        padded = jnp.pad(per_head, ((0, 0), (0, head_dim * head_dim - heads_here)))
        return padded.reshape(trajs, 1, head_dim, head_dim)

    local_both = jnp.concatenate([local_state, as_block(local_mass)], axis=1)
    factor_both = jnp.concatenate(
        [jnp.broadcast_to(factor[:, :, None, None], local_state.shape), as_block(factor * factor)],
        axis=1,
    )

    def relay_turn(turn, carry):
        return shifted((factor_both * carry + local_both).astype(jnp.bfloat16), "seq", 1).astype(
            jnp.float32
        )

    local_both, prior_keys, prior_values = lax.optimization_barrier((local_both, prior_keys, prior_values))
    entering_both = jnp.zeros_like(local_both)
    for turn in range(lax.axis_size("seq") - 1):
        entering_both = relay_turn(turn, entering_both)
    entering = entering_both[:, :heads_here]
    entering_mass = entering_both[:, heads_here].reshape(trajs, head_dim * head_dim)[:, :heads_here]
    entering = entering * keep[:, None, None, None]
    entering_mass = entering_mass * keep[:, None]
    read = jnp.einsum(
        "bthd,bhde->bthe", queries, entering.astype(jnp.bfloat16), preferred_element_type=jnp.float32
    )
    read = read * jnp.exp(climb).transpose(0, 2, 1)[..., None]
    read = read / jnp.sqrt(head_dim * (1.0 + entering_mass))[:, None, :, None]
    allow = (keep > 0.5) & (lax.axis_index("seq") > 0)
    window = window_mix(
        queries,
        lookup_vectors,
        values,
        prior_keys.reshape(trajs, span, heads_here, head_dim),
        prior_values.reshape(trajs, span, heads_here, head_dim),
        allow,
        scale,
    )
    attended = (window + read).astype(jnp.bfloat16).reshape(count, inner_here)
    w_output = lax.optimization_barrier((w_output, pair_raw))[0]
    w_output_rows = lax.all_gather(w_output, "wloop", axis=1, tiled=True)
    cores = lax.axis_size("heads")
    core = lax.axis_index("heads")
    share = width // cores

    def output_share(index):
        return jnp.dot(
            attended,
            lax.dynamic_slice_in_dim(w_output_rows, index * share, share, 1),
            preferred_element_type=jnp.float32,
        )

    received = [
        lax.ppermute(
            output_share((core + step) % cores).astype(jnp.bfloat16),
            "heads",
            [(source, (source + step) % cores) for source in range(cores)],
        )
        for step in range(1, cores)
    ]
    summed = output_share(core)
    for piece in received:
        summed = summed + piece.astype(jnp.float32)
    residual = lax.dynamic_slice_in_dim(
        activations.reshape(count, width), core * share, share, 1
    )
    return (residual.astype(jnp.float32) + summed).astype(jnp.bfloat16).reshape(trajs, span, share)


def solution(mesh):
    placed = (
        P(("groups", "wloop"), "seq", None),
        P(),
        P("wloop", "heads"),
        P("wloop", None, "heads"),
        P("heads", "wloop"),
        P(("groups", "wloop"), "heads", "seq"),
        P(("groups", "wloop"), "seq"),
    )
    return jax.shard_map(
        shards,
        mesh=mesh,
        in_specs=placed,
        out_specs=P(("groups", "wloop"), "seq", "heads"),
        check_vma=False,
    )
```

```python
import math

import jax
import jax.numpy as jnp
from jax import lax
from jax.sharding import PartitionSpec as P

SCORE_SCALE = 2.0


def shifted(value, axis, steps):
    count = lax.axis_size(axis)
    initial, last = (max(0, -steps), min(count, count - steps))
    return lax.ppermute(value, axis, [(source, source + steps) for source in range(initial, last)])


def rms_rows(values, eps):
    return values * lax.rsqrt(jnp.mean(values * values, axis=-1, keepdims=True) + eps)


def window_mix(queries, lookup_vectors, values, prior_keys, prior_values, allow, scale):
    own = (
        jnp.einsum("bihd,bjhd->bhij", queries, lookup_vectors, preferred_element_type=jnp.float32)
        * scale
    )
    prior = (
        jnp.einsum("bihd,bjhd->bhij", queries, prior_keys, preferred_element_type=jnp.float32)
        * scale
    )
    span = queries.shape[1]
    row_pos = lax.broadcasted_iota(jnp.int32, (span, span), 0)
    column_pos = lax.broadcasted_iota(jnp.int32, (span, span), 1)
    own_w = jnp.where(column_pos <= row_pos, jnp.exp(own), 0.0)
    prior_w = jnp.where((column_pos > row_pos) & allow[:, None, None, None], jnp.exp(prior), 0.0)
    total = jnp.sum(own_w, axis=-1, keepdims=True) + jnp.sum(prior_w, axis=-1, keepdims=True)
    own_p = (own_w / total).astype(jnp.bfloat16)
    prior_p = (prior_w / total).astype(jnp.bfloat16)
    return jnp.einsum(
        "bhij,bjhd->bihd", own_p, values, preferred_element_type=jnp.float32
    ) + jnp.einsum("bhij,bjhd->bihd", prior_p, prior_values, preferred_element_type=jnp.float32)


def shards(activations, norm_gain, w_query, w_keyvalue, w_output, log_retain, resets):
    trajs, span, width = activations.shape
    heads_here = log_retain.shape[1]
    inner_here = w_query.shape[1]
    head_dim = inner_here // heads_here
    scale = SCORE_SCALE / math.sqrt(head_dim)
    count = trajs * span
    normed = (rms_rows(activations.astype(jnp.float32), 1e-05) * norm_gain).astype(jnp.bfloat16)
    normed = normed.reshape(count, width)
    ways = lax.axis_size("wloop")
    me = lax.axis_index("wloop")
    block = width // ways

    def feature_block(index):
        return lax.dynamic_slice_in_dim(normed, index * block, block, 1)

    cores = lax.axis_size("heads")
    core = lax.axis_index("heads")
    share_rows = count // cores

    def from_cores(part):
        pieces = [part]
        for step in range(1, cores):
            pieces.append(
                lax.ppermute(part, "heads", [(source, (source + step) % cores) for source in range(cores)])
            )
        order = (core - jnp.arange(cores)) % cores
        return jnp.take(jnp.stack(pieces), order, axis=0).reshape(count, block)

    stacked = [feature_block(me)]
    for step in range(1, ways):
        part = lax.dynamic_slice_in_dim(feature_block((me + step) % ways), core * share_rows, share_rows, 0)
        stacked.append(
            from_cores(
                lax.ppermute(
                    part,
                    "wloop",
                    [(source, (source + step) % ways) for source in range(ways)],
                )
            )
        )

    def gathered_sum(partials, after=None):
        total = partials[0]
        for step in range(1, ways):
            outgoing = partials[step].astype(jnp.bfloat16)
            if after is not None:
                outgoing = lax.optimization_barrier((outgoing, after))[0]
            total = total + lax.ppermute(
                outgoing,
                "wloop",
                [(source, (source - step) % ways) for source in range(ways)],
            ).astype(jnp.float32)
        return total

    pair_raw = gathered_sum(
        [
            jnp.einsum("td,dje->jte", rows, w_keyvalue, preferred_element_type=jnp.float32)
            for rows in stacked
        ]
    )
    query_raw = gathered_sum(
        [jnp.dot(rows, w_query, preferred_element_type=jnp.float32) for rows in stacked],
        after=pair_raw,
    )
    lookup_vectors = rms_rows(pair_raw[0].reshape(trajs, span, heads_here, head_dim), 1e-06).astype(
        jnp.bfloat16
    )
    values = pair_raw[1].reshape(trajs, span, heads_here, head_dim).astype(jnp.bfloat16)
    prior_keys, prior_values = shifted(
        (lookup_vectors.reshape(trajs, span, inner_here), values.reshape(trajs, span, inner_here)),
        "seq",
        1,
    )
    queries = rms_rows(query_raw.reshape(trajs, span, heads_here, head_dim), 1e-06).astype(
        jnp.bfloat16
    )
    keep = (1 - resets[:, 0]).astype(jnp.float32)
    climb = jnp.cumsum(log_retain, axis=-1)
    whole = climb[:, :, -1]
    factor = jnp.exp(whole) * keep[:, None]
    weight = jnp.exp(whole[:, :, None] - climb)
    local_state = jnp.einsum(
        "bht,bthd,bthe->bhde",
        weight,
        lookup_vectors.astype(jnp.float32),
        values.astype(jnp.float32),
        precision=lax.Precision.HIGHEST,
    )
    local_mass = jnp.sum(weight * weight, axis=-1)

    def as_block(per_head):
        padded = jnp.pad(per_head, ((0, 0), (0, head_dim * head_dim - heads_here)))
        return padded.reshape(trajs, 1, head_dim, head_dim)

    local_both = jnp.concatenate([local_state, as_block(local_mass)], axis=1)
    factor_both = jnp.concatenate(
        [jnp.broadcast_to(factor[:, :, None, None], local_state.shape), as_block(factor * factor)],
        axis=1,
    )

    def relay_turn(turn, carry):
        return shifted((factor_both * carry + local_both).astype(jnp.bfloat16), "seq", 1).astype(
            jnp.float32
        )

    local_both, prior_keys, prior_values = lax.optimization_barrier((local_both, prior_keys, prior_values))
    entering_both = jnp.zeros_like(local_both)
    for turn in range(lax.axis_size("seq") - 1):
        entering_both = relay_turn(turn, entering_both)
    entering = entering_both[:, :heads_here]
    entering_mass = entering_both[:, heads_here].reshape(trajs, head_dim * head_dim)[:, :heads_here]
    entering = entering * keep[:, None, None, None]
    entering_mass = entering_mass * keep[:, None]
    read = jnp.einsum(
        "bthd,bhde->bthe", queries, entering.astype(jnp.bfloat16), preferred_element_type=jnp.float32
    )
    read = read * jnp.exp(climb).transpose(0, 2, 1)[..., None]
    read = read / jnp.sqrt(head_dim * (1.0 + entering_mass))[:, None, :, None]
    allow = (keep > 0.5) & (lax.axis_index("seq") > 0)
    window = window_mix(
        queries,
        lookup_vectors,
        values,
        prior_keys.reshape(trajs, span, heads_here, head_dim),
        prior_values.reshape(trajs, span, heads_here, head_dim),
        allow,
        scale,
    )
    attended = (window + read).astype(jnp.bfloat16).reshape(count, inner_here)
    w_output = lax.optimization_barrier((w_output, pair_raw))[0]
    out_block = w_output.shape[1]
    from_ranks = jnp.stack(
        [w_output]
        + [
            lax.ppermute(w_output, "wloop", [(source, (source + step) % ways) for source in range(ways)])
            for step in range(1, ways)
        ]
    )
    cores = lax.axis_size("heads")
    core = lax.axis_index("heads")
    share = width // cores

    blocks_per_share = share // out_block

    def output_share(index):
        parts = []
        for part in range(blocks_per_share):
            rank = index * blocks_per_share + part
            parts.append(
                jnp.dot(
                    attended,
                    lax.dynamic_index_in_dim(from_ranks, (me - rank) % ways, 0, keepdims=False),
                    preferred_element_type=jnp.float32,
                )
            )
        return jnp.concatenate(parts, axis=1) if blocks_per_share > 1 else parts[0]

    received = [
        lax.ppermute(
            output_share((core + step) % cores).astype(jnp.bfloat16),
            "heads",
            [(source, (source + step) % cores) for source in range(cores)],
        )
        for step in range(1, cores)
    ]
    summed = output_share(core)
    for piece in received:
        summed = summed + piece.astype(jnp.float32)
    residual = lax.dynamic_slice_in_dim(
        activations.reshape(count, width), core * share, share, 1
    )
    return (residual.astype(jnp.float32) + summed).astype(jnp.bfloat16).reshape(trajs, span, share)


def solution(mesh):
    placed = (
        P(("groups", "wloop"), "seq", None),
        P(),
        P("wloop", "heads"),
        P("wloop", None, "heads"),
        P("heads", "wloop"),
        P(("groups", "wloop"), "heads", "seq"),
        P(("groups", "wloop"), "seq"),
    )
    return jax.shard_map(
        shards,
        mesh=mesh,
        in_specs=placed,
        out_specs=P(("groups", "wloop"), "seq", "heads"),
        check_vma=False,
    )
```

```python
import math

import jax
import jax.numpy as jnp
from jax import lax
from jax.sharding import PartitionSpec as P

SCORE_SCALE = 2.0


def shifted(value, axis, steps):
    count = lax.axis_size(axis)
    initial, last = (max(0, -steps), min(count, count - steps))
    return lax.ppermute(value, axis, [(source, source + steps) for source in range(initial, last)])


def rms_rows(values, eps):
    return values * lax.rsqrt(jnp.mean(values * values, axis=-1, keepdims=True) + eps)


def window_mix(queries, lookup_vectors, values, prior_keys, prior_values, allow, scale):
    own = (
        jnp.einsum("bihd,bjhd->bhij", queries, lookup_vectors, preferred_element_type=jnp.float32)
        * scale
    )
    prior = (
        jnp.einsum("bihd,bjhd->bhij", queries, prior_keys, preferred_element_type=jnp.float32)
        * scale
    )
    span = queries.shape[1]
    row_pos = lax.broadcasted_iota(jnp.int32, (span, span), 0)
    column_pos = lax.broadcasted_iota(jnp.int32, (span, span), 1)
    own_w = jnp.where(column_pos <= row_pos, jnp.exp(own), 0.0)
    prior_w = jnp.where((column_pos > row_pos) & allow[:, None, None, None], jnp.exp(prior), 0.0)
    total = jnp.sum(own_w, axis=-1, keepdims=True) + jnp.sum(prior_w, axis=-1, keepdims=True)
    own_p = (own_w / total).astype(jnp.bfloat16)
    prior_p = (prior_w / total).astype(jnp.bfloat16)
    return jnp.einsum(
        "bhij,bjhd->bihd", own_p, values, preferred_element_type=jnp.float32
    ) + jnp.einsum("bhij,bjhd->bihd", prior_p, prior_values, preferred_element_type=jnp.float32)


def shards(activations, norm_gain, w_query, w_keyvalue, w_output, log_retain, resets):
    trajs, span, width = activations.shape
    heads_here = log_retain.shape[1]
    inner_here = w_query.shape[1]
    head_dim = inner_here // heads_here
    scale = SCORE_SCALE / math.sqrt(head_dim)
    count = trajs * span
    normed = (rms_rows(activations.astype(jnp.float32), 1e-05) * norm_gain).astype(jnp.bfloat16)
    normed = normed.reshape(count, width)
    ways = lax.axis_size("wloop")
    me = lax.axis_index("wloop")
    block = width // ways

    def feature_block(index):
        return lax.dynamic_slice_in_dim(normed, index * block, block, 1)

    cores = lax.axis_size("heads")
    core = lax.axis_index("heads")
    share_rows = count // cores

    def from_cores(part):
        pieces = [part]
        for step in range(1, cores):
            pieces.append(
                lax.ppermute(part, "heads", [(source, (source + step) % cores) for source in range(cores)])
            )
        order = (core - jnp.arange(cores)) % cores
        return jnp.take(jnp.stack(pieces), order, axis=0).reshape(count, block)

    stacked = [feature_block(me)]
    for step in range(1, ways):
        part = lax.dynamic_slice_in_dim(feature_block((me + step) % ways), core * share_rows, share_rows, 0)
        stacked.append(
            from_cores(
                lax.ppermute(
                    part,
                    "wloop",
                    [(source, (source + step) % ways) for source in range(ways)],
                )
            )
        )

    def gathered_sum(partials, after=None):
        total = partials[0]
        for step in range(1, ways):
            outgoing = partials[step].astype(jnp.bfloat16)
            if after is not None:
                outgoing = lax.optimization_barrier((outgoing, after))[0]
            total = total + lax.ppermute(
                outgoing,
                "wloop",
                [(source, (source - step) % ways) for source in range(ways)],
            ).astype(jnp.float32)
        return total

    pair_raw = gathered_sum(
        [
            jnp.einsum("td,dje->jte", rows, w_keyvalue, preferred_element_type=jnp.float32)
            for rows in stacked
        ]
    )
    query_raw = gathered_sum(
        [jnp.dot(rows, w_query, preferred_element_type=jnp.float32) for rows in stacked],
        after=pair_raw,
    )
    lookup_vectors = rms_rows(pair_raw[0].reshape(trajs, span, heads_here, head_dim), 1e-06).astype(
        jnp.bfloat16
    )
    values = pair_raw[1].reshape(trajs, span, heads_here, head_dim).astype(jnp.bfloat16)
    prior_keys, prior_values = shifted(
        (lookup_vectors.reshape(trajs, span, inner_here), values.reshape(trajs, span, inner_here)),
        "seq",
        1,
    )
    queries = rms_rows(query_raw.reshape(trajs, span, heads_here, head_dim), 1e-06).astype(
        jnp.bfloat16
    )
    keep = (1 - resets[:, 0]).astype(jnp.float32)
    climb = jnp.cumsum(log_retain, axis=-1)
    whole = climb[:, :, -1]
    factor = jnp.exp(whole) * keep[:, None]
    weight = jnp.exp(whole[:, :, None] - climb)
    local_state = jnp.einsum(
        "bht,bthd,bthe->bhde",
        weight,
        lookup_vectors.astype(jnp.float32),
        values.astype(jnp.float32),
        precision=lax.Precision.HIGHEST,
    )
    local_mass = jnp.sum(weight * weight, axis=-1)

    def as_block(per_head):
        padded = jnp.pad(per_head, ((0, 0), (0, head_dim * head_dim - heads_here)))
        return padded.reshape(trajs, 1, head_dim, head_dim)

    local_both = jnp.concatenate([local_state, as_block(local_mass)], axis=1)
    factor_both = jnp.concatenate(
        [jnp.broadcast_to(factor[:, :, None, None], local_state.shape), as_block(factor * factor)],
        axis=1,
    )

    def relay_turn(turn, carry):
        return shifted((factor_both * carry + local_both).astype(jnp.bfloat16), "seq", 1).astype(
            jnp.float32
        )

    local_both, prior_keys, prior_values = lax.optimization_barrier((local_both, prior_keys, prior_values))
    entering_both = jnp.zeros_like(local_both)
    for turn in range(lax.axis_size("seq") - 1):
        entering_both = relay_turn(turn, entering_both)
    entering = entering_both[:, :heads_here]
    entering_mass = entering_both[:, heads_here].reshape(trajs, head_dim * head_dim)[:, :heads_here]
    entering = entering * keep[:, None, None, None]
    entering_mass = entering_mass * keep[:, None]
    read = jnp.einsum(
        "bthd,bhde->bthe", queries, entering.astype(jnp.bfloat16), preferred_element_type=jnp.float32
    )
    read = read * jnp.exp(climb).transpose(0, 2, 1)[..., None]
    read = read / jnp.sqrt(head_dim * (1.0 + entering_mass))[:, None, :, None]
    allow = (keep > 0.5) & (lax.axis_index("seq") > 0)
    window = window_mix(
        queries,
        lookup_vectors,
        values,
        prior_keys.reshape(trajs, span, heads_here, head_dim),
        prior_values.reshape(trajs, span, heads_here, head_dim),
        allow,
        scale,
    )
    attended = (window + read).astype(jnp.bfloat16).reshape(count, inner_here)
    w_output = lax.optimization_barrier((w_output, pair_raw))[0]
    out_block = w_output.shape[1]
    from_ranks = jnp.stack(
        [w_output]
        + [
            lax.ppermute(w_output, "wloop", [(source, (source + step) % ways) for source in range(ways)])
            for step in range(1, ways)
        ]
    )
    cores = lax.axis_size("heads")
    core = lax.axis_index("heads")
    share = width // cores

    blocks_per_share = share // out_block

    def output_share(index):
        parts = []
        for part in range(blocks_per_share):
            rank = index * blocks_per_share + part
            parts.append(
                jnp.dot(
                    attended,
                    lax.dynamic_index_in_dim(from_ranks, (me - rank) % ways, 0, keepdims=False),
                    preferred_element_type=jnp.float32,
                )
            )
        return jnp.concatenate(parts, axis=1) if blocks_per_share > 1 else parts[0]

    received = [
        lax.ppermute(
            output_share((core + step) % cores).astype(jnp.bfloat16),
            "heads",
            [(source, (source + step) % cores) for source in range(cores)],
        )
        for step in range(1, cores)
    ]
    summed = lax.optimization_barrier(output_share(core))
    for piece in received:
        summed = summed + piece.astype(jnp.float32)
    residual = lax.dynamic_slice_in_dim(
        activations.reshape(count, width), core * share, share, 1
    )
    return (residual.astype(jnp.float32) + summed).astype(jnp.bfloat16).reshape(trajs, span, share)


def solution(mesh):
    placed = (
        P(("groups", "wloop"), "seq", None),
        P(),
        P("wloop", "heads"),
        P("wloop", None, "heads"),
        P("heads", "wloop"),
        P(("groups", "wloop"), "heads", "seq"),
        P(("groups", "wloop"), "seq"),
    )
    return jax.shard_map(
        shards,
        mesh=mesh,
        in_specs=placed,
        out_specs=P(("groups", "wloop"), "seq", "heads"),
        check_vma=False,
    )
```

```python
import math

import jax
import jax.numpy as jnp
from jax import lax
from jax.sharding import PartitionSpec as P

SCORE_SCALE = 2.0


def shifted(value, axis, steps):
    count = lax.axis_size(axis)
    initial, last = (max(0, -steps), min(count, count - steps))
    return lax.ppermute(value, axis, [(source, source + steps) for source in range(initial, last)])


def rms_rows(values, eps):
    return values * lax.rsqrt(jnp.mean(values * values, axis=-1, keepdims=True) + eps)


def window_mix(queries, lookup_vectors, values, prior_keys, prior_values, allow, scale):
    own = (
        jnp.einsum("bihd,bjhd->bhij", queries, lookup_vectors, preferred_element_type=jnp.float32)
        * scale
    )
    prior = (
        jnp.einsum("bihd,bjhd->bhij", queries, prior_keys, preferred_element_type=jnp.float32)
        * scale
    )
    span = queries.shape[1]
    row_pos = lax.broadcasted_iota(jnp.int32, (span, span), 0)
    column_pos = lax.broadcasted_iota(jnp.int32, (span, span), 1)
    own_w = jnp.where(column_pos <= row_pos, jnp.exp(own), 0.0)
    prior_w = jnp.where((column_pos > row_pos) & allow[:, None, None, None], jnp.exp(prior), 0.0)
    total = jnp.sum(own_w, axis=-1, keepdims=True) + jnp.sum(prior_w, axis=-1, keepdims=True)
    own_p = (own_w / total).astype(jnp.bfloat16)
    prior_p = (prior_w / total).astype(jnp.bfloat16)
    return jnp.einsum(
        "bhij,bjhd->bihd", own_p, values, preferred_element_type=jnp.float32
    ) + jnp.einsum("bhij,bjhd->bihd", prior_p, prior_values, preferred_element_type=jnp.float32)


def shards(activations, norm_gain, w_query, w_keyvalue, w_output, log_retain, resets):
    trajs, span, width = activations.shape
    heads_here = log_retain.shape[1]
    inner_here = w_query.shape[1]
    head_dim = inner_here // heads_here
    scale = SCORE_SCALE / math.sqrt(head_dim)
    count = trajs * span
    normed = (rms_rows(activations.astype(jnp.float32), 1e-05) * norm_gain).astype(jnp.bfloat16)
    normed = normed.reshape(count, width)
    ways = lax.axis_size("wloop")
    me = lax.axis_index("wloop")
    block = width // ways

    def feature_block(index):
        return lax.dynamic_slice_in_dim(normed, index * block, block, 1)

    cores = lax.axis_size("heads")
    core = lax.axis_index("heads")
    share_rows = count // cores

    def from_cores(part):
        pieces = [part]
        for step in range(1, cores):
            pieces.append(
                lax.ppermute(part, "heads", [(source, (source + step) % cores) for source in range(cores)])
            )
        order = (core - jnp.arange(cores)) % cores
        return jnp.take(jnp.stack(pieces), order, axis=0).reshape(count, block)

    stacked = [feature_block(me)]
    for step in range(1, ways):
        part = lax.dynamic_slice_in_dim(feature_block((me + step) % ways), core * share_rows, share_rows, 0)
        stacked.append(
            from_cores(
                lax.ppermute(
                    part,
                    "wloop",
                    [(source, (source + step) % ways) for source in range(ways)],
                )
            )
        )

    def gathered_sum(partials, after=None):
        total = partials[0]
        for step in range(1, ways):
            outgoing = partials[step].astype(jnp.bfloat16)
            if after is not None:
                outgoing = lax.optimization_barrier((outgoing, after))[0]
            total = total + lax.ppermute(
                outgoing,
                "wloop",
                [(source, (source - step) % ways) for source in range(ways)],
            ).astype(jnp.float32)
        return total

    kv_partials = [
        jnp.einsum("td,dje->jte", rows, w_keyvalue, preferred_element_type=jnp.float32)
        for rows in stacked
    ]
    pieces = 2
    rows_per = count // pieces
    raw_chunks, key_chunks, value_chunks, prior_chunks = [], [], [], []
    for piece in range(pieces):
        raw = gathered_sum(
            [p[:, piece * rows_per : (piece + 1) * rows_per] for p in kv_partials],
            after=key_chunks[-1] if key_chunks else None,
        )
        keys_here = rms_rows(raw[0].reshape(rows_per, heads_here, head_dim), 1e-06).astype(jnp.bfloat16)
        values_here = raw[1].reshape(rows_per, heads_here, head_dim).astype(jnp.bfloat16)
        keys_here, values_here = lax.optimization_barrier((keys_here, values_here))
        prior_chunks.append(
            shifted(
                (keys_here.reshape(rows_per, inner_here), values_here.reshape(rows_per, inner_here)),
                "seq",
                1,
            )
        )
        raw_chunks.append(raw)
        key_chunks.append(keys_here)
        value_chunks.append(values_here)
    pair_raw = jnp.concatenate(raw_chunks, axis=1)
    query_raw = gathered_sum(
        [jnp.dot(rows, w_query, preferred_element_type=jnp.float32) for rows in stacked],
        after=pair_raw,
    )
    lookup_vectors = jnp.concatenate(key_chunks, axis=0).reshape(trajs, span, heads_here, head_dim)
    values = jnp.concatenate(value_chunks, axis=0).reshape(trajs, span, heads_here, head_dim)
    prior_keys = jnp.concatenate([p[0] for p in prior_chunks], axis=0).reshape(trajs, span, inner_here)
    prior_values = jnp.concatenate([p[1] for p in prior_chunks], axis=0).reshape(trajs, span, inner_here)
    queries = rms_rows(query_raw.reshape(trajs, span, heads_here, head_dim), 1e-06).astype(
        jnp.bfloat16
    )
    keep = (1 - resets[:, 0]).astype(jnp.float32)
    climb = jnp.cumsum(log_retain, axis=-1)
    whole = climb[:, :, -1]
    factor = jnp.exp(whole) * keep[:, None]
    weight = jnp.exp(whole[:, :, None] - climb)
    local_state = jnp.einsum(
        "bht,bthd,bthe->bhde",
        weight,
        lookup_vectors.astype(jnp.float32),
        values.astype(jnp.float32),
        precision=lax.Precision.HIGHEST,
    )
    local_mass = jnp.sum(weight * weight, axis=-1)

    def as_block(per_head):
        padded = jnp.pad(per_head, ((0, 0), (0, head_dim * head_dim - heads_here)))
        return padded.reshape(trajs, 1, head_dim, head_dim)

    local_both = jnp.concatenate([local_state, as_block(local_mass)], axis=1)
    factor_both = jnp.concatenate(
        [jnp.broadcast_to(factor[:, :, None, None], local_state.shape), as_block(factor * factor)],
        axis=1,
    )

    def relay_turn(turn, carry):
        return shifted((factor_both * carry + local_both).astype(jnp.bfloat16), "seq", 1).astype(
            jnp.float32
        )

    local_both, prior_keys, prior_values = lax.optimization_barrier((local_both, prior_keys, prior_values))
    entering_both = jnp.zeros_like(local_both)
    for turn in range(lax.axis_size("seq") - 1):
        entering_both = relay_turn(turn, entering_both)
    entering = entering_both[:, :heads_here]
    entering_mass = entering_both[:, heads_here].reshape(trajs, head_dim * head_dim)[:, :heads_here]
    entering = entering * keep[:, None, None, None]
    entering_mass = entering_mass * keep[:, None]
    read = jnp.einsum(
        "bthd,bhde->bthe", queries, entering.astype(jnp.bfloat16), preferred_element_type=jnp.float32
    )
    read = read * jnp.exp(climb).transpose(0, 2, 1)[..., None]
    read = read / jnp.sqrt(head_dim * (1.0 + entering_mass))[:, None, :, None]
    allow = (keep > 0.5) & (lax.axis_index("seq") > 0)
    window = window_mix(
        queries,
        lookup_vectors,
        values,
        prior_keys.reshape(trajs, span, heads_here, head_dim),
        prior_values.reshape(trajs, span, heads_here, head_dim),
        allow,
        scale,
    )
    attended = (window + read).astype(jnp.bfloat16).reshape(count, inner_here)
    w_output = lax.optimization_barrier((w_output, pair_raw))[0]
    out_block = w_output.shape[1]
    from_ranks = jnp.stack(
        [w_output]
        + [
            lax.ppermute(w_output, "wloop", [(source, (source + step) % ways) for source in range(ways)])
            for step in range(1, ways)
        ]
    )
    cores = lax.axis_size("heads")
    core = lax.axis_index("heads")
    share = width // cores

    blocks_per_share = share // out_block

    def output_share(index):
        parts = []
        for part in range(blocks_per_share):
            rank = index * blocks_per_share + part
            parts.append(
                jnp.dot(
                    attended,
                    lax.dynamic_index_in_dim(from_ranks, (me - rank) % ways, 0, keepdims=False),
                    preferred_element_type=jnp.float32,
                )
            )
        return jnp.concatenate(parts, axis=1) if blocks_per_share > 1 else parts[0]

    received = [
        lax.ppermute(
            output_share((core + step) % cores).astype(jnp.bfloat16),
            "heads",
            [(source, (source + step) % cores) for source in range(cores)],
        )
        for step in range(1, cores)
    ]
    summed = lax.optimization_barrier(output_share(core))
    for piece in received:
        summed = summed + piece.astype(jnp.float32)
    residual = lax.dynamic_slice_in_dim(
        activations.reshape(count, width), core * share, share, 1
    )
    return (residual.astype(jnp.float32) + summed).astype(jnp.bfloat16).reshape(trajs, span, share)


def solution(mesh):
    placed = (
        P(("groups", "wloop"), "seq", None),
        P(),
        P("wloop", "heads"),
        P("wloop", None, "heads"),
        P("heads", "wloop"),
        P(("groups", "wloop"), "heads", "seq"),
        P(("groups", "wloop"), "seq"),
    )
    return jax.shard_map(
        shards,
        mesh=mesh,
        in_specs=placed,
        out_specs=P(("groups", "wloop"), "seq", "heads"),
        check_vma=False,
    )
```

```python
import math

import jax
import jax.numpy as jnp
from jax import lax
from jax.sharding import PartitionSpec as P

SCORE_SCALE = 2.0


def shifted(value, axis, steps):
    count = lax.axis_size(axis)
    initial, last = (max(0, -steps), min(count, count - steps))
    return lax.ppermute(value, axis, [(source, source + steps) for source in range(initial, last)])


def rms_rows(values, eps):
    return values * lax.rsqrt(jnp.mean(values * values, axis=-1, keepdims=True) + eps)


def window_mix(queries, lookup_vectors, values, prior_keys, prior_values, allow, scale):
    own = (
        jnp.einsum("bihd,bjhd->bhij", queries, lookup_vectors, preferred_element_type=jnp.float32)
        * scale
    )
    prior = (
        jnp.einsum("bihd,bjhd->bhij", queries, prior_keys, preferred_element_type=jnp.float32)
        * scale
    )
    span = queries.shape[1]
    row_pos = lax.broadcasted_iota(jnp.int32, (span, span), 0)
    column_pos = lax.broadcasted_iota(jnp.int32, (span, span), 1)
    own_w = jnp.where(column_pos <= row_pos, jnp.exp(own), 0.0)
    prior_w = jnp.where((column_pos > row_pos) & allow[:, None, None, None], jnp.exp(prior), 0.0)
    total = jnp.sum(own_w, axis=-1, keepdims=True) + jnp.sum(prior_w, axis=-1, keepdims=True)
    own_p = (own_w / total).astype(jnp.bfloat16)
    prior_p = (prior_w / total).astype(jnp.bfloat16)
    return jnp.einsum(
        "bhij,bjhd->bihd", own_p, values, preferred_element_type=jnp.float32
    ) + jnp.einsum("bhij,bjhd->bihd", prior_p, prior_values, preferred_element_type=jnp.float32)


def shards(activations, norm_gain, w_query, w_keyvalue, w_output, log_retain, resets):
    trajs, span, width = activations.shape
    heads_here = log_retain.shape[1]
    inner_here = w_query.shape[1]
    head_dim = inner_here // heads_here
    scale = SCORE_SCALE / math.sqrt(head_dim)
    count = trajs * span
    normed = (rms_rows(activations.astype(jnp.float32), 1e-05) * norm_gain).astype(jnp.bfloat16)
    normed = normed.reshape(count, width)
    ways = lax.axis_size("wloop")
    me = lax.axis_index("wloop")
    block = width // ways

    def feature_block(index):
        return lax.dynamic_slice_in_dim(normed, index * block, block, 1)

    cores = lax.axis_size("heads")
    core = lax.axis_index("heads")
    share_rows = count // cores

    def from_cores(part):
        pieces = [part]
        for step in range(1, cores):
            pieces.append(
                lax.ppermute(part, "heads", [(source, (source + step) % cores) for source in range(cores)])
            )
        order = (core - jnp.arange(cores)) % cores
        return jnp.take(jnp.stack(pieces), order, axis=0).reshape(count, block)

    stacked = [feature_block(me)]
    for step in range(1, ways):
        part = lax.dynamic_slice_in_dim(feature_block((me + step) % ways), core * share_rows, share_rows, 0)
        stacked.append(
            from_cores(
                lax.ppermute(
                    part,
                    "wloop",
                    [(source, (source + step) % ways) for source in range(ways)],
                )
            )
        )

    def gathered_sum(partials, after=None):
        total = partials[0]
        for step in range(1, ways):
            outgoing = partials[step].astype(jnp.bfloat16)
            if after is not None:
                outgoing = lax.optimization_barrier((outgoing, after))[0]
            total = total + lax.ppermute(
                outgoing,
                "wloop",
                [(source, (source - step) % ways) for source in range(ways)],
            ).astype(jnp.float32)
        return total

    kv_partials = [
        jnp.einsum("td,dje->jte", rows, w_keyvalue, preferred_element_type=jnp.float32)
        for rows in stacked
    ]
    pieces = 2
    rows_per = count // pieces
    raw_chunks, key_chunks, value_chunks, prior_chunks = [], [], [], []
    for piece in range(pieces):
        raw = gathered_sum(
            [p[:, piece * rows_per : (piece + 1) * rows_per] for p in kv_partials],
            after=key_chunks[-1] if key_chunks else None,
        )
        keys_here = rms_rows(raw[0].reshape(rows_per, heads_here, head_dim), 1e-06).astype(jnp.bfloat16)
        values_here = raw[1].reshape(rows_per, heads_here, head_dim).astype(jnp.bfloat16)
        keys_here, values_here = lax.optimization_barrier((keys_here, values_here))
        prior_chunks.append(
            shifted(
                (keys_here.reshape(rows_per, inner_here), values_here.reshape(rows_per, inner_here)),
                "seq",
                1,
            )
        )
        raw_chunks.append(raw)
        key_chunks.append(keys_here)
        value_chunks.append(values_here)
    pair_raw = jnp.concatenate(raw_chunks, axis=1)
    query_raw = gathered_sum(
        [jnp.dot(rows, w_query, preferred_element_type=jnp.float32) for rows in stacked],
        after=pair_raw,
    )
    lookup_vectors = jnp.concatenate(key_chunks, axis=0).reshape(trajs, span, heads_here, head_dim)
    values = jnp.concatenate(value_chunks, axis=0).reshape(trajs, span, heads_here, head_dim)
    prior_keys = jnp.concatenate([p[0] for p in prior_chunks], axis=0).reshape(trajs, span, inner_here)
    prior_values = jnp.concatenate([p[1] for p in prior_chunks], axis=0).reshape(trajs, span, inner_here)
    queries = rms_rows(query_raw.reshape(trajs, span, heads_here, head_dim), 1e-06).astype(
        jnp.bfloat16
    )
    keep = (1 - resets[:, 0]).astype(jnp.float32)
    climb = jnp.cumsum(log_retain, axis=-1)
    whole = climb[:, :, -1]
    factor = jnp.exp(whole) * keep[:, None]
    weight = jnp.exp(whole[:, :, None] - climb)
    local_state = jnp.einsum(
        "bht,bthd,bthe->bhde",
        weight,
        lookup_vectors.astype(jnp.float32),
        values.astype(jnp.float32),
        precision=lax.Precision.HIGHEST,
    )
    local_mass = jnp.sum(weight * weight, axis=-1)

    def as_block(per_head):
        padded = jnp.pad(per_head, ((0, 0), (0, head_dim * head_dim - heads_here)))
        return padded.reshape(trajs, 1, head_dim, head_dim)

    local_both = jnp.concatenate([local_state, as_block(local_mass)], axis=1)
    factor_both = jnp.concatenate(
        [jnp.broadcast_to(factor[:, :, None, None], local_state.shape), as_block(factor * factor)],
        axis=1,
    )

    def relay_turn(turn, carry):
        return shifted((factor_both * carry + local_both).astype(jnp.bfloat16), "seq", 1).astype(
            jnp.float32
        )

    local_both, prior_keys, prior_values = lax.optimization_barrier((local_both, prior_keys, prior_values))
    entering_both = jnp.zeros_like(local_both)
    for turn in range(lax.axis_size("seq") - 1):
        entering_both = relay_turn(turn, entering_both)
    entering = entering_both[:, :heads_here]
    entering_mass = entering_both[:, heads_here].reshape(trajs, head_dim * head_dim)[:, :heads_here]
    entering = entering * keep[:, None, None, None]
    entering_mass = entering_mass * keep[:, None]
    read = jnp.einsum(
        "bthd,bhde->bthe", queries, entering.astype(jnp.bfloat16), preferred_element_type=jnp.float32
    )
    read = read * jnp.exp(climb).transpose(0, 2, 1)[..., None]
    read = read / jnp.sqrt(head_dim * (1.0 + entering_mass))[:, None, :, None]
    allow = (keep > 0.5) & (lax.axis_index("seq") > 0)
    window = window_mix(
        queries,
        lookup_vectors,
        values,
        prior_keys.reshape(trajs, span, heads_here, head_dim),
        prior_values.reshape(trajs, span, heads_here, head_dim),
        allow,
        scale,
    )
    attended = (window + read).astype(jnp.bfloat16).reshape(count, inner_here)
    w_output = lax.optimization_barrier((w_output, pair_raw))[0]
    out_block = w_output.shape[1]
    half_rows = w_output.shape[0] // 2
    from_ranks = jnp.stack(
        [w_output]
        + [
            jnp.concatenate(
                [
                    lax.ppermute(
                        w_output[half * half_rows : (half + 1) * half_rows],
                        "wloop",
                        [(source, (source + step) % ways) for source in range(ways)],
                    )
                    for half in range(2)
                ],
                axis=0,
            )
            for step in range(1, ways)
        ]
    )
    cores = lax.axis_size("heads")
    core = lax.axis_index("heads")
    share = width // cores

    blocks_per_share = share // out_block

    def output_share(index):
        parts = []
        for part in range(blocks_per_share):
            rank = index * blocks_per_share + part
            parts.append(
                jnp.dot(
                    attended,
                    lax.dynamic_index_in_dim(from_ranks, (me - rank) % ways, 0, keepdims=False),
                    preferred_element_type=jnp.float32,
                )
            )
        return jnp.concatenate(parts, axis=1) if blocks_per_share > 1 else parts[0]

    received = [
        lax.ppermute(
            output_share((core + step) % cores).astype(jnp.bfloat16),
            "heads",
            [(source, (source + step) % cores) for source in range(cores)],
        )
        for step in range(1, cores)
    ]
    summed = lax.optimization_barrier(output_share(core))
    for piece in received:
        summed = summed + piece.astype(jnp.float32)
    residual = lax.dynamic_slice_in_dim(
        activations.reshape(count, width), core * share, share, 1
    )
    return (residual.astype(jnp.float32) + summed).astype(jnp.bfloat16).reshape(trajs, span, share)


def solution(mesh):
    placed = (
        P(("groups", "wloop"), "seq", None),
        P(),
        P("wloop", "heads"),
        P("wloop", None, "heads"),
        P("heads", "wloop"),
        P(("groups", "wloop"), "heads", "seq"),
        P(("groups", "wloop"), "seq"),
    )
    return jax.shard_map(
        shards,
        mesh=mesh,
        in_specs=placed,
        out_specs=P(("groups", "wloop"), "seq", "heads"),
        check_vma=False,
    )
```

```python
import math

import jax
import jax.numpy as jnp
from jax import lax
from jax.sharding import PartitionSpec as P

SCORE_SCALE = 2.0


def shifted(value, axis, steps):
    count = lax.axis_size(axis)
    initial, last = (max(0, -steps), min(count, count - steps))
    return lax.ppermute(value, axis, [(source, source + steps) for source in range(initial, last)])


def rms_rows(values, eps):
    return values * lax.rsqrt(jnp.mean(values * values, axis=-1, keepdims=True) + eps)


def window_mix(queries, lookup_vectors, values, prior_keys, prior_values, allow, scale):
    own = (
        jnp.einsum("bihd,bjhd->bhij", queries, lookup_vectors, preferred_element_type=jnp.float32)
        * scale
    )
    prior = (
        jnp.einsum("bihd,bjhd->bhij", queries, prior_keys, preferred_element_type=jnp.float32)
        * scale
    )
    span = queries.shape[1]
    row_pos = lax.broadcasted_iota(jnp.int32, (span, span), 0)
    column_pos = lax.broadcasted_iota(jnp.int32, (span, span), 1)
    own_w = jnp.where(column_pos <= row_pos, jnp.exp(own), 0.0)
    prior_w = jnp.where((column_pos > row_pos) & allow[:, None, None, None], jnp.exp(prior), 0.0)
    total = jnp.sum(own_w, axis=-1, keepdims=True) + jnp.sum(prior_w, axis=-1, keepdims=True)
    own_p = (own_w / total).astype(jnp.bfloat16)
    prior_p = (prior_w / total).astype(jnp.bfloat16)
    return jnp.einsum(
        "bhij,bjhd->bihd", own_p, values, preferred_element_type=jnp.float32
    ) + jnp.einsum("bhij,bjhd->bihd", prior_p, prior_values, preferred_element_type=jnp.float32)


def shards(activations, norm_gain, w_query, w_keyvalue, w_output, log_retain, resets):
    trajs, span, width = activations.shape
    heads_here = log_retain.shape[1]
    inner_here = w_query.shape[1]
    head_dim = inner_here // heads_here
    scale = SCORE_SCALE / math.sqrt(head_dim)
    count = trajs * span
    normed = (rms_rows(activations.astype(jnp.float32), 1e-05) * norm_gain).astype(jnp.bfloat16)
    normed = normed.reshape(count, width)
    ways = lax.axis_size("wloop")
    me = lax.axis_index("wloop")
    block = width // ways

    def feature_block(index):
        return lax.dynamic_slice_in_dim(normed, index * block, block, 1)

    cores = lax.axis_size("heads")
    core = lax.axis_index("heads")
    share_rows = count // cores

    def from_cores(part):
        pieces = [part]
        for step in range(1, cores):
            pieces.append(
                lax.ppermute(part, "heads", [(source, (source + step) % cores) for source in range(cores)])
            )
        order = (core - jnp.arange(cores)) % cores
        return jnp.take(jnp.stack(pieces), order, axis=0).reshape(count, block)

    stacked = [feature_block(me)]
    for step in range(1, ways):
        part = lax.dynamic_slice_in_dim(feature_block((me + step) % ways), core * share_rows, share_rows, 0)
        stacked.append(
            from_cores(
                lax.ppermute(
                    part,
                    "wloop",
                    [(source, (source + step) % ways) for source in range(ways)],
                )
            )
        )

    arrived = []

    def gathered_sum(partials, after=None):
        total = partials[0]
        for step in range(1, ways):
            outgoing = partials[step].astype(jnp.bfloat16)
            if after is not None:
                outgoing = lax.optimization_barrier((outgoing, after))[0]
            incoming = lax.ppermute(
                outgoing,
                "wloop",
                [(source, (source - step) % ways) for source in range(ways)],
            )
            arrived.append(incoming)
            total = total + incoming.astype(jnp.float32)
        return total

    pair_raw = gathered_sum(
        [
            jnp.einsum("td,dje->jte", rows, w_keyvalue, preferred_element_type=jnp.float32)
            for rows in stacked
        ]
    )
    query_raw = gathered_sum(
        [jnp.dot(rows, w_query, preferred_element_type=jnp.float32) for rows in stacked],
        after=tuple(arrived),
    )
    lookup_vectors = rms_rows(pair_raw[0].reshape(trajs, span, heads_here, head_dim), 1e-06).astype(
        jnp.bfloat16
    )
    values = pair_raw[1].reshape(trajs, span, heads_here, head_dim).astype(jnp.bfloat16)
    prior_keys, prior_values = shifted(
        (lookup_vectors.reshape(trajs, span, inner_here), values.reshape(trajs, span, inner_here)),
        "seq",
        1,
    )
    queries = rms_rows(query_raw.reshape(trajs, span, heads_here, head_dim), 1e-06).astype(
        jnp.bfloat16
    )
    keep = (1 - resets[:, 0]).astype(jnp.float32)
    climb = jnp.cumsum(log_retain, axis=-1)
    whole = climb[:, :, -1]
    factor = jnp.exp(whole) * keep[:, None]
    weight = jnp.exp(whole[:, :, None] - climb)
    local_state = jnp.einsum(
        "bht,bthd,bthe->bhde",
        weight,
        lookup_vectors.astype(jnp.float32),
        values.astype(jnp.float32),
        precision=lax.Precision.HIGHEST,
    )
    local_mass = jnp.sum(weight * weight, axis=-1)

    def as_block(per_head):
        padded = jnp.pad(per_head, ((0, 0), (0, head_dim * head_dim - heads_here)))
        return padded.reshape(trajs, 1, head_dim, head_dim)

    local_both = jnp.concatenate([local_state, as_block(local_mass)], axis=1)
    factor_both = jnp.concatenate(
        [jnp.broadcast_to(factor[:, :, None, None], local_state.shape), as_block(factor * factor)],
        axis=1,
    )

    def relay_turn(turn, carry):
        return shifted((factor_both * carry + local_both).astype(jnp.bfloat16), "seq", 1).astype(
            jnp.float32
        )

    local_both, prior_keys, prior_values = lax.optimization_barrier((local_both, prior_keys, prior_values))
    entering_both = jnp.zeros_like(local_both)
    for turn in range(lax.axis_size("seq") - 1):
        entering_both = relay_turn(turn, entering_both)
    entering = entering_both[:, :heads_here]
    entering_mass = entering_both[:, heads_here].reshape(trajs, head_dim * head_dim)[:, :heads_here]
    entering = entering * keep[:, None, None, None]
    entering_mass = entering_mass * keep[:, None]
    read = jnp.einsum(
        "bthd,bhde->bthe", queries, entering.astype(jnp.bfloat16), preferred_element_type=jnp.float32
    )
    read = read * jnp.exp(climb).transpose(0, 2, 1)[..., None]
    read = read / jnp.sqrt(head_dim * (1.0 + entering_mass))[:, None, :, None]
    allow = (keep > 0.5) & (lax.axis_index("seq") > 0)
    window = window_mix(
        queries,
        lookup_vectors,
        values,
        prior_keys.reshape(trajs, span, heads_here, head_dim),
        prior_values.reshape(trajs, span, heads_here, head_dim),
        allow,
        scale,
    )
    attended = (window + read).astype(jnp.bfloat16).reshape(count, inner_here)
    w_output = lax.optimization_barrier((w_output, arrived[0]))[0]
    out_block = w_output.shape[1]
    from_ranks = jnp.stack(
        [w_output]
        + [
            lax.ppermute(w_output, "wloop", [(source, (source + step) % ways) for source in range(ways)])
            for step in range(1, ways)
        ]
    )
    cores = lax.axis_size("heads")
    core = lax.axis_index("heads")
    share = width // cores

    blocks_per_share = share // out_block

    def output_share(index):
        parts = []
        for part in range(blocks_per_share):
            rank = index * blocks_per_share + part
            parts.append(
                jnp.dot(
                    attended,
                    lax.dynamic_index_in_dim(from_ranks, (me - rank) % ways, 0, keepdims=False),
                    preferred_element_type=jnp.float32,
                )
            )
        return jnp.concatenate(parts, axis=1) if blocks_per_share > 1 else parts[0]

    received = [
        lax.ppermute(
            output_share((core + step) % cores).astype(jnp.bfloat16),
            "heads",
            [(source, (source + step) % cores) for source in range(cores)],
        )
        for step in range(1, cores)
    ]
    summed = lax.optimization_barrier(output_share(core))
    for piece in received:
        summed = summed + piece.astype(jnp.float32)
    residual = lax.dynamic_slice_in_dim(
        activations.reshape(count, width), core * share, share, 1
    )
    return (residual.astype(jnp.float32) + summed).astype(jnp.bfloat16).reshape(trajs, span, share)


def solution(mesh):
    placed = (
        P(("groups", "wloop"), "seq", None),
        P(),
        P("wloop", "heads"),
        P("wloop", None, "heads"),
        P("heads", "wloop"),
        P(("groups", "wloop"), "heads", "seq"),
        P(("groups", "wloop"), "seq"),
    )
    return jax.shard_map(
        shards,
        mesh=mesh,
        in_specs=placed,
        out_specs=P(("groups", "wloop"), "seq", "heads"),
        check_vma=False,
    )
```

```python
import math

import jax
import jax.numpy as jnp
from jax import lax
from jax.sharding import PartitionSpec as P

SCORE_SCALE = 2.0


def shifted(value, axis, steps):
    count = lax.axis_size(axis)
    initial, last = (max(0, -steps), min(count, count - steps))
    return lax.ppermute(value, axis, [(source, source + steps) for source in range(initial, last)])


def rms_rows(values, eps):
    return values * lax.rsqrt(jnp.mean(values * values, axis=-1, keepdims=True) + eps)


def window_mix(queries, lookup_vectors, values, prior_keys, prior_values, allow, scale):
    own = (
        jnp.einsum("bihd,bjhd->bhij", queries, lookup_vectors, preferred_element_type=jnp.float32)
        * scale
    )
    prior = (
        jnp.einsum("bihd,bjhd->bhij", queries, prior_keys, preferred_element_type=jnp.float32)
        * scale
    )
    span = queries.shape[1]
    row_pos = lax.broadcasted_iota(jnp.int32, (span, span), 0)
    column_pos = lax.broadcasted_iota(jnp.int32, (span, span), 1)
    own_w = jnp.where(column_pos <= row_pos, jnp.exp(own), 0.0)
    prior_w = jnp.where((column_pos > row_pos) & allow[:, None, None, None], jnp.exp(prior), 0.0)
    total = jnp.sum(own_w, axis=-1, keepdims=True) + jnp.sum(prior_w, axis=-1, keepdims=True)
    own_p = (own_w / total).astype(jnp.bfloat16)
    prior_p = (prior_w / total).astype(jnp.bfloat16)
    return jnp.einsum(
        "bhij,bjhd->bihd", own_p, values, preferred_element_type=jnp.float32
    ) + jnp.einsum("bhij,bjhd->bihd", prior_p, prior_values, preferred_element_type=jnp.float32)


def shards(activations, norm_gain, w_query, w_keyvalue, w_output, log_retain, resets):
    trajs, span, width = activations.shape
    heads_here = log_retain.shape[1]
    inner_here = w_query.shape[1]
    head_dim = inner_here // heads_here
    scale = SCORE_SCALE / math.sqrt(head_dim)
    count = trajs * span
    normed = (rms_rows(activations.astype(jnp.float32), 1e-05) * norm_gain).astype(jnp.bfloat16)
    normed = normed.reshape(count, width)
    ways = lax.axis_size("wloop")
    me = lax.axis_index("wloop")
    block = width // ways

    def feature_block(index):
        return lax.dynamic_slice_in_dim(normed, index * block, block, 1)

    cores = lax.axis_size("heads")
    core = lax.axis_index("heads")
    share_rows = count // cores

    def from_cores(part):
        pieces = [part]
        for step in range(1, cores):
            pieces.append(
                lax.ppermute(part, "heads", [(source, (source + step) % cores) for source in range(cores)])
            )
        order = (core - jnp.arange(cores)) % cores
        return jnp.take(jnp.stack(pieces), order, axis=0).reshape(count, block)

    stacked = [feature_block(me)]
    for step in range(1, ways):
        part = lax.dynamic_slice_in_dim(feature_block((me + step) % ways), core * share_rows, share_rows, 0)
        stacked.append(
            from_cores(
                lax.ppermute(
                    part,
                    "wloop",
                    [(source, (source + step) % ways) for source in range(ways)],
                )
            )
        )

    def gathered_sum(partials, after=None):
        total = partials[0]
        for step in range(1, ways):
            outgoing = partials[step].astype(jnp.bfloat16)
            if after is not None:
                outgoing = lax.optimization_barrier((outgoing, after))[0]
            total = total + lax.ppermute(
                outgoing,
                "wloop",
                [(source, (source - step) % ways) for source in range(ways)],
            ).astype(jnp.float32)
        return total

    half_rows = count // 2
    pair_raw = jnp.concatenate(
        [
            gathered_sum(
                [
                    jnp.einsum("td,dje->jte", rows[lo:hi], w_keyvalue, preferred_element_type=jnp.float32)
                    for rows in stacked
                ]
            )
            for lo, hi in ((0, half_rows), (half_rows, count))
        ],
        axis=1,
    )
    query_raw = gathered_sum(
        [jnp.dot(rows, w_query, preferred_element_type=jnp.float32) for rows in stacked],
        after=pair_raw,
    )
    lookup_vectors = rms_rows(pair_raw[0].reshape(trajs, span, heads_here, head_dim), 1e-06).astype(
        jnp.bfloat16
    )
    values = pair_raw[1].reshape(trajs, span, heads_here, head_dim).astype(jnp.bfloat16)
    prior_keys, prior_values = shifted(
        (lookup_vectors.reshape(trajs, span, inner_here), values.reshape(trajs, span, inner_here)),
        "seq",
        1,
    )
    queries = rms_rows(query_raw.reshape(trajs, span, heads_here, head_dim), 1e-06).astype(
        jnp.bfloat16
    )
    keep = (1 - resets[:, 0]).astype(jnp.float32)
    climb = jnp.cumsum(log_retain, axis=-1)
    whole = climb[:, :, -1]
    factor = jnp.exp(whole) * keep[:, None]
    weight = jnp.exp(whole[:, :, None] - climb)
    local_state = jnp.einsum(
        "bht,bthd,bthe->bhde",
        weight,
        lookup_vectors.astype(jnp.float32),
        values.astype(jnp.float32),
        precision=lax.Precision.HIGHEST,
    )
    local_mass = jnp.sum(weight * weight, axis=-1)

    def as_block(per_head):
        padded = jnp.pad(per_head, ((0, 0), (0, head_dim * head_dim - heads_here)))
        return padded.reshape(trajs, 1, head_dim, head_dim)

    local_both = jnp.concatenate([local_state, as_block(local_mass)], axis=1)
    factor_both = jnp.concatenate(
        [jnp.broadcast_to(factor[:, :, None, None], local_state.shape), as_block(factor * factor)],
        axis=1,
    )

    def relay_turn(turn, carry):
        return shifted((factor_both * carry + local_both).astype(jnp.bfloat16), "seq", 1).astype(
            jnp.float32
        )

    local_both, prior_keys, prior_values = lax.optimization_barrier((local_both, prior_keys, prior_values))
    entering_both = jnp.zeros_like(local_both)
    for turn in range(lax.axis_size("seq") - 1):
        entering_both = relay_turn(turn, entering_both)
    entering = entering_both[:, :heads_here]
    entering_mass = entering_both[:, heads_here].reshape(trajs, head_dim * head_dim)[:, :heads_here]
    entering = entering * keep[:, None, None, None]
    entering_mass = entering_mass * keep[:, None]
    read = jnp.einsum(
        "bthd,bhde->bthe", queries, entering.astype(jnp.bfloat16), preferred_element_type=jnp.float32
    )
    read = read * jnp.exp(climb).transpose(0, 2, 1)[..., None]
    read = read / jnp.sqrt(head_dim * (1.0 + entering_mass))[:, None, :, None]
    allow = (keep > 0.5) & (lax.axis_index("seq") > 0)
    window = window_mix(
        queries,
        lookup_vectors,
        values,
        prior_keys.reshape(trajs, span, heads_here, head_dim),
        prior_values.reshape(trajs, span, heads_here, head_dim),
        allow,
        scale,
    )
    attended = (window + read).astype(jnp.bfloat16).reshape(count, inner_here)
    w_output = lax.optimization_barrier((w_output, pair_raw))[0]
    out_block = w_output.shape[1]
    from_ranks = jnp.stack(
        [w_output]
        + [
            lax.ppermute(w_output, "wloop", [(source, (source + step) % ways) for source in range(ways)])
            for step in range(1, ways)
        ]
    )
    cores = lax.axis_size("heads")
    core = lax.axis_index("heads")
    share = width // cores

    blocks_per_share = share // out_block

    def output_share(index):
        parts = []
        for part in range(blocks_per_share):
            rank = index * blocks_per_share + part
            parts.append(
                jnp.dot(
                    attended,
                    lax.dynamic_index_in_dim(from_ranks, (me - rank) % ways, 0, keepdims=False),
                    preferred_element_type=jnp.float32,
                )
            )
        return jnp.concatenate(parts, axis=1) if blocks_per_share > 1 else parts[0]

    received = [
        lax.ppermute(
            output_share((core + step) % cores).astype(jnp.bfloat16),
            "heads",
            [(source, (source + step) % cores) for source in range(cores)],
        )
        for step in range(1, cores)
    ]
    summed = lax.optimization_barrier(output_share(core))
    for piece in received:
        summed = summed + piece.astype(jnp.float32)
    residual = lax.dynamic_slice_in_dim(
        activations.reshape(count, width), core * share, share, 1
    )
    return (residual.astype(jnp.float32) + summed).astype(jnp.bfloat16).reshape(trajs, span, share)


def solution(mesh):
    placed = (
        P(("groups", "wloop"), "seq", None),
        P(),
        P("wloop", "heads"),
        P("wloop", None, "heads"),
        P("heads", "wloop"),
        P(("groups", "wloop"), "heads", "seq"),
        P(("groups", "wloop"), "seq"),
    )
    return jax.shard_map(
        shards,
        mesh=mesh,
        in_specs=placed,
        out_specs=P(("groups", "wloop"), "seq", "heads"),
        check_vma=False,
    )
```

```python
import math

import jax
import jax.numpy as jnp
from jax import lax
from jax.sharding import PartitionSpec as P

SCORE_SCALE = 2.0


def shifted(value, axis, steps):
    count = lax.axis_size(axis)
    initial, last = (max(0, -steps), min(count, count - steps))
    return lax.ppermute(value, axis, [(source, source + steps) for source in range(initial, last)])


def rms_rows(values, eps):
    return values * lax.rsqrt(jnp.mean(values * values, axis=-1, keepdims=True) + eps)


def window_mix(queries, lookup_vectors, values, prior_keys, prior_values, allow, scale):
    own = (
        jnp.einsum("bihd,bjhd->bhij", queries, lookup_vectors, preferred_element_type=jnp.float32)
        * scale
    )
    prior = (
        jnp.einsum("bihd,bjhd->bhij", queries, prior_keys, preferred_element_type=jnp.float32)
        * scale
    )
    span = queries.shape[1]
    row_pos = lax.broadcasted_iota(jnp.int32, (span, span), 0)
    column_pos = lax.broadcasted_iota(jnp.int32, (span, span), 1)
    own_w = jnp.where(column_pos <= row_pos, jnp.exp(own), 0.0)
    prior_w = jnp.where((column_pos > row_pos) & allow[:, None, None, None], jnp.exp(prior), 0.0)
    total = jnp.sum(own_w, axis=-1, keepdims=True) + jnp.sum(prior_w, axis=-1, keepdims=True)
    own_p = (own_w / total).astype(jnp.bfloat16)
    prior_p = (prior_w / total).astype(jnp.bfloat16)
    return jnp.einsum(
        "bhij,bjhd->bihd", own_p, values, preferred_element_type=jnp.float32
    ) + jnp.einsum("bhij,bjhd->bihd", prior_p, prior_values, preferred_element_type=jnp.float32)


def shards(activations, norm_gain, w_query, w_keyvalue, w_output, log_retain, resets):
    trajs, span, width = activations.shape
    heads_here = log_retain.shape[1]
    inner_here = w_query.shape[1]
    head_dim = inner_here // heads_here
    scale = SCORE_SCALE / math.sqrt(head_dim)
    count = trajs * span
    normed = (rms_rows(activations.astype(jnp.float32), 1e-05) * norm_gain).astype(jnp.bfloat16)
    normed = normed.reshape(count, width)
    ways = lax.axis_size("wloop")
    me = lax.axis_index("wloop")
    block = width // ways

    def feature_block(index):
        return lax.dynamic_slice_in_dim(normed, index * block, block, 1)

    cores = lax.axis_size("heads")
    core = lax.axis_index("heads")
    share_rows = count // cores

    def from_cores(part):
        pieces = [part]
        for step in range(1, cores):
            pieces.append(
                lax.ppermute(part, "heads", [(source, (source + step) % cores) for source in range(cores)])
            )
        order = (core - jnp.arange(cores)) % cores
        return jnp.take(jnp.stack(pieces), order, axis=0).reshape(count, block)

    stacked = [feature_block(me)]
    for step in range(1, ways):
        part = lax.dynamic_slice_in_dim(feature_block((me + step) % ways), core * share_rows, share_rows, 0)
        stacked.append(
            from_cores(
                lax.ppermute(
                    part,
                    "wloop",
                    [(source, (source + step) % ways) for source in range(ways)],
                )
            )
        )

    def gathered_sum(partials, after=None):
        total = partials[0]
        for step in range(1, ways):
            outgoing = partials[step].astype(jnp.bfloat16)
            if after is not None:
                outgoing = lax.optimization_barrier((outgoing, after))[0]
            total = total + lax.ppermute(
                outgoing,
                "wloop",
                [(source, (source - step) % ways) for source in range(ways)],
            ).astype(jnp.float32)
        return total

    half_rows = count // 2
    pair_raw = jnp.concatenate(
        [
            gathered_sum(
                [
                    jnp.einsum("td,dje->jte", rows[lo:hi], w_keyvalue, preferred_element_type=jnp.float32)
                    for rows in stacked
                ]
            )
            for lo, hi in ((0, half_rows), (half_rows, count))
        ],
        axis=1,
    )
    query_raw = gathered_sum(
        [jnp.dot(rows, w_query, preferred_element_type=jnp.float32) for rows in stacked],
        after=pair_raw,
    )
    lookup_vectors = rms_rows(pair_raw[0].reshape(trajs, span, heads_here, head_dim), 1e-06).astype(
        jnp.bfloat16
    )
    values = pair_raw[1].reshape(trajs, span, heads_here, head_dim).astype(jnp.bfloat16)
    prior_keys, prior_values = shifted(
        (lookup_vectors.reshape(trajs, span, inner_here), values.reshape(trajs, span, inner_here)),
        "seq",
        1,
    )
    queries = rms_rows(query_raw.reshape(trajs, span, heads_here, head_dim), 1e-06).astype(
        jnp.bfloat16
    )
    keep = (1 - resets[:, 0]).astype(jnp.float32)
    climb = jnp.cumsum(log_retain, axis=-1)
    whole = climb[:, :, -1]
    factor = jnp.exp(whole) * keep[:, None]
    weight = jnp.exp(whole[:, :, None] - climb)
    local_state = jnp.einsum(
        "bht,bthd,bthe->bhde",
        weight,
        lookup_vectors.astype(jnp.float32),
        values.astype(jnp.float32),
        precision=lax.Precision.HIGHEST,
    )
    local_mass = jnp.sum(weight * weight, axis=-1)

    def as_block(per_head):
        padded = jnp.pad(per_head, ((0, 0), (0, head_dim * head_dim - heads_here)))
        return padded.reshape(trajs, 1, head_dim, head_dim)

    local_both = jnp.concatenate([local_state, as_block(local_mass)], axis=1)
    factor_both = jnp.concatenate(
        [jnp.broadcast_to(factor[:, :, None, None], local_state.shape), as_block(factor * factor)],
        axis=1,
    )

    def relay_turn(turn, carry):
        return shifted((factor_both * carry + local_both).astype(jnp.bfloat16), "seq", 1).astype(
            jnp.float32
        )

    local_both, prior_keys, prior_values = lax.optimization_barrier((local_both, prior_keys, prior_values))
    entering_both = jnp.zeros_like(local_both)
    for turn in range(lax.axis_size("seq") - 1):
        entering_both = relay_turn(turn, entering_both)
    entering = entering_both[:, :heads_here]
    entering_mass = entering_both[:, heads_here].reshape(trajs, head_dim * head_dim)[:, :heads_here]
    entering = entering * keep[:, None, None, None]
    entering_mass = entering_mass * keep[:, None]
    read = jnp.einsum(
        "bthd,bhde->bthe", queries, entering.astype(jnp.bfloat16), preferred_element_type=jnp.float32
    )
    read = read * jnp.exp(climb).transpose(0, 2, 1)[..., None]
    read = read / jnp.sqrt(head_dim * (1.0 + entering_mass))[:, None, :, None]
    allow = (keep > 0.5) & (lax.axis_index("seq") > 0)
    window = window_mix(
        queries,
        lookup_vectors,
        values,
        prior_keys.reshape(trajs, span, heads_here, head_dim),
        prior_values.reshape(trajs, span, heads_here, head_dim),
        allow,
        scale,
    )
    attended = (window + read).astype(jnp.bfloat16).reshape(count, inner_here)
    w_output = lax.optimization_barrier((w_output, pair_raw))[0]
    out_block = w_output.shape[1]
    from_ranks = jnp.stack(
        [w_output]
        + [
            lax.ppermute(w_output, "wloop", [(source, (source + step) % ways) for source in range(ways)])
            for step in range(1, ways)
        ]
    )
    cores = lax.axis_size("heads")
    core = lax.axis_index("heads")
    share = width // cores

    blocks_per_share = share // out_block

    def output_share(index):
        parts = []
        for part in range(blocks_per_share):
            rank = index * blocks_per_share + part
            parts.append(
                jnp.dot(
                    attended,
                    lax.dynamic_index_in_dim(from_ranks, (me - rank) % ways, 0, keepdims=False),
                    preferred_element_type=jnp.float32,
                )
            )
        return jnp.concatenate(parts, axis=1) if blocks_per_share > 1 else parts[0]

    def output_rows(index, lo, hi):
        parts = [
            jnp.dot(
                attended[lo:hi],
                lax.dynamic_index_in_dim(from_ranks, (me - (index * blocks_per_share + part)) % ways, 0, keepdims=False),
                preferred_element_type=jnp.float32,
            )
            for part in range(blocks_per_share)
        ]
        return jnp.concatenate(parts, axis=1) if blocks_per_share > 1 else parts[0]

    half_count = count // 2
    received = [
        jnp.concatenate(
            [
                lax.ppermute(
                    output_rows((core + step) % cores, lo, hi).astype(jnp.bfloat16),
                    "heads",
                    [(source, (source + step) % cores) for source in range(cores)],
                )
                for lo, hi in ((0, half_count), (half_count, count))
            ],
            axis=0,
        )
        for step in range(1, cores)
    ]
    summed = lax.optimization_barrier(output_share(core))
    for piece in received:
        summed = summed + piece.astype(jnp.float32)
    residual = lax.dynamic_slice_in_dim(
        activations.reshape(count, width), core * share, share, 1
    )
    return (residual.astype(jnp.float32) + summed).astype(jnp.bfloat16).reshape(trajs, span, share)


def solution(mesh):
    placed = (
        P(("groups", "wloop"), "seq", None),
        P(),
        P("wloop", "heads"),
        P("wloop", None, "heads"),
        P("heads", "wloop"),
        P(("groups", "wloop"), "heads", "seq"),
        P(("groups", "wloop"), "seq"),
    )
    return jax.shard_map(
        shards,
        mesh=mesh,
        in_specs=placed,
        out_specs=P(("groups", "wloop"), "seq", "heads"),
        check_vma=False,
    )
```

```python
import math

import jax
import jax.numpy as jnp
from jax import lax
from jax.sharding import PartitionSpec as P

SCORE_SCALE = 2.0


def shifted(value, axis, steps):
    count = lax.axis_size(axis)
    initial, last = (max(0, -steps), min(count, count - steps))
    return lax.ppermute(value, axis, [(source, source + steps) for source in range(initial, last)])


def rms_rows(values, eps):
    return values * lax.rsqrt(jnp.mean(values * values, axis=-1, keepdims=True) + eps)


def window_mix(queries, lookup_vectors, values, prior_keys, prior_values, allow, scale):
    own = (
        jnp.einsum("bihd,bjhd->bhij", queries, lookup_vectors, preferred_element_type=jnp.float32)
        * scale
    )
    prior = (
        jnp.einsum("bihd,bjhd->bhij", queries, prior_keys, preferred_element_type=jnp.float32)
        * scale
    )
    span = queries.shape[1]
    row_pos = lax.broadcasted_iota(jnp.int32, (span, span), 0)
    column_pos = lax.broadcasted_iota(jnp.int32, (span, span), 1)
    own_w = jnp.where(column_pos <= row_pos, jnp.exp(own), 0.0)
    prior_w = jnp.where((column_pos > row_pos) & allow[:, None, None, None], jnp.exp(prior), 0.0)
    total = jnp.sum(own_w, axis=-1, keepdims=True) + jnp.sum(prior_w, axis=-1, keepdims=True)
    own_p = (own_w / total).astype(jnp.bfloat16)
    prior_p = (prior_w / total).astype(jnp.bfloat16)
    return jnp.einsum(
        "bhij,bjhd->bihd", own_p, values, preferred_element_type=jnp.float32
    ) + jnp.einsum("bhij,bjhd->bihd", prior_p, prior_values, preferred_element_type=jnp.float32)


def shards(activations, norm_gain, w_query, w_keyvalue, w_output, log_retain, resets):
    trajs, span, width = activations.shape
    heads_here = log_retain.shape[1]
    inner_here = w_query.shape[1]
    head_dim = inner_here // heads_here
    scale = SCORE_SCALE / math.sqrt(head_dim)
    count = trajs * span
    normed = (rms_rows(activations.astype(jnp.float32), 1e-05) * norm_gain).astype(jnp.bfloat16)
    normed = normed.reshape(count, width)
    ways = lax.axis_size("wloop")
    me = lax.axis_index("wloop")
    block = width // ways

    def feature_block(index):
        return lax.dynamic_slice_in_dim(normed, index * block, block, 1)

    cores = lax.axis_size("heads")
    core = lax.axis_index("heads")
    share_rows = count // cores

    def from_cores(part):
        pieces = [part]
        for step in range(1, cores):
            pieces.append(
                lax.ppermute(part, "heads", [(source, (source + step) % cores) for source in range(cores)])
            )
        order = (core - jnp.arange(cores)) % cores
        return jnp.take(jnp.stack(pieces), order, axis=0).reshape(count, block)

    stacked = [feature_block(me)]
    for step in range(1, ways):
        part = lax.dynamic_slice_in_dim(feature_block((me + step) % ways), core * share_rows, share_rows, 0)
        stacked.append(
            from_cores(
                lax.ppermute(
                    part,
                    "wloop",
                    [(source, (source + step) % ways) for source in range(ways)],
                )
            )
        )

    def gathered_sum(partials, after=None):
        total = partials[0]
        for step in range(1, ways):
            outgoing = partials[step].astype(jnp.bfloat16)
            if after is not None:
                outgoing = lax.optimization_barrier((outgoing, after))[0]
            total = total + lax.ppermute(
                outgoing,
                "wloop",
                [(source, (source - step) % ways) for source in range(ways)],
            ).astype(jnp.float32)
        return total

    piece_rows = count // 4
    pair_raw = jnp.concatenate(
        [
            gathered_sum(
                [
                    jnp.einsum("td,dje->jte", rows[lo:hi], w_keyvalue, preferred_element_type=jnp.float32)
                    for rows in stacked
                ]
            )
            for lo, hi in [(k * piece_rows, (k + 1) * piece_rows) for k in range(4)]
        ],
        axis=1,
    )
    query_raw = gathered_sum(
        [jnp.dot(rows, w_query, preferred_element_type=jnp.float32) for rows in stacked],
        after=pair_raw,
    )
    lookup_vectors = rms_rows(pair_raw[0].reshape(trajs, span, heads_here, head_dim), 1e-06).astype(
        jnp.bfloat16
    )
    values = pair_raw[1].reshape(trajs, span, heads_here, head_dim).astype(jnp.bfloat16)
    prior_keys, prior_values = shifted(
        (lookup_vectors.reshape(trajs, span, inner_here), values.reshape(trajs, span, inner_here)),
        "seq",
        1,
    )
    queries = rms_rows(query_raw.reshape(trajs, span, heads_here, head_dim), 1e-06).astype(
        jnp.bfloat16
    )
    keep = (1 - resets[:, 0]).astype(jnp.float32)
    climb = jnp.cumsum(log_retain, axis=-1)
    whole = climb[:, :, -1]
    factor = jnp.exp(whole) * keep[:, None]
    weight = jnp.exp(whole[:, :, None] - climb)
    local_state = jnp.einsum(
        "bht,bthd,bthe->bhde",
        weight,
        lookup_vectors.astype(jnp.float32),
        values.astype(jnp.float32),
        precision=lax.Precision.HIGHEST,
    )
    local_mass = jnp.sum(weight * weight, axis=-1)

    def as_block(per_head):
        padded = jnp.pad(per_head, ((0, 0), (0, head_dim * head_dim - heads_here)))
        return padded.reshape(trajs, 1, head_dim, head_dim)

    local_both = jnp.concatenate([local_state, as_block(local_mass)], axis=1)
    factor_both = jnp.concatenate(
        [jnp.broadcast_to(factor[:, :, None, None], local_state.shape), as_block(factor * factor)],
        axis=1,
    )

    def relay_turn(turn, carry):
        return shifted((factor_both * carry + local_both).astype(jnp.bfloat16), "seq", 1).astype(
            jnp.float32
        )

    local_both, prior_keys, prior_values = lax.optimization_barrier((local_both, prior_keys, prior_values))
    entering_both = jnp.zeros_like(local_both)
    for turn in range(lax.axis_size("seq") - 1):
        entering_both = relay_turn(turn, entering_both)
    entering = entering_both[:, :heads_here]
    entering_mass = entering_both[:, heads_here].reshape(trajs, head_dim * head_dim)[:, :heads_here]
    entering = entering * keep[:, None, None, None]
    entering_mass = entering_mass * keep[:, None]
    read = jnp.einsum(
        "bthd,bhde->bthe", queries, entering.astype(jnp.bfloat16), preferred_element_type=jnp.float32
    )
    read = read * jnp.exp(climb).transpose(0, 2, 1)[..., None]
    read = read / jnp.sqrt(head_dim * (1.0 + entering_mass))[:, None, :, None]
    allow = (keep > 0.5) & (lax.axis_index("seq") > 0)
    window = window_mix(
        queries,
        lookup_vectors,
        values,
        prior_keys.reshape(trajs, span, heads_here, head_dim),
        prior_values.reshape(trajs, span, heads_here, head_dim),
        allow,
        scale,
    )
    attended = (window + read).astype(jnp.bfloat16).reshape(count, inner_here)
    w_output = lax.optimization_barrier((w_output, pair_raw))[0]
    out_block = w_output.shape[1]
    from_ranks = jnp.stack(
        [w_output]
        + [
            lax.ppermute(w_output, "wloop", [(source, (source + step) % ways) for source in range(ways)])
            for step in range(1, ways)
        ]
    )
    cores = lax.axis_size("heads")
    core = lax.axis_index("heads")
    share = width // cores

    blocks_per_share = share // out_block

    def output_share(index):
        parts = []
        for part in range(blocks_per_share):
            rank = index * blocks_per_share + part
            parts.append(
                jnp.dot(
                    attended,
                    lax.dynamic_index_in_dim(from_ranks, (me - rank) % ways, 0, keepdims=False),
                    preferred_element_type=jnp.float32,
                )
            )
        return jnp.concatenate(parts, axis=1) if blocks_per_share > 1 else parts[0]

    received = [
        lax.ppermute(
            output_share((core + step) % cores).astype(jnp.bfloat16),
            "heads",
            [(source, (source + step) % cores) for source in range(cores)],
        )
        for step in range(1, cores)
    ]
    summed = lax.optimization_barrier(output_share(core))
    for piece in received:
        summed = summed + piece.astype(jnp.float32)
    residual = lax.dynamic_slice_in_dim(
        activations.reshape(count, width), core * share, share, 1
    )
    return (residual.astype(jnp.float32) + summed).astype(jnp.bfloat16).reshape(trajs, span, share)


def solution(mesh):
    placed = (
        P(("groups", "wloop"), "seq", None),
        P(),
        P("wloop", "heads"),
        P("wloop", None, "heads"),
        P("heads", "wloop"),
        P(("groups", "wloop"), "heads", "seq"),
        P(("groups", "wloop"), "seq"),
    )
    return jax.shard_map(
        shards,
        mesh=mesh,
        in_specs=placed,
        out_specs=P(("groups", "wloop"), "seq", "heads"),
        check_vma=False,
    )
```

```python
import math

import jax
import jax.numpy as jnp
from jax import lax
from jax.sharding import PartitionSpec as P

SCORE_SCALE = 2.0


def shifted(value, axis, steps):
    count = lax.axis_size(axis)
    initial, last = (max(0, -steps), min(count, count - steps))
    return lax.ppermute(value, axis, [(source, source + steps) for source in range(initial, last)])


def rms_rows(values, eps):
    return values * lax.rsqrt(jnp.mean(values * values, axis=-1, keepdims=True) + eps)


def window_mix(queries, lookup_vectors, values, prior_keys, prior_values, allow, scale):
    own = (
        jnp.einsum("bihd,bjhd->bhij", queries, lookup_vectors, preferred_element_type=jnp.float32)
        * scale
    )
    prior = (
        jnp.einsum("bihd,bjhd->bhij", queries, prior_keys, preferred_element_type=jnp.float32)
        * scale
    )
    span = queries.shape[1]
    row_pos = lax.broadcasted_iota(jnp.int32, (span, span), 0)
    column_pos = lax.broadcasted_iota(jnp.int32, (span, span), 1)
    own_w = jnp.where(column_pos <= row_pos, jnp.exp(own), 0.0)
    prior_w = jnp.where((column_pos > row_pos) & allow[:, None, None, None], jnp.exp(prior), 0.0)
    total = jnp.sum(own_w, axis=-1, keepdims=True) + jnp.sum(prior_w, axis=-1, keepdims=True)
    own_p = (own_w / total).astype(jnp.bfloat16)
    prior_p = (prior_w / total).astype(jnp.bfloat16)
    return jnp.einsum(
        "bhij,bjhd->bihd", own_p, values, preferred_element_type=jnp.float32
    ) + jnp.einsum("bhij,bjhd->bihd", prior_p, prior_values, preferred_element_type=jnp.float32)


def shards(activations, norm_gain, w_query, w_keyvalue, w_output, log_retain, resets):
    trajs, span, width = activations.shape
    heads_here = log_retain.shape[1]
    inner_here = w_query.shape[1]
    head_dim = inner_here // heads_here
    scale = SCORE_SCALE / math.sqrt(head_dim)
    count = trajs * span
    normed = (rms_rows(activations.astype(jnp.float32), 1e-05) * norm_gain).astype(jnp.bfloat16)
    normed = normed.reshape(count, width)
    ways = lax.axis_size("wloop")
    me = lax.axis_index("wloop")
    block = width // ways

    def feature_block(index):
        return lax.dynamic_slice_in_dim(normed, index * block, block, 1)

    cores = lax.axis_size("heads")
    core = lax.axis_index("heads")
    share_rows = count // cores

    def from_cores(part):
        pieces = [part]
        for step in range(1, cores):
            pieces.append(
                lax.ppermute(part, "heads", [(source, (source + step) % cores) for source in range(cores)])
            )
        order = (core - jnp.arange(cores)) % cores
        return jnp.take(jnp.stack(pieces), order, axis=0).reshape(count, block)

    stacked = [feature_block(me)]
    for step in range(1, ways):
        part = lax.dynamic_slice_in_dim(feature_block((me + step) % ways), core * share_rows, share_rows, 0)
        stacked.append(
            from_cores(
                lax.ppermute(
                    part,
                    "wloop",
                    [(source, (source + step) % ways) for source in range(ways)],
                )
            )
        )

    arrived = []

    def gathered_sum(partials, after=None):
        total = partials[0]
        for step in range(1, ways):
            outgoing = partials[step].astype(jnp.bfloat16)
            if after is not None:
                outgoing = lax.optimization_barrier((outgoing, after))[0]
            incoming = lax.ppermute(
                outgoing,
                "wloop",
                [(source, (source - step) % ways) for source in range(ways)],
            )
            arrived.append(incoming)
            total = total + incoming.astype(jnp.float32)
        return total

    half_rows = count // 2
    pair_raw = jnp.concatenate(
        [
            gathered_sum(
                [
                    jnp.einsum("td,dje->jte", rows[lo:hi], w_keyvalue, preferred_element_type=jnp.float32)
                    for rows in stacked
                ]
            )
            for lo, hi in ((0, half_rows), (half_rows, count))
        ],
        axis=1,
    )
    query_raw = gathered_sum(
        [jnp.dot(rows, w_query, preferred_element_type=jnp.float32) for rows in stacked],
        after=tuple(arrived),
    )
    lookup_vectors = rms_rows(pair_raw[0].reshape(trajs, span, heads_here, head_dim), 1e-06).astype(
        jnp.bfloat16
    )
    values = pair_raw[1].reshape(trajs, span, heads_here, head_dim).astype(jnp.bfloat16)
    prior_keys, prior_values = shifted(
        (lookup_vectors.reshape(trajs, span, inner_here), values.reshape(trajs, span, inner_here)),
        "seq",
        1,
    )
    queries = rms_rows(query_raw.reshape(trajs, span, heads_here, head_dim), 1e-06).astype(
        jnp.bfloat16
    )
    keep = (1 - resets[:, 0]).astype(jnp.float32)
    climb = jnp.cumsum(log_retain, axis=-1)
    whole = climb[:, :, -1]
    factor = jnp.exp(whole) * keep[:, None]
    weight = jnp.exp(whole[:, :, None] - climb)
    local_state = jnp.einsum(
        "bht,bthd,bthe->bhde",
        weight,
        lookup_vectors.astype(jnp.float32),
        values.astype(jnp.float32),
        precision=lax.Precision.HIGHEST,
    )
    local_mass = jnp.sum(weight * weight, axis=-1)

    def as_block(per_head):
        padded = jnp.pad(per_head, ((0, 0), (0, head_dim * head_dim - heads_here)))
        return padded.reshape(trajs, 1, head_dim, head_dim)

    local_both = jnp.concatenate([local_state, as_block(local_mass)], axis=1)
    factor_both = jnp.concatenate(
        [jnp.broadcast_to(factor[:, :, None, None], local_state.shape), as_block(factor * factor)],
        axis=1,
    )

    def relay_turn(turn, carry):
        return shifted((factor_both * carry + local_both).astype(jnp.bfloat16), "seq", 1).astype(
            jnp.float32
        )

    local_both, prior_keys, prior_values = lax.optimization_barrier((local_both, prior_keys, prior_values))
    entering_both = jnp.zeros_like(local_both)
    for turn in range(lax.axis_size("seq") - 1):
        entering_both = relay_turn(turn, entering_both)
    entering = entering_both[:, :heads_here]
    entering_mass = entering_both[:, heads_here].reshape(trajs, head_dim * head_dim)[:, :heads_here]
    entering = entering * keep[:, None, None, None]
    entering_mass = entering_mass * keep[:, None]
    read = jnp.einsum(
        "bthd,bhde->bthe", queries, entering.astype(jnp.bfloat16), preferred_element_type=jnp.float32
    )
    read = read * jnp.exp(climb).transpose(0, 2, 1)[..., None]
    read = read / jnp.sqrt(head_dim * (1.0 + entering_mass))[:, None, :, None]
    allow = (keep > 0.5) & (lax.axis_index("seq") > 0)
    window = window_mix(
        queries,
        lookup_vectors,
        values,
        prior_keys.reshape(trajs, span, heads_here, head_dim),
        prior_values.reshape(trajs, span, heads_here, head_dim),
        allow,
        scale,
    )
    attended = (window + read).astype(jnp.bfloat16).reshape(count, inner_here)
    w_output = lax.optimization_barrier((w_output, arrived[ways - 1]))[0]
    out_block = w_output.shape[1]
    from_ranks = jnp.stack(
        [w_output]
        + [
            lax.ppermute(w_output, "wloop", [(source, (source + step) % ways) for source in range(ways)])
            for step in range(1, ways)
        ]
    )
    cores = lax.axis_size("heads")
    core = lax.axis_index("heads")
    share = width // cores

    blocks_per_share = share // out_block

    def output_share(index):
        parts = []
        for part in range(blocks_per_share):
            rank = index * blocks_per_share + part
            parts.append(
                jnp.dot(
                    attended,
                    lax.dynamic_index_in_dim(from_ranks, (me - rank) % ways, 0, keepdims=False),
                    preferred_element_type=jnp.float32,
                )
            )
        return jnp.concatenate(parts, axis=1) if blocks_per_share > 1 else parts[0]

    received = [
        lax.ppermute(
            output_share((core + step) % cores).astype(jnp.bfloat16),
            "heads",
            [(source, (source + step) % cores) for source in range(cores)],
        )
        for step in range(1, cores)
    ]
    summed = lax.optimization_barrier(output_share(core))
    for piece in received:
        summed = summed + piece.astype(jnp.float32)
    residual = lax.dynamic_slice_in_dim(
        activations.reshape(count, width), core * share, share, 1
    )
    return (residual.astype(jnp.float32) + summed).astype(jnp.bfloat16).reshape(trajs, span, share)


def solution(mesh):
    placed = (
        P(("groups", "wloop"), "seq", None),
        P(),
        P("wloop", "heads"),
        P("wloop", None, "heads"),
        P("heads", "wloop"),
        P(("groups", "wloop"), "heads", "seq"),
        P(("groups", "wloop"), "seq"),
    )
    return jax.shard_map(
        shards,
        mesh=mesh,
        in_specs=placed,
        out_specs=P(("groups", "wloop"), "seq", "heads"),
        check_vma=False,
    )
```

```python
import math

import jax
import jax.numpy as jnp
from jax import lax
from jax.sharding import PartitionSpec as P

SCORE_SCALE = 2.0


def shifted(value, axis, steps):
    count = lax.axis_size(axis)
    initial, last = (max(0, -steps), min(count, count - steps))
    return lax.ppermute(value, axis, [(source, source + steps) for source in range(initial, last)])


def rms_rows(values, eps):
    return values * lax.rsqrt(jnp.mean(values * values, axis=-1, keepdims=True) + eps)


def window_mix(queries, lookup_vectors, values, prior_keys, prior_values, allow, scale):
    own = (
        jnp.einsum("bihd,bjhd->bhij", queries, lookup_vectors, preferred_element_type=jnp.float32)
        * scale
    )
    prior = (
        jnp.einsum("bihd,bjhd->bhij", queries, prior_keys, preferred_element_type=jnp.float32)
        * scale
    )
    span = queries.shape[1]
    row_pos = lax.broadcasted_iota(jnp.int32, (span, span), 0)
    column_pos = lax.broadcasted_iota(jnp.int32, (span, span), 1)
    own_w = jnp.where(column_pos <= row_pos, jnp.exp(own), 0.0)
    prior_w = jnp.where((column_pos > row_pos) & allow[:, None, None, None], jnp.exp(prior), 0.0)
    total = jnp.sum(own_w, axis=-1, keepdims=True) + jnp.sum(prior_w, axis=-1, keepdims=True)
    own_p = (own_w / total).astype(jnp.bfloat16)
    prior_p = (prior_w / total).astype(jnp.bfloat16)
    return jnp.einsum(
        "bhij,bjhd->bihd", own_p, values, preferred_element_type=jnp.float32
    ) + jnp.einsum("bhij,bjhd->bihd", prior_p, prior_values, preferred_element_type=jnp.float32)


def shards(activations, norm_gain, w_query, w_keyvalue, w_output, log_retain, resets):
    trajs, span, width = activations.shape
    heads_here = log_retain.shape[1]
    inner_here = w_query.shape[1]
    head_dim = inner_here // heads_here
    scale = SCORE_SCALE / math.sqrt(head_dim)
    count = trajs * span
    normed = (rms_rows(activations.astype(jnp.float32), 1e-05) * norm_gain).astype(jnp.bfloat16)
    normed = normed.reshape(count, width)
    ways = lax.axis_size("wloop")
    me = lax.axis_index("wloop")
    block = width // ways

    def feature_block(index):
        return lax.dynamic_slice_in_dim(normed, index * block, block, 1)

    cores = lax.axis_size("heads")
    core = lax.axis_index("heads")
    share_rows = count // cores

    def from_cores(part):
        pieces = [part]
        for step in range(1, cores):
            pieces.append(
                lax.ppermute(part, "heads", [(source, (source + step) % cores) for source in range(cores)])
            )
        order = (core - jnp.arange(cores)) % cores
        return jnp.take(jnp.stack(pieces), order, axis=0).reshape(count, block)

    stacked = [feature_block(me)]
    for step in range(1, ways):
        part = lax.dynamic_slice_in_dim(feature_block((me + step) % ways), core * share_rows, share_rows, 0)
        stacked.append(
            from_cores(
                lax.ppermute(
                    part,
                    "wloop",
                    [(source, (source + step) % ways) for source in range(ways)],
                )
            )
        )

    def gathered_sum(partials, after=None):
        total = partials[0]
        for step in range(1, ways):
            outgoing = partials[step].astype(jnp.bfloat16)
            if after is not None:
                outgoing = lax.optimization_barrier((outgoing, after))[0]
            total = total + lax.ppermute(
                outgoing,
                "wloop",
                [(source, (source - step) % ways) for source in range(ways)],
            ).astype(jnp.float32)
        return total

    half_rows = count // 2
    pair_raw = jnp.concatenate(
        [
            gathered_sum(
                [
                    jnp.einsum("td,dje->jte", rows[lo:hi], w_keyvalue, preferred_element_type=jnp.float32)
                    for rows in stacked
                ]
            )
            for lo, hi in ((0, half_rows), (half_rows, count))
        ],
        axis=1,
    )
    query_raw = gathered_sum(
        [jnp.dot(rows, w_query, preferred_element_type=jnp.float32) for rows in stacked],
        after=pair_raw,
    )
    lookup_vectors = rms_rows(pair_raw[0].reshape(trajs, span, heads_here, head_dim), 1e-06).astype(
        jnp.bfloat16
    )
    values = pair_raw[1].reshape(trajs, span, heads_here, head_dim).astype(jnp.bfloat16)
    prior_keys, prior_values = shifted(
        (lookup_vectors.reshape(trajs, span, inner_here), values.reshape(trajs, span, inner_here)),
        "seq",
        1,
    )
    queries = rms_rows(query_raw.reshape(trajs, span, heads_here, head_dim), 1e-06).astype(
        jnp.bfloat16
    )
    keep = (1 - resets[:, 0]).astype(jnp.float32)
    climb = jnp.cumsum(log_retain, axis=-1)
    whole = climb[:, :, -1]
    factor = jnp.exp(whole) * keep[:, None]
    weight = jnp.exp(whole[:, :, None] - climb)
    weighted = weight.transpose(0, 2, 1)[..., None] * lookup_vectors.astype(jnp.float32)
    weighted_hi = weighted.astype(jnp.bfloat16)
    weighted_lo = (weighted - weighted_hi.astype(jnp.float32)).astype(jnp.bfloat16)
    local_state = jnp.einsum(
        "bthd,bthe->bhde", weighted_hi, values, preferred_element_type=jnp.float32
    ) + jnp.einsum("bthd,bthe->bhde", weighted_lo, values, preferred_element_type=jnp.float32)
    local_mass = jnp.sum(weight * weight, axis=-1)

    def as_block(per_head):
        padded = jnp.pad(per_head, ((0, 0), (0, head_dim * head_dim - heads_here)))
        return padded.reshape(trajs, 1, head_dim, head_dim)

    local_both = jnp.concatenate([local_state, as_block(local_mass)], axis=1)
    factor_both = jnp.concatenate(
        [jnp.broadcast_to(factor[:, :, None, None], local_state.shape), as_block(factor * factor)],
        axis=1,
    )

    def relay_turn(turn, carry):
        return shifted((factor_both * carry + local_both).astype(jnp.bfloat16), "seq", 1).astype(
            jnp.float32
        )

    local_both, prior_keys, prior_values = lax.optimization_barrier((local_both, prior_keys, prior_values))
    entering_both = jnp.zeros_like(local_both)
    for turn in range(lax.axis_size("seq") - 1):
        entering_both = relay_turn(turn, entering_both)
    entering = entering_both[:, :heads_here]
    entering_mass = entering_both[:, heads_here].reshape(trajs, head_dim * head_dim)[:, :heads_here]
    entering = entering * keep[:, None, None, None]
    entering_mass = entering_mass * keep[:, None]
    read = jnp.einsum(
        "bthd,bhde->bthe", queries, entering.astype(jnp.bfloat16), preferred_element_type=jnp.float32
    )
    read = read * jnp.exp(climb).transpose(0, 2, 1)[..., None]
    read = read / jnp.sqrt(head_dim * (1.0 + entering_mass))[:, None, :, None]
    allow = (keep > 0.5) & (lax.axis_index("seq") > 0)
    window = window_mix(
        queries,
        lookup_vectors,
        values,
        prior_keys.reshape(trajs, span, heads_here, head_dim),
        prior_values.reshape(trajs, span, heads_here, head_dim),
        allow,
        scale,
    )
    attended = (window + read).astype(jnp.bfloat16).reshape(count, inner_here)
    w_output = lax.optimization_barrier((w_output, pair_raw))[0]
    out_block = w_output.shape[1]
    from_ranks = jnp.stack(
        [w_output]
        + [
            lax.ppermute(w_output, "wloop", [(source, (source + step) % ways) for source in range(ways)])
            for step in range(1, ways)
        ]
    )
    cores = lax.axis_size("heads")
    core = lax.axis_index("heads")
    share = width // cores

    blocks_per_share = share // out_block

    def output_share(index):
        parts = []
        for part in range(blocks_per_share):
            rank = index * blocks_per_share + part
            parts.append(
                jnp.dot(
                    attended,
                    lax.dynamic_index_in_dim(from_ranks, (me - rank) % ways, 0, keepdims=False),
                    preferred_element_type=jnp.float32,
                )
            )
        return jnp.concatenate(parts, axis=1) if blocks_per_share > 1 else parts[0]

    received = [
        lax.ppermute(
            output_share((core + step) % cores).astype(jnp.bfloat16),
            "heads",
            [(source, (source + step) % cores) for source in range(cores)],
        )
        for step in range(1, cores)
    ]
    summed = lax.optimization_barrier(output_share(core))
    for piece in received:
        summed = summed + piece.astype(jnp.float32)
    residual = lax.dynamic_slice_in_dim(
        activations.reshape(count, width), core * share, share, 1
    )
    return (residual.astype(jnp.float32) + summed).astype(jnp.bfloat16).reshape(trajs, span, share)


def solution(mesh):
    placed = (
        P(("groups", "wloop"), "seq", None),
        P(),
        P("wloop", "heads"),
        P("wloop", None, "heads"),
        P("heads", "wloop"),
        P(("groups", "wloop"), "heads", "seq"),
        P(("groups", "wloop"), "seq"),
    )
    return jax.shard_map(
        shards,
        mesh=mesh,
        in_specs=placed,
        out_specs=P(("groups", "wloop"), "seq", "heads"),
        check_vma=False,
    )
```
